32 devices in a mesh: groups: 2 (over y), lat: 4 (over x, core), lon: 4 (over z).
Axes of the slice: x: 2, y: 2, z: 4, core: 2. Of those that a mesh axis runs over, the one named last changes fastest.
Arguments:
- fields: bfloat16 [512, 4, 512], P('groups', 'lat', 'lon'), parts along dimension 0, may hold values from -6 to 6
- upstream: bfloat16 [512, 4, 512], P('groups', 'lat', 'lon'), parts along dimension 0, may hold values from -6 to 6
- weights: bfloat16 [9, 256, 256], replicated, may hold values from -0.125 to 0.125
- filter_taps: bfloat16 [4, 9, 3, 2, 64], P('lat'), may hold values from -0.3125 to 0.3125
- cycle_counts: int32 [4], P('lat'), may hold values from 1 to 2, as said below
- cycle_blocks: int32 [4, 2], P('lat'), may hold values from -2 to 1, as said below
Outputs:
- outputs: bfloat16 [512, 4, 512], P('groups', 'lat', 'lon'), parts along dimension 0
- input_grad: bfloat16 [512, 4, 512], P('groups', 'lat', 'lon'), parts along dimension 0
- weight_grad: float32 [18, 256, 256], P('groups', 'lon'), parts along dimension 0
The draws below stay inside these ranges and needn't reach their ends.
There are 2 independent parts, one for each index of `groups`. The reference program is written for one: setup_inputs(seed, part) draws one part's arguments, and reference() takes and returns one part's arrays. A program takes and returns all parts, laid end to end along the dimension named above; an argument that names none is the same for every part. Nothing has to cross between parts.
Inputs may be any that keep to these rules, and one draw needn't show every extreme that they name: Cycle i uses its first cycle_counts[i] slots; the first quarter of the cycles (at least one) uses all 2, the last cycle one. `cycle_blocks`: the 2 block numbers of a cycle are distinct; the first cycle holds the lowest and the highest.
All inputs are finite; a program needn't handle non-finite values.
Results may differ from the reference program's by a relative error of at most 0.0049.
Values may be sent and summed in bfloat16 or wider, within the bound.
No kernel may reach another device: no remote copies, remote signals or barrier semaphores. Data moves between devices by JAX's collectives and lax.ppermute only.
A program may use at most 64 MiB of HBM per device.

```python
import math
import jax
import jax.numpy as jnp
from jax import lax

C = 256
K = 9
BW = 64
MAXB = 2
HALO = 128
LON_DEV = 128
NLAT = 4
NLON = 512
N_LON = 4


def draw_cycle_counts(key, part):
    cycle_ids = jnp.arange(NLAT, dtype=jnp.int32)
    slot_counts = jax.random.randint(key, (NLAT,), 1, MAXB + 1, dtype=jnp.int32)
    polar_cycles = cycle_ids < max(NLAT // 4, 1)
    slot_counts = jnp.where(polar_cycles, MAXB, slot_counts)
    slot_counts = jnp.where(cycle_ids == NLAT - 1, 1, slot_counts)
    return slot_counts.astype(jnp.int32)


def draw_cycle_blocks(key, part):
    reach_blocks = HALO // BW
    cycle_keys = jax.random.split(key, NLAT)
    orders = jax.vmap(lambda cycle_key: jax.random.permutation(cycle_key, 2 * reach_blocks))(cycle_keys)
    chosen = orders[:, :MAXB].astype(jnp.int32) - reach_blocks
    first_row = jnp.where(jnp.arange(MAXB, dtype=jnp.int32) == 0, -reach_blocks, reach_blocks - 1)
    cycle_ids = jnp.arange(NLAT, dtype=jnp.int32)
    return jnp.where(cycle_ids[:, None] == 0, first_row[None, :], chosen).astype(jnp.int32)


def spiked(values, stream_key, source, target, blocks, factor):
    def block_of(axis_at):
        return (jnp.arange(values.shape[axis_at]) // (values.shape[axis_at] // blocks)).reshape((-1,) + (1,) * (values.ndim - 1 - axis_at))

    near = jax.random.permutation(stream_key, blocks)[block_of(target)]
    far = (block_of(target) + blocks // 2) % blocks
    return jnp.where((block_of(source) == near) | (block_of(source) == far), factor * values, values)


def shard_levels(key, shape, cuts, low, high):
    gain = 1.0
    for dim, parts in cuts:
        steps = jax.random.uniform(jax.random.fold_in(jax.random.fold_in(key, 6), dim), (parts,), jnp.float32, low / len(cuts), high / len(cuts))
        gain = gain * jnp.repeat(jnp.exp(steps), shape[dim] // parts).reshape((-1,) + (1,) * (len(shape) - 1 - dim))
    return gain


def noise(rng, dims, deviation, reach, shards=(), kind=jnp.bfloat16):
    factor_of = shard_levels(rng, dims, shards, -0.22, 0.18) if shards else 1.0
    drawn = jax.random.normal(rng, dims, jnp.float32) * deviation * factor_of
    return jnp.minimum(jnp.maximum(drawn, -reach), reach).astype(kind)


def noise_with(stream_key, shape, spread, reach, cuts, heavy, kind=jnp.bfloat16):
    result = spread * jax.random.normal(stream_key, shape, jnp.float32)
    if cuts:
        result = result * shard_levels(stream_key, shape, cuts, -0.22, 0.18)
    return jnp.clip(spiked(result, jax.random.fold_in(stream_key, 3), *heavy), -reach, reach).astype(kind)


def setup_inputs(seed: int = 0, part: int = 0) -> dict:
    keys = jax.random.split(jax.random.key(seed), 7)
    part_splits = jax.random.split(jax.random.fold_in(keys[6], part), 7)
    fields = noise(part_splits[0], (C, NLAT, NLON), 1.0, 6.0, ((1, 4), (2, 4)))
    upstream = noise_with(part_splits[1], (C, NLAT, NLON), 1.0, 6.0, ((1, 4), (2, 4)), (2, 0, 4, 2.0))
    weights = noise(keys[2], (K, C, C), (K * C) ** -0.5, 0.125)
    filter_taps = noise(keys[3], (NLAT, K, 3, MAXB, BW), (3 * MAXB * BW) ** -0.5, 0.3125, ((0, 4),))
    cycle_counts = draw_cycle_counts(jax.random.fold_in(keys[6], 71), part)
    cycle_blocks = draw_cycle_blocks(jax.random.fold_in(keys[6], 71), part)
    return {"fields": fields, "upstream": upstream, "weights": weights, "filter_taps": filter_taps, "cycle_counts": cycle_counts, "cycle_blocks": cycle_blocks}


def build_taps(filter_taps, cycle_counts, cycle_blocks):
    slot_total = cycle_blocks.shape[1]
    width_block = filter_taps.shape[4]
    offsets = jnp.arange(width_block, dtype=jnp.int32)
    places = HALO + width_block * cycle_blocks[:, :, None] + offsets[None, None, :]
    live_slots = jnp.arange(slot_total, dtype=jnp.int32)[None, :] < cycle_counts[:, None]
    positions = jnp.arange(2 * HALO, dtype=jnp.int32)
    onehot = jnp.where((places[:, :, :, None] == positions) & live_slots[:, :, None, None], 1.0, 0.0).astype(jnp.float32)
    return jnp.einsum("ikrst,istu->ikru", filter_taps.astype(jnp.float32), onehot)


def banded_matrix(tap_row, out_width, tap_reach):
    kernels = tap_row.shape[0]
    stencil_rows = tap_row.shape[1]
    window_len = out_width + tap_reach
    padded = jnp.concatenate([tap_row, jnp.zeros((kernels, stencil_rows, window_len + 1 - tap_reach), tap_row.dtype)], axis=2)
    repeated = jnp.tile(padded, (1, 1, out_width))[:, :, :out_width * window_len]
    repeated = repeated.reshape(kernels, stencil_rows, out_width, window_len)
    return jnp.transpose(repeated, (1, 3, 0, 2))


def reference(fields, upstream, weights, filter_taps, cycle_counts, cycle_blocks):
    tap_table = build_taps(filter_taps, cycle_counts, cycle_blocks)
    block_len = LON_DEV * math.gcd(N_LON, 4)
    window_len = block_len + 2 * HALO
    block_count = NLON // block_len
    padded = jnp.pad(fields.astype(jnp.float32), ((0, 0), (1, 1), (0, 0)))
    widened = jnp.concatenate([padded[:, :, NLON - HALO:], padded, padded[:, :, :HALO]], axis=2)

    def one_cycle(position):
        position = position.astype(jnp.int32)
        cycle_rows = lax.dynamic_slice_in_dim(widened, position, 3, axis=1)
        matrix = banded_matrix(tap_table[position], block_len, 2 * HALO).reshape(3 * window_len, K * block_len)

        def one_block(block_index):
            begin_at = (block_index * block_len).astype(jnp.int32)
            window = lax.dynamic_slice_in_dim(cycle_rows, begin_at, window_len, axis=2).reshape(C, 3 * window_len)
            return jnp.dot(window, matrix, precision=lax.Precision.HIGHEST, preferred_element_type=jnp.float32)

        pieces = lax.map(one_block, jnp.arange(block_count, dtype=jnp.int32))
        return jnp.transpose(pieces.reshape(block_count, C, K, block_len), (1, 2, 0, 3)).reshape(C, K, NLON)

    response32 = jnp.transpose(lax.map(one_cycle, jnp.arange(NLAT, dtype=jnp.int32)), (1, 0, 2, 3))
    response = response32.astype(jnp.bfloat16)
    weights32 = weights.astype(jnp.float32)
    upstream32 = upstream.astype(jnp.float32)
    response_f = response.astype(jnp.float32)
    outputs = jnp.einsum("koc,cikj->oij", weights32, response_f).astype(jnp.bfloat16)
    response_grad = jnp.einsum("koc,oij->cikj", weights32, upstream32).astype(jnp.bfloat16)
    weight_grad = jnp.einsum("oij,cikj->koc", upstream32, response_f)
    grad32 = response_grad.astype(jnp.float32)

    def per_cycle(position, accumulated):
        position = position.astype(jnp.int32)
        matrix = banded_matrix(tap_table[position], block_len, 2 * HALO).reshape(3 * window_len, K * block_len)
        grad_row = lax.dynamic_index_in_dim(grad32, position, axis=1, keepdims=False)

        def per_block(block_index, inner_acc):
            begin_at = (block_index * block_len).astype(jnp.int32)
            grad_piece = lax.dynamic_slice_in_dim(grad_row, begin_at, block_len, axis=2).reshape(C, K * block_len)
            contrib = jnp.dot(grad_piece, matrix.T, precision=lax.Precision.HIGHEST, preferred_element_type=jnp.float32)
            contrib = contrib.reshape(C, 3, window_len)
            anchor = (jnp.zeros((), jnp.int32), position, begin_at)
            current = lax.dynamic_slice(inner_acc, anchor, (C, 3, window_len))
            return lax.dynamic_update_slice(inner_acc, current + contrib, anchor)

        return lax.fori_loop(0, block_count, per_block, accumulated)

    accumulated = jnp.zeros((C, NLAT + 2, NLON + 2 * HALO), jnp.float32)
    accumulated = lax.fori_loop(0, NLAT, per_cycle, accumulated)
    interior = accumulated[:, 1:NLAT + 1, HALO:HALO + NLON]
    interior = interior.at[:, :, :HALO].add(accumulated[:, 1:NLAT + 1, NLON + HALO:])
    interior = interior.at[:, :, NLON - HALO:].add(accumulated[:, 1:NLAT + 1, :HALO])
    return outputs, interior.astype(jnp.bfloat16), weight_grad
```

```python
import jax
import jax.numpy as jnp
from jax import lax
from jax.experimental import pallas as pl
from jax.experimental.pallas import tpu as pltpu
from jax.sharding import PartitionSpec as P

HALO = 128


def padded_2(cells, sides, width, closed):
    for axis, dim in sides:
        count = lax.axis_size(axis)
        ends = count if closed else count - 1
        head = lax.slice_in_dim(cells, 0, width, axis=dim)
        tail = lax.slice_in_dim(cells, cells.shape[dim] - width, cells.shape[dim], axis=dim)
        cells = jnp.concatenate(
            [
                lax.ppermute(tail, axis, [(i, (i + 1) % count) for i in range(ends)]),
                cells,
                lax.ppermute(head, axis, [((i + 1) % count, i) for i in range(ends)]),
            ],
            axis=dim,
        )
    return cells


def build_taps(filter_taps, cycle_counts, cycle_blocks):
    slot_total = cycle_blocks.shape[1]
    width_block = filter_taps.shape[4]
    offsets = jnp.arange(width_block, dtype=jnp.int32)
    places = HALO + width_block * cycle_blocks[:, :, None] + offsets[None, None, :]
    live_slots = jnp.arange(slot_total, dtype=jnp.int32)[None, :] < cycle_counts[:, None]
    positions = jnp.arange(2 * HALO, dtype=jnp.int32)
    onehot = jnp.where(
        (places[:, :, :, None] == positions) & live_slots[:, :, None, None], 1.0, 0.0
    ).astype(jnp.float32)
    return jnp.einsum("ikrst,istu->ikru", filter_taps.astype(jnp.float32), onehot)


def toeplitz_kernel(tap_ref, out_ref):
    kernels, lon_cols, width = out_ref.shape
    window_len = tap_ref.shape[1]
    stencil_rows = width // window_len
    for k in range(kernels):
        for r in range(stencil_rows):
            row = tap_ref[pl.ds(k * stencil_rows + r, 1), :]
            tiled = jnp.broadcast_to(row, (lon_cols, window_len))
            rolled = pltpu.roll(tiled, 0, 1, stride=1, stride_axis=0)
            out_ref[k, :, pl.ds(r * window_len, window_len)] = rolled.astype(out_ref.dtype)


def toeplitz(tap_row, out_width):
    kernels, stencil_rows, reach = tap_row.shape
    window_len = out_width + reach
    padded = jnp.pad(tap_row.astype(jnp.float32), ((0, 0), (0, 0), (0, window_len - reach)))
    padded = padded.reshape(kernels * stencil_rows, window_len)
    out = pl.pallas_call(
        toeplitz_kernel,
        out_shape=jax.ShapeDtypeStruct((kernels, out_width, stencil_rows * window_len), jnp.bfloat16),
    )(padded)
    return out.reshape(kernels * out_width, stencil_rows * window_len)


def body(fields, upstream, weights, filter_taps, cycle_counts, cycle_blocks):
    channels, lat_rows, lon_cols = fields.shape
    kernels = weights.shape[0]
    window_len = lon_cols + 2 * HALO
    tap_table = build_taps(filter_taps, cycle_counts, cycle_blocks).astype(jnp.bfloat16)
    banded = padded_2(fields, (("lat", 1),), 1, False)
    widened = padded_2(banded, (("lon", 2),), HALO, True)
    matrices = [toeplitz(tap_table[0], lon_cols)]
    cycle_row = 0
    responses = [
        lax.dot_general(
            widened.reshape(channels, 3 * window_len),
            matrices[cycle_row],
            (((1,), (1,)), ((), ())),
            preferred_element_type=jnp.float32,
        )
    ]
    response = (
        jnp.stack(responses, axis=1)
        .reshape(channels, lat_rows, kernels, lon_cols)
        .astype(jnp.bfloat16)
    )
    outputs = jnp.einsum(
        "koc,cikj->oij", weights, response, preferred_element_type=jnp.float32
    ).astype(jnp.bfloat16)
    response_grad = jnp.einsum(
        "koc,oij->cikj", weights, upstream, preferred_element_type=jnp.float32
    ).astype(jnp.bfloat16)
    grad_terms = jnp.einsum("oij,cikj->koc", upstream, response, preferred_element_type=jnp.float32)
    grad_share = lax.psum_scatter(grad_terms, "lon", scatter_dimension=1, tiled=True)
    weight_grad = lax.psum(grad_share, "lat")
    accumulated = jnp.zeros((channels, lat_rows + 2, window_len), jnp.float32)
    cycle_row = 0
    grad_piece = response_grad[:, cycle_row].reshape(channels, kernels * lon_cols)
    contrib = jnp.dot(grad_piece, matrices[cycle_row], preferred_element_type=jnp.float32)
    accumulated = accumulated.at[:, cycle_row : cycle_row + 3].add(
        contrib.reshape(channels, 3, window_len)
    )
    rim_columns = jnp.concatenate(
        [accumulated[:, :, :HALO], accumulated[:, :, HALO + lon_cols :]], axis=2
    )
    arrived = padded_2(rim_columns, (("lon", 2),), HALO, True)
    interior = accumulated[:, :, HALO : HALO + lon_cols]
    interior = interior.at[:, :, :HALO].add(arrived[:, :, :HALO])
    interior = interior.at[:, :, lon_cols - HALO :].add(arrived[:, :, 3 * HALO :])
    edge_rows = jnp.stack([interior[:, 0], interior[:, lat_rows + 1]], axis=1)
    arrived = padded_2(edge_rows, (("lat", 1),), 1, False)
    result = interior[:, 1 : lat_rows + 1]
    result = result.at[:, 0].add(arrived[:, 0])
    result = result.at[:, lat_rows - 1].add(arrived[:, 3])
    return (outputs, result.astype(jnp.bfloat16), weight_grad)


def solution(mesh):
    return jax.shard_map(
        body,
        mesh=mesh,
        in_specs=(
            P("groups", "lat", "lon"),
            P("groups", "lat", "lon"),
            P(),
            P("lat", None, None, None, None),
            P("lat"),
            P("lat", None),
        ),
        out_specs=(P("groups", "lat", "lon"), P("groups", "lat", "lon"), P("groups", "lon", None)),
        check_vma=False,
    )
```

```python
import jax
import jax.numpy as jnp
from jax import lax
from jax.experimental import pallas as pl
from jax.experimental.pallas import tpu as pltpu
from jax.sharding import PartitionSpec as P

HALO = 128


def padded_2(cells, sides, width, closed):
    for axis, dim in sides:
        count = lax.axis_size(axis)
        ends = count if closed else count - 1
        head = lax.slice_in_dim(cells, 0, width, axis=dim)
        tail = lax.slice_in_dim(cells, cells.shape[dim] - width, cells.shape[dim], axis=dim)
        cells = jnp.concatenate(
            [
                lax.ppermute(tail, axis, [(i, (i + 1) % count) for i in range(ends)]),
                cells,
                lax.ppermute(head, axis, [((i + 1) % count, i) for i in range(ends)]),
            ],
            axis=dim,
        )
    return cells


def build_taps(filter_taps, cycle_counts, cycle_blocks):
    slot_total = cycle_blocks.shape[1]
    width_block = filter_taps.shape[4]
    offsets = jnp.arange(width_block, dtype=jnp.int32)
    places = HALO + width_block * cycle_blocks[:, :, None] + offsets[None, None, :]
    live_slots = jnp.arange(slot_total, dtype=jnp.int32)[None, :] < cycle_counts[:, None]
    positions = jnp.arange(2 * HALO, dtype=jnp.int32)
    onehot = jnp.where(
        (places[:, :, :, None] == positions) & live_slots[:, :, None, None], 1.0, 0.0
    ).astype(jnp.float32)
    return jnp.einsum("ikrst,istu->ikru", filter_taps.astype(jnp.float32), onehot)


def toeplitz_kernel(tap_ref, out_ref):
    kernels, lon_cols, width = out_ref.shape
    window_len = tap_ref.shape[1]
    stencil_rows = width // window_len
    for k in range(kernels):
        for r in range(stencil_rows):
            row = tap_ref[pl.ds(k * stencil_rows + r, 1), :]
            tiled = jnp.broadcast_to(row, (lon_cols, window_len))
            rolled = pltpu.roll(tiled, 0, 1, stride=1, stride_axis=0)
            out_ref[k, :, pl.ds(r * window_len, window_len)] = rolled.astype(out_ref.dtype)


def toeplitz(tap_row, out_width):
    kernels, stencil_rows, reach = tap_row.shape
    window_len = out_width + reach
    padded = jnp.pad(tap_row.astype(jnp.float32), ((0, 0), (0, 0), (0, window_len - reach)))
    padded = padded.reshape(kernels * stencil_rows, window_len)
    out = pl.pallas_call(
        toeplitz_kernel,
        out_shape=jax.ShapeDtypeStruct((kernels, out_width, stencil_rows * window_len), jnp.bfloat16),
    )(padded)
    return out.reshape(kernels * out_width, stencil_rows * window_len)


def lat_allreduce(x, axis, dim):
    count = lax.axis_size(axis)
    steps = count.bit_length() - 1
    if (1 << steps) != count or x.shape[dim] % count:
        return lax.psum(x, axis)
    index = lax.axis_index(axis)
    buf = x
    for s in range(steps):
        half = buf.shape[dim] // 2
        bit = (index >> s) & 1
        keep = lax.dynamic_slice_in_dim(buf, bit * half, half, axis=dim)
        send = lax.dynamic_slice_in_dim(buf, (1 - bit) * half, half, axis=dim)
        recv = lax.ppermute(send, axis, [(i, i ^ (1 << s)) for i in range(count)])
        buf = keep + recv
    for s in reversed(range(steps)):
        size = buf.shape[dim]
        bit = (index >> s) & 1
        recv = lax.ppermute(buf, axis, [(i, i ^ (1 << s)) for i in range(count)])
        shape = list(buf.shape)
        shape[dim] = 2 * size
        out = jnp.zeros(shape, buf.dtype)
        out = lax.dynamic_update_slice_in_dim(out, buf, bit * size, axis=dim)
        buf = lax.dynamic_update_slice_in_dim(out, recv, (1 - bit) * size, axis=dim)
    return buf


def body(fields, upstream, weights, filter_taps, cycle_counts, cycle_blocks):
    channels, lat_rows, lon_cols = fields.shape
    kernels = weights.shape[0]
    window_len = lon_cols + 2 * HALO
    n_lon = lax.axis_size("lon")
    lon_at = lax.axis_index("lon")
    tap_table = build_taps(filter_taps, cycle_counts, cycle_blocks).astype(jnp.bfloat16)
    matrix = toeplitz(tap_table[0], lon_cols)
    banded = padded_2(fields, (("lat", 1),), 1, False)
    blocks = [banded] + [
        lax.ppermute(banded, "lon", [(p, (p - d) % n_lon) for p in range(n_lon)])
        for d in range(1, n_lon)
    ]
    row = jnp.concatenate(blocks, axis=2)
    ext = jnp.concatenate([row[:, :, row.shape[2] - HALO :], row, row[:, :, :HALO]], axis=2)
    windows = jnp.stack(
        [ext[:, :, d * lon_cols : d * lon_cols + window_len] for d in range(n_lon)], axis=0
    )
    response_all = lax.dot_general(
        windows.reshape(n_lon * channels, 3 * window_len),
        matrix,
        (((1,), (1,)), ((), ())),
        preferred_element_type=jnp.float32,
    ).astype(jnp.bfloat16).reshape(n_lon, channels, kernels, lon_cols)
    response = response_all[0].reshape(channels, lat_rows, kernels, lon_cols)
    outputs = jnp.einsum(
        "koc,cikj->oij", weights, response, preferred_element_type=jnp.float32
    ).astype(jnp.bfloat16)
    response_grad = jnp.einsum(
        "koc,oij->cikj", weights, upstream, preferred_element_type=jnp.float32
    ).astype(jnp.bfloat16)
    o_block = upstream.shape[0] // n_lon
    up_row = upstream[:, 0]
    up_parts = [lax.dynamic_slice_in_dim(up_row, lon_at * o_block, o_block, axis=0)]
    for d in range(1, n_lon):
        part = lax.dynamic_slice_in_dim(up_row, ((lon_at - d) % n_lon) * o_block, o_block, axis=0)
        up_parts.append(lax.ppermute(part, "lon", [(p, (p - d) % n_lon) for p in range(n_lon)]))
    up_rel = jnp.stack(up_parts, axis=0)
    grad_terms = jnp.einsum(
        "doj,dckj->koc", up_rel, response_all, preferred_element_type=jnp.float32
    )
    weight_grad = lat_allreduce(grad_terms, "lat", 1)
    accumulated = jnp.zeros((channels, lat_rows + 2, window_len), jnp.float32)
    cycle_row = 0
    grad_piece = response_grad[:, cycle_row].reshape(channels, kernels * lon_cols)
    contrib = jnp.dot(grad_piece, matrix, preferred_element_type=jnp.float32)
    accumulated = accumulated.at[:, cycle_row : cycle_row + 3].add(
        contrib.reshape(channels, 3, window_len)
    )
    rim_columns = jnp.concatenate(
        [accumulated[:, :, :HALO], accumulated[:, :, HALO + lon_cols :]], axis=2
    )
    arrived = padded_2(rim_columns, (("lon", 2),), HALO, True)
    interior = accumulated[:, :, HALO : HALO + lon_cols]
    interior = interior.at[:, :, :HALO].add(arrived[:, :, :HALO])
    interior = interior.at[:, :, lon_cols - HALO :].add(arrived[:, :, 3 * HALO :])
    edge_rows = jnp.stack([interior[:, 0], interior[:, lat_rows + 1]], axis=1)
    arrived = padded_2(edge_rows, (("lat", 1),), 1, False)
    result = interior[:, 1 : lat_rows + 1]
    result = result.at[:, 0].add(arrived[:, 0])
    result = result.at[:, lat_rows - 1].add(arrived[:, 3])
    return (outputs, result.astype(jnp.bfloat16), weight_grad)


def solution(mesh):
    return jax.shard_map(
        body,
        mesh=mesh,
        in_specs=(
            P("groups", "lat", "lon"),
            P("groups", "lat", "lon"),
            P(),
            P("lat", None, None, None, None),
            P("lat"),
            P("lat", None),
        ),
        out_specs=(P("groups", "lat", "lon"), P("groups", "lat", "lon"), P("groups", "lon", None)),
        check_vma=False,
    )
```

```python
import jax
import jax.numpy as jnp
from jax import lax
from jax.experimental import pallas as pl
from jax.experimental.pallas import tpu as pltpu
from jax.sharding import PartitionSpec as P

HALO = 128


def padded_2(cells, sides, width, closed):
    for axis, dim in sides:
        count = lax.axis_size(axis)
        ends = count if closed else count - 1
        head = lax.slice_in_dim(cells, 0, width, axis=dim)
        tail = lax.slice_in_dim(cells, cells.shape[dim] - width, cells.shape[dim], axis=dim)
        cells = jnp.concatenate(
            [
                lax.ppermute(tail, axis, [(i, (i + 1) % count) for i in range(ends)]),
                cells,
                lax.ppermute(head, axis, [((i + 1) % count, i) for i in range(ends)]),
            ],
            axis=dim,
        )
    return cells


def build_taps(filter_taps, cycle_counts, cycle_blocks):
    slot_total = cycle_blocks.shape[1]
    width_block = filter_taps.shape[4]
    offsets = jnp.arange(width_block, dtype=jnp.int32)
    places = HALO + width_block * cycle_blocks[:, :, None] + offsets[None, None, :]
    live_slots = jnp.arange(slot_total, dtype=jnp.int32)[None, :] < cycle_counts[:, None]
    positions = jnp.arange(2 * HALO, dtype=jnp.int32)
    onehot = jnp.where(
        (places[:, :, :, None] == positions) & live_slots[:, :, None, None], 1.0, 0.0
    ).astype(jnp.float32)
    return jnp.einsum("ikrst,istu->ikru", filter_taps.astype(jnp.float32), onehot)


def toeplitz_kernel(tap_ref, out_ref):
    kernels, lon_cols, width = out_ref.shape
    window_len = tap_ref.shape[1]
    stencil_rows = width // window_len
    for k in range(kernels):
        for r in range(stencil_rows):
            row = tap_ref[pl.ds(k * stencil_rows + r, 1), :]
            tiled = jnp.broadcast_to(row, (lon_cols, window_len))
            rolled = pltpu.roll(tiled, 0, 1, stride=1, stride_axis=0)
            out_ref[k, :, pl.ds(r * window_len, window_len)] = rolled.astype(out_ref.dtype)


def toeplitz(tap_row, out_width):
    kernels, stencil_rows, reach = tap_row.shape
    window_len = out_width + reach
    padded = jnp.pad(tap_row.astype(jnp.float32), ((0, 0), (0, 0), (0, window_len - reach)))
    padded = padded.reshape(kernels * stencil_rows, window_len)
    out = pl.pallas_call(
        toeplitz_kernel,
        out_shape=jax.ShapeDtypeStruct((kernels, out_width, stencil_rows * window_len), jnp.bfloat16),
    )(padded)
    return out.reshape(kernels * out_width, stencil_rows * window_len)


def lat_allreduce(x, axis, dim):
    count = lax.axis_size(axis)
    steps = count.bit_length() - 1
    if (1 << steps) != count or x.shape[dim] % count:
        return lax.psum(x, axis)
    index = lax.axis_index(axis)
    size = x.shape[dim] // count
    parts = [lax.dynamic_slice_in_dim(x, index * size, size, axis=dim)]
    for d in range(1, count):
        send = lax.dynamic_slice_in_dim(x, (index ^ d) * size, size, axis=dim)
        parts.append(lax.ppermute(send, axis, [(i, i ^ d) for i in range(count)]))
    for s in range(steps):
        parts = [parts[2 * e] + parts[2 * e + 1] for e in range(len(parts) // 2)]
    mine = parts[0]
    out = jnp.zeros(x.shape, x.dtype)
    out = lax.dynamic_update_slice_in_dim(out, mine, index * size, axis=dim)
    for d in range(1, count):
        recv = lax.ppermute(mine, axis, [(i, i ^ d) for i in range(count)])
        out = lax.dynamic_update_slice_in_dim(out, recv, (index ^ d) * size, axis=dim)
    return out


def body(fields, upstream, weights, filter_taps, cycle_counts, cycle_blocks):
    channels, lat_rows, lon_cols = fields.shape
    kernels = weights.shape[0]
    window_len = lon_cols + 2 * HALO
    n_lon = lax.axis_size("lon")
    lon_at = lax.axis_index("lon")
    tap_table = build_taps(filter_taps, cycle_counts, cycle_blocks).astype(jnp.bfloat16)
    matrix = toeplitz(tap_table[0], lon_cols)
    blocks = [fields] + [
        lax.ppermute(fields, "lon", [(p, (p - d) % n_lon) for p in range(n_lon)])
        for d in range(1, n_lon)
    ]
    row = padded_2(jnp.concatenate(blocks, axis=2), (("lat", 1),), 1, False)
    ext = jnp.concatenate([row[:, :, row.shape[2] - HALO :], row, row[:, :, :HALO]], axis=2)
    windows = jnp.stack(
        [ext[:, :, d * lon_cols : d * lon_cols + window_len] for d in range(n_lon)], axis=0
    )
    response_all = lax.dot_general(
        windows.reshape(n_lon * channels, 3 * window_len),
        matrix,
        (((1,), (1,)), ((), ())),
        preferred_element_type=jnp.float32,
    ).astype(jnp.bfloat16).reshape(n_lon, channels, kernels, lon_cols)
    response = response_all[0].reshape(channels, lat_rows, kernels, lon_cols)
    outputs = jnp.einsum(
        "koc,cikj->oij", weights, response, preferred_element_type=jnp.float32
    ).astype(jnp.bfloat16)
    response_grad = jnp.einsum(
        "koc,oij->cikj", weights, upstream, preferred_element_type=jnp.float32
    ).astype(jnp.bfloat16)
    o_block = upstream.shape[0] // n_lon
    up_row = upstream[:, 0]
    up_parts = [lax.dynamic_slice_in_dim(up_row, lon_at * o_block, o_block, axis=0)]
    for d in range(1, n_lon):
        part = lax.dynamic_slice_in_dim(up_row, ((lon_at - d) % n_lon) * o_block, o_block, axis=0)
        up_parts.append(lax.ppermute(part, "lon", [(p, (p - d) % n_lon) for p in range(n_lon)]))
    up_rel = jnp.stack(up_parts, axis=0)
    grad_terms = jnp.einsum(
        "doj,dckj->koc", up_rel, response_all, preferred_element_type=jnp.float32
    )
    weight_grad = lat_allreduce(grad_terms, "lat", 1)
    accumulated = jnp.zeros((channels, lat_rows + 2, window_len), jnp.float32)
    cycle_row = 0
    grad_piece = response_grad[:, cycle_row].reshape(channels, kernels * lon_cols)
    contrib = jnp.dot(grad_piece, matrix, preferred_element_type=jnp.float32)
    accumulated = accumulated.at[:, cycle_row : cycle_row + 3].add(
        contrib.reshape(channels, 3, window_len)
    )
    rim_columns = jnp.concatenate(
        [accumulated[:, :, :HALO], accumulated[:, :, HALO + lon_cols :]], axis=2
    )
    arrived = padded_2(rim_columns, (("lon", 2),), HALO, True)
    interior = accumulated[:, :, HALO : HALO + lon_cols]
    interior = interior.at[:, :, :HALO].add(arrived[:, :, :HALO])
    interior = interior.at[:, :, lon_cols - HALO :].add(arrived[:, :, 3 * HALO :])
    edge_rows = jnp.stack([interior[:, 0], interior[:, lat_rows + 1]], axis=1)
    arrived = padded_2(edge_rows, (("lat", 1),), 1, False)
    result = interior[:, 1 : lat_rows + 1]
    result = result.at[:, 0].add(arrived[:, 0])
    result = result.at[:, lat_rows - 1].add(arrived[:, 3])
    return (outputs, result.astype(jnp.bfloat16), weight_grad)


def solution(mesh):
    return jax.shard_map(
        body,
        mesh=mesh,
        in_specs=(
            P("groups", "lat", "lon"),
            P("groups", "lat", "lon"),
            P(),
            P("lat", None, None, None, None),
            P("lat"),
            P("lat", None),
        ),
        out_specs=(P("groups", "lat", "lon"), P("groups", "lat", "lon"), P("groups", "lon", None)),
        check_vma=False,
    )
```

```python
import jax
import jax.numpy as jnp
from jax import lax
from jax.experimental import pallas as pl
from jax.experimental.pallas import tpu as pltpu
from jax.sharding import PartitionSpec as P

HALO = 128


def padded_2(cells, sides, width, closed):
    for axis, dim in sides:
        count = lax.axis_size(axis)
        ends = count if closed else count - 1
        head = lax.slice_in_dim(cells, 0, width, axis=dim)
        tail = lax.slice_in_dim(cells, cells.shape[dim] - width, cells.shape[dim], axis=dim)
        cells = jnp.concatenate(
            [
                lax.ppermute(tail, axis, [(i, (i + 1) % count) for i in range(ends)]),
                cells,
                lax.ppermute(head, axis, [((i + 1) % count, i) for i in range(ends)]),
            ],
            axis=dim,
        )
    return cells


def build_taps(filter_taps, cycle_counts, cycle_blocks):
    slot_total = cycle_blocks.shape[1]
    width_block = filter_taps.shape[4]
    offsets = jnp.arange(width_block, dtype=jnp.int32)
    places = HALO + width_block * cycle_blocks[:, :, None] + offsets[None, None, :]
    live_slots = jnp.arange(slot_total, dtype=jnp.int32)[None, :] < cycle_counts[:, None]
    positions = jnp.arange(2 * HALO, dtype=jnp.int32)
    onehot = jnp.where(
        (places[:, :, :, None] == positions) & live_slots[:, :, None, None], 1.0, 0.0
    ).astype(jnp.float32)
    return jnp.einsum("ikrst,istu->ikru", filter_taps.astype(jnp.float32), onehot)


def toeplitz_kernel(tap_ref, out_ref):
    kernels, lon_cols, width = out_ref.shape
    window_len = tap_ref.shape[1]
    stencil_rows = width // window_len
    for k in range(kernels):
        for r in range(stencil_rows):
            row = tap_ref[pl.ds(k * stencil_rows + r, 1), :]
            tiled = jnp.broadcast_to(row, (lon_cols, window_len))
            rolled = pltpu.roll(tiled, 0, 1, stride=1, stride_axis=0)
            out_ref[k, :, pl.ds(r * window_len, window_len)] = rolled.astype(out_ref.dtype)


def toeplitz(tap_row, out_width):
    kernels, stencil_rows, reach = tap_row.shape
    window_len = out_width + reach
    padded = jnp.pad(tap_row.astype(jnp.float32), ((0, 0), (0, 0), (0, window_len - reach)))
    padded = padded.reshape(kernels * stencil_rows, window_len)
    out = pl.pallas_call(
        toeplitz_kernel,
        out_shape=jax.ShapeDtypeStruct((kernels, out_width, stencil_rows * window_len), jnp.bfloat16),
    )(padded)
    return out.reshape(kernels * out_width, stencil_rows * window_len)


def lat_allreduce(x, axis, dim):
    count = lax.axis_size(axis)
    steps = count.bit_length() - 1
    if (1 << steps) != count or x.shape[dim] % count:
        return lax.psum(x, axis)
    index = lax.axis_index(axis)
    size = x.shape[dim] // count
    parts = [lax.dynamic_slice_in_dim(x, index * size, size, axis=dim)]
    for d in range(1, count):
        send = lax.dynamic_slice_in_dim(x, (index ^ d) * size, size, axis=dim)
        parts.append(lax.ppermute(send, axis, [(i, i ^ d) for i in range(count)]))
    for s in range(steps):
        parts = [parts[2 * e] + parts[2 * e + 1] for e in range(len(parts) // 2)]
    mine = parts[0]
    out = jnp.zeros(x.shape, x.dtype)
    out = lax.dynamic_update_slice_in_dim(out, mine, index * size, axis=dim)
    for d in range(1, count):
        recv = lax.ppermute(mine, axis, [(i, i ^ d) for i in range(count)])
        out = lax.dynamic_update_slice_in_dim(out, recv, (index ^ d) * size, axis=dim)
    return out


def row_kernel(ext_ref, mt_ref, w_ref, up_ref, out_ref, gt_ref):
    stencil_rows, channels, _ = ext_ref.shape
    n_blocks, o_block, lon_cols = up_ref.shape
    kernels = w_ref.shape[0]
    window_len = mt_ref.shape[1] // stencil_rows
    contract_last = (((1,), (1,)), ((), ()))
    gt_ref[...] = jnp.zeros(gt_ref.shape, gt_ref.dtype)
    for d in range(n_blocks):
        acc = None
        for r in range(stencil_rows):
            win = ext_ref[r, :, pl.ds(d * lon_cols, window_len)]
            part = lax.dot_general(
                win,
                mt_ref[:, pl.ds(r * window_len, window_len)],
                contract_last,
                preferred_element_type=jnp.float32,
            )
            acc = part if acc is None else acc + part
        resp = acc.astype(jnp.bfloat16)
        up_d = up_ref[d]
        for k in range(kernels):
            resp_k = resp[:, k * lon_cols : (k + 1) * lon_cols]
            gt_ref[k] += lax.dot_general(
                up_d, resp_k, contract_last, preferred_element_type=jnp.float32
            )
        if d == 0:
            total = None
            for k in range(kernels):
                term = jnp.dot(
                    w_ref[k],
                    resp[:, k * lon_cols : (k + 1) * lon_cols],
                    preferred_element_type=jnp.float32,
                )
                total = term if total is None else total + term
            out_ref[...] = total.astype(out_ref.dtype)


def row_products(ext, matrix, weights, up_rel):
    stencil_rows, channels, _ = ext.shape
    n_blocks, o_block, lon_cols = up_rel.shape
    kernels = weights.shape[0]
    flops = 2 * n_blocks * channels * matrix.shape[0] * matrix.shape[1]
    flops += 2 * n_blocks * kernels * o_block * lon_cols * channels
    flops += 2 * kernels * weights.shape[1] * channels * lon_cols
    nbytes = 2 * (ext.size + matrix.size + weights.size + up_rel.size)
    nbytes += 2 * weights.shape[1] * lon_cols + 4 * kernels * o_block * channels
    return pl.pallas_call(
        row_kernel,
        out_shape=(
            jax.ShapeDtypeStruct((weights.shape[1], lon_cols), jnp.bfloat16),
            jax.ShapeDtypeStruct((kernels, o_block, channels), jnp.float32),
        ),
        cost_estimate=pl.CostEstimate(flops=flops, transcendentals=0, bytes_accessed=nbytes),
    )(ext, matrix, weights, up_rel)


def body(fields, upstream, weights, filter_taps, cycle_counts, cycle_blocks):
    channels, lat_rows, lon_cols = fields.shape
    kernels = weights.shape[0]
    window_len = lon_cols + 2 * HALO
    n_lon = lax.axis_size("lon")
    lon_at = lax.axis_index("lon")
    tap_table = build_taps(filter_taps, cycle_counts, cycle_blocks).astype(jnp.bfloat16)
    matrix = toeplitz(tap_table[0], lon_cols)
    blocks = [fields] + [
        lax.ppermute(fields, "lon", [(p, (p - d) % n_lon) for p in range(n_lon)])
        for d in range(1, n_lon)
    ]
    row = jnp.concatenate(blocks, axis=2)[:, 0]
    count = lax.axis_size("lat")
    below = lax.ppermute(row, "lat", [(i, i + 1) for i in range(count - 1)])
    above = lax.ppermute(row, "lat", [(i + 1, i) for i in range(count - 1)])
    rows = jnp.stack([below, row, above], axis=0)
    ext = jnp.concatenate([rows[:, :, rows.shape[2] - HALO :], rows, rows[:, :, :HALO]], axis=2)
    response_grad = jnp.einsum(
        "koc,oij->cikj", weights, upstream, preferred_element_type=jnp.float32
    ).astype(jnp.bfloat16)
    o_block = upstream.shape[0] // n_lon
    up_row = upstream[:, 0]
    up_parts = [lax.dynamic_slice_in_dim(up_row, lon_at * o_block, o_block, axis=0)]
    for d in range(1, n_lon):
        part = lax.dynamic_slice_in_dim(up_row, ((lon_at - d) % n_lon) * o_block, o_block, axis=0)
        up_parts.append(lax.ppermute(part, "lon", [(p, (p - d) % n_lon) for p in range(n_lon)]))
    up_rel = jnp.stack(up_parts, axis=0)
    out_row, grad_terms = row_products(ext, matrix, weights, up_rel)
    outputs = out_row[:, None, :]
    weight_grad = lat_allreduce(grad_terms, "lat", 1)
    accumulated = jnp.zeros((channels, lat_rows + 2, window_len), jnp.float32)
    cycle_row = 0
    grad_piece = response_grad[:, cycle_row].reshape(channels, kernels * lon_cols)
    contrib = jnp.dot(grad_piece, matrix, preferred_element_type=jnp.float32)
    accumulated = accumulated.at[:, cycle_row : cycle_row + 3].add(
        contrib.reshape(channels, 3, window_len)
    )
    rim_columns = jnp.concatenate(
        [accumulated[:, :, :HALO], accumulated[:, :, HALO + lon_cols :]], axis=2
    )
    arrived = padded_2(rim_columns, (("lon", 2),), HALO, True)
    interior = accumulated[:, :, HALO : HALO + lon_cols]
    interior = interior.at[:, :, :HALO].add(arrived[:, :, :HALO])
    interior = interior.at[:, :, lon_cols - HALO :].add(arrived[:, :, 3 * HALO :])
    edge_rows = jnp.stack([interior[:, 0], interior[:, lat_rows + 1]], axis=1)
    arrived = padded_2(edge_rows, (("lat", 1),), 1, False)
    result = interior[:, 1 : lat_rows + 1]
    result = result.at[:, 0].add(arrived[:, 0])
    result = result.at[:, lat_rows - 1].add(arrived[:, 3])
    return (outputs, result.astype(jnp.bfloat16), weight_grad)


def solution(mesh):
    return jax.shard_map(
        body,
        mesh=mesh,
        in_specs=(
            P("groups", "lat", "lon"),
            P("groups", "lat", "lon"),
            P(),
            P("lat", None, None, None, None),
            P("lat"),
            P("lat", None),
        ),
        out_specs=(P("groups", "lat", "lon"), P("groups", "lat", "lon"), P("groups", "lon", None)),
        check_vma=False,
    )
```

```python
import jax
import jax.numpy as jnp
from jax import lax
from jax.experimental import pallas as pl
from jax.experimental.pallas import tpu as pltpu
from jax.sharding import PartitionSpec as P

HALO = 128


def padded_2(cells, sides, width, closed):
    for axis, dim in sides:
        count = lax.axis_size(axis)
        ends = count if closed else count - 1
        head = lax.slice_in_dim(cells, 0, width, axis=dim)
        tail = lax.slice_in_dim(cells, cells.shape[dim] - width, cells.shape[dim], axis=dim)
        cells = jnp.concatenate(
            [
                lax.ppermute(tail, axis, [(i, (i + 1) % count) for i in range(ends)]),
                cells,
                lax.ppermute(head, axis, [((i + 1) % count, i) for i in range(ends)]),
            ],
            axis=dim,
        )
    return cells


def build_taps(filter_taps, cycle_counts, cycle_blocks):
    slot_total = cycle_blocks.shape[1]
    width_block = filter_taps.shape[4]
    offsets = jnp.arange(width_block, dtype=jnp.int32)
    places = HALO + width_block * cycle_blocks[:, :, None] + offsets[None, None, :]
    live_slots = jnp.arange(slot_total, dtype=jnp.int32)[None, :] < cycle_counts[:, None]
    positions = jnp.arange(2 * HALO, dtype=jnp.int32)
    onehot = jnp.where(
        (places[:, :, :, None] == positions) & live_slots[:, :, None, None], 1.0, 0.0
    ).astype(jnp.float32)
    return jnp.einsum("ikrst,istu->ikru", filter_taps.astype(jnp.float32), onehot)


def toeplitz_kernel(tap_ref, out_ref):
    kernels, lon_cols, width = out_ref.shape
    window_len = tap_ref.shape[1]
    stencil_rows = width // window_len
    for k in range(kernels):
        for r in range(stencil_rows):
            row = tap_ref[pl.ds(k * stencil_rows + r, 1), :]
            tiled = jnp.broadcast_to(row, (lon_cols, window_len))
            rolled = pltpu.roll(tiled, 0, 1, stride=1, stride_axis=0)
            out_ref[k, :, pl.ds(r * window_len, window_len)] = rolled.astype(out_ref.dtype)


def toeplitz(tap_row, out_width):
    kernels, stencil_rows, reach = tap_row.shape
    window_len = out_width + reach
    padded = jnp.pad(tap_row.astype(jnp.float32), ((0, 0), (0, 0), (0, window_len - reach)))
    padded = padded.reshape(kernels * stencil_rows, window_len)
    out = pl.pallas_call(
        toeplitz_kernel,
        out_shape=jax.ShapeDtypeStruct((kernels, out_width, stencil_rows * window_len), jnp.bfloat16),
    )(padded)
    return out.reshape(kernels * out_width, stencil_rows * window_len)


def lat_allreduce(x, axis, dim):
    count = lax.axis_size(axis)
    if x.shape[dim] % count:
        return lax.psum(x, axis)
    size = x.shape[dim] // count
    gathered = lax.all_to_all(x, axis, dim, dim, tiled=True)
    parts = [lax.slice_in_dim(gathered, s * size, (s + 1) * size, axis=dim) for s in range(count)]
    while len(parts) > 1:
        paired = [parts[2 * e] + parts[2 * e + 1] for e in range(len(parts) // 2)]
        parts = paired + parts[2 * len(paired) :]
    mine = parts[0]
    return lax.all_to_all(jnp.concatenate([mine] * count, axis=dim), axis, dim, dim, tiled=True)


def row_kernel(ext_ref, mt_ref, w_ref, up_ref, out_ref, gt_ref):
    stencil_rows, channels, _ = ext_ref.shape
    n_blocks, o_block, lon_cols = up_ref.shape
    kernels = w_ref.shape[0]
    window_len = mt_ref.shape[1] // stencil_rows
    contract_last = (((1,), (1,)), ((), ()))
    gt_ref[...] = jnp.zeros(gt_ref.shape, gt_ref.dtype)
    for d in range(n_blocks):
        acc = None
        for r in range(stencil_rows):
            win = ext_ref[r, :, pl.ds(d * lon_cols, window_len)]
            part = lax.dot_general(
                win,
                mt_ref[:, pl.ds(r * window_len, window_len)],
                contract_last,
                preferred_element_type=jnp.float32,
            )
            acc = part if acc is None else acc + part
        resp = acc.astype(jnp.bfloat16)
        up_d = up_ref[d]
        for k in range(kernels):
            resp_k = resp[:, k * lon_cols : (k + 1) * lon_cols]
            gt_ref[k] += lax.dot_general(
                up_d, resp_k, contract_last, preferred_element_type=jnp.float32
            )
        if d == 0:
            total = None
            for k in range(kernels):
                term = jnp.dot(
                    w_ref[k],
                    resp[:, k * lon_cols : (k + 1) * lon_cols],
                    preferred_element_type=jnp.float32,
                )
                total = term if total is None else total + term
            out_ref[...] = total.astype(out_ref.dtype)


def row_products(ext, matrix, weights, up_rel):
    stencil_rows, channels, _ = ext.shape
    n_blocks, o_block, lon_cols = up_rel.shape
    kernels = weights.shape[0]
    flops = 2 * n_blocks * channels * matrix.shape[0] * matrix.shape[1]
    flops += 2 * n_blocks * kernels * o_block * lon_cols * channels
    flops += 2 * kernels * weights.shape[1] * channels * lon_cols
    nbytes = 2 * (ext.size + matrix.size + weights.size + up_rel.size)
    nbytes += 2 * weights.shape[1] * lon_cols + 4 * kernels * o_block * channels
    return pl.pallas_call(
        row_kernel,
        out_shape=(
            jax.ShapeDtypeStruct((weights.shape[1], lon_cols), jnp.bfloat16),
            jax.ShapeDtypeStruct((kernels, o_block, channels), jnp.float32),
        ),
        cost_estimate=pl.CostEstimate(flops=flops, transcendentals=0, bytes_accessed=nbytes),
    )(ext, matrix, weights, up_rel)


def body(fields, upstream, weights, filter_taps, cycle_counts, cycle_blocks):
    channels, lat_rows, lon_cols = fields.shape
    kernels = weights.shape[0]
    window_len = lon_cols + 2 * HALO
    n_lon = lax.axis_size("lon")
    lon_at = lax.axis_index("lon")
    tap_table = build_taps(filter_taps, cycle_counts, cycle_blocks).astype(jnp.bfloat16)
    matrix = toeplitz(tap_table[0], lon_cols)
    o_block = upstream.shape[0] // n_lon
    up_row = upstream[:, 0]
    blocks = [fields[:, 0]]
    up_parts = [lax.dynamic_slice_in_dim(up_row, lon_at * o_block, o_block, axis=0)]
    for d in range(1, n_lon):
        part = lax.dynamic_slice_in_dim(up_row, ((lon_at - d) % n_lon) * o_block, o_block, axis=0)
        both = lax.ppermute(
            jnp.concatenate([fields[:, 0], part], axis=0),
            "lon",
            [(p, (p - d) % n_lon) for p in range(n_lon)],
        )
        blocks.append(both[:channels])
        up_parts.append(both[channels:])
    up_rel = jnp.stack(up_parts, axis=0)
    row = jnp.concatenate(blocks, axis=1)
    count = lax.axis_size("lat")
    below = lax.ppermute(row, "lat", [(i, i + 1) for i in range(count - 1)])
    above = lax.ppermute(row, "lat", [(i + 1, i) for i in range(count - 1)])
    rows = jnp.stack([below, row, above], axis=0)
    ext = jnp.concatenate([rows[:, :, rows.shape[2] - HALO :], rows, rows[:, :, :HALO]], axis=2)
    response_grad = jnp.einsum(
        "koc,oij->cikj", weights, upstream, preferred_element_type=jnp.float32
    ).astype(jnp.bfloat16)
    out_row, grad_terms = row_products(ext, matrix, weights, up_rel)
    outputs = out_row[:, None, :]
    weight_grad = lat_allreduce(grad_terms, "lat", 1)
    accumulated = jnp.zeros((channels, lat_rows + 2, window_len), jnp.float32)
    cycle_row = 0
    grad_piece = response_grad[:, cycle_row].reshape(channels, kernels * lon_cols)
    contrib = jnp.dot(grad_piece, matrix, preferred_element_type=jnp.float32)
    accumulated = accumulated.at[:, cycle_row : cycle_row + 3].add(
        contrib.reshape(channels, 3, window_len)
    )
    rim_columns = jnp.concatenate(
        [accumulated[:, :, :HALO], accumulated[:, :, HALO + lon_cols :]], axis=2
    )
    arrived = padded_2(rim_columns, (("lon", 2),), HALO, True)
    interior = accumulated[:, :, HALO : HALO + lon_cols]
    interior = interior.at[:, :, :HALO].add(arrived[:, :, :HALO])
    interior = interior.at[:, :, lon_cols - HALO :].add(arrived[:, :, 3 * HALO :])
    edge_rows = jnp.stack([interior[:, 0], interior[:, lat_rows + 1]], axis=1)
    arrived = padded_2(edge_rows, (("lat", 1),), 1, False)
    result = interior[:, 1 : lat_rows + 1]
    result = result.at[:, 0].add(arrived[:, 0])
    result = result.at[:, lat_rows - 1].add(arrived[:, 3])
    return (outputs, result.astype(jnp.bfloat16), weight_grad)


def solution(mesh):
    return jax.shard_map(
        body,
        mesh=mesh,
        in_specs=(
            P("groups", "lat", "lon"),
            P("groups", "lat", "lon"),
            P(),
            P("lat", None, None, None, None),
            P("lat"),
            P("lat", None),
        ),
        out_specs=(P("groups", "lat", "lon"), P("groups", "lat", "lon"), P("groups", "lon", None)),
        check_vma=False,
    )
```

```python
import jax
import jax.numpy as jnp
from jax import lax
from jax.experimental import pallas as pl
from jax.experimental.pallas import tpu as pltpu
from jax.sharding import PartitionSpec as P

HALO = 128


def padded_2(cells, sides, width, closed):
    for axis, dim in sides:
        count = lax.axis_size(axis)
        ends = count if closed else count - 1
        head = lax.slice_in_dim(cells, 0, width, axis=dim)
        tail = lax.slice_in_dim(cells, cells.shape[dim] - width, cells.shape[dim], axis=dim)
        cells = jnp.concatenate(
            [
                lax.ppermute(tail, axis, [(i, (i + 1) % count) for i in range(ends)]),
                cells,
                lax.ppermute(head, axis, [((i + 1) % count, i) for i in range(ends)]),
            ],
            axis=dim,
        )
    return cells


def build_taps(filter_taps, cycle_counts, cycle_blocks):
    slot_total = cycle_blocks.shape[1]
    width_block = filter_taps.shape[4]
    offsets = jnp.arange(width_block, dtype=jnp.int32)
    places = HALO + width_block * cycle_blocks[:, :, None] + offsets[None, None, :]
    live_slots = jnp.arange(slot_total, dtype=jnp.int32)[None, :] < cycle_counts[:, None]
    positions = jnp.arange(2 * HALO, dtype=jnp.int32)
    onehot = jnp.where(
        (places[:, :, :, None] == positions) & live_slots[:, :, None, None], 1.0, 0.0
    ).astype(jnp.float32)
    return jnp.einsum("ikrst,istu->ikru", filter_taps.astype(jnp.float32), onehot)


def toeplitz_kernel(tap_ref, grad_ref, out_ref, contrib_ref):
    kernels, lon_cols, width = out_ref.shape
    window_len = tap_ref.shape[1]
    stencil_rows = width // window_len
    acc = None
    for k in range(kernels):
        for r in range(stencil_rows):
            row = tap_ref[pl.ds(k * stencil_rows + r, 1), :]
            tiled = jnp.broadcast_to(row, (lon_cols, window_len))
            rolled = pltpu.roll(tiled, 0, 1, stride=1, stride_axis=0)
            out_ref[k, :, pl.ds(r * window_len, window_len)] = rolled.astype(out_ref.dtype)
        term = jnp.dot(
            grad_ref[:, pl.ds(k * lon_cols, lon_cols)],
            out_ref[k],
            preferred_element_type=jnp.float32,
        )
        acc = term if acc is None else acc + term
    contrib_ref[...] = acc


def toeplitz(tap_row, out_width, grad_piece):
    kernels, stencil_rows, reach = tap_row.shape
    window_len = out_width + reach
    padded = jnp.pad(tap_row.astype(jnp.float32), ((0, 0), (0, 0), (0, window_len - reach)))
    padded = padded.reshape(kernels * stencil_rows, window_len)
    out, contrib = pl.pallas_call(
        toeplitz_kernel,
        out_shape=(
            jax.ShapeDtypeStruct((kernels, out_width, stencil_rows * window_len), jnp.bfloat16),
            jax.ShapeDtypeStruct((grad_piece.shape[0], stencil_rows * window_len), jnp.float32),
        ),
    )(padded, grad_piece)
    return out.reshape(kernels * out_width, stencil_rows * window_len), contrib


def lat_allreduce(x, axis, dim):
    count = lax.axis_size(axis)
    steps = count.bit_length() - 1
    if (1 << steps) != count or x.shape[dim] % count:
        return lax.psum(x, axis)
    index = lax.axis_index(axis)
    size = x.shape[dim] // count
    parts = [lax.dynamic_slice_in_dim(x, index * size, size, axis=dim)]
    for d in range(1, count):
        send = lax.dynamic_slice_in_dim(x, (index ^ d) * size, size, axis=dim)
        parts.append(lax.ppermute(send, axis, [(i, i ^ d) for i in range(count)]))
    for s in range(steps):
        parts = [parts[2 * e] + parts[2 * e + 1] for e in range(len(parts) // 2)]
    mine = parts[0]
    out = jnp.zeros(x.shape, x.dtype)
    out = lax.dynamic_update_slice_in_dim(out, mine, index * size, axis=dim)
    for d in range(1, count):
        recv = lax.ppermute(mine, axis, [(i, i ^ d) for i in range(count)])
        out = lax.dynamic_update_slice_in_dim(out, recv, (index ^ d) * size, axis=dim)
    return out


def row_kernel(ext_ref, mt_ref, w_ref, up_ref, out_ref, gt_ref):
    stencil_rows, channels, _ = ext_ref.shape
    n_blocks, o_block, lon_cols = up_ref.shape
    kernels = w_ref.shape[0]
    window_len = mt_ref.shape[1] // stencil_rows
    contract_last = (((1,), (1,)), ((), ()))
    gt_ref[...] = jnp.zeros(gt_ref.shape, gt_ref.dtype)
    for d in range(n_blocks):
        acc = None
        for r in range(stencil_rows):
            win = ext_ref[r, :, pl.ds(d * lon_cols, window_len)]
            part = lax.dot_general(
                win,
                mt_ref[:, pl.ds(r * window_len, window_len)],
                contract_last,
                preferred_element_type=jnp.float32,
            )
            acc = part if acc is None else acc + part
        resp = acc.astype(jnp.bfloat16)
        up_d = up_ref[d]
        for k in range(kernels):
            resp_k = resp[:, k * lon_cols : (k + 1) * lon_cols]
            gt_ref[k] += lax.dot_general(
                up_d, resp_k, contract_last, preferred_element_type=jnp.float32
            )
        if d == 0:
            total = None
            for k in range(kernels):
                term = jnp.dot(
                    w_ref[k],
                    resp[:, k * lon_cols : (k + 1) * lon_cols],
                    preferred_element_type=jnp.float32,
                )
                total = term if total is None else total + term
            out_ref[...] = total.astype(out_ref.dtype)


def row_products(ext, matrix, weights, up_rel):
    stencil_rows, channels, _ = ext.shape
    n_blocks, o_block, lon_cols = up_rel.shape
    kernels = weights.shape[0]
    flops = 2 * n_blocks * channels * matrix.shape[0] * matrix.shape[1]
    flops += 2 * n_blocks * kernels * o_block * lon_cols * channels
    flops += 2 * kernels * weights.shape[1] * channels * lon_cols
    nbytes = 2 * (ext.size + matrix.size + weights.size + up_rel.size)
    nbytes += 2 * weights.shape[1] * lon_cols + 4 * kernels * o_block * channels
    return pl.pallas_call(
        row_kernel,
        out_shape=(
            jax.ShapeDtypeStruct((weights.shape[1], lon_cols), jnp.bfloat16),
            jax.ShapeDtypeStruct((kernels, o_block, channels), jnp.float32),
        ),
        cost_estimate=pl.CostEstimate(flops=flops, transcendentals=0, bytes_accessed=nbytes),
    )(ext, matrix, weights, up_rel)


def body(fields, upstream, weights, filter_taps, cycle_counts, cycle_blocks):
    channels, lat_rows, lon_cols = fields.shape
    kernels = weights.shape[0]
    window_len = lon_cols + 2 * HALO
    n_lon = lax.axis_size("lon")
    lon_at = lax.axis_index("lon")
    tap_table = build_taps(filter_taps, cycle_counts, cycle_blocks).astype(jnp.bfloat16)
    response_grad = jnp.einsum(
        "koc,oij->cikj", weights, upstream, preferred_element_type=jnp.float32
    ).astype(jnp.bfloat16)
    grad_piece = response_grad[:, 0].reshape(channels, kernels * lon_cols)
    matrix, contrib = toeplitz(tap_table[0], lon_cols, grad_piece)
    o_block = upstream.shape[0] // n_lon
    up_row = upstream[:, 0]
    blocks = [fields[:, 0]]
    up_parts = [lax.dynamic_slice_in_dim(up_row, lon_at * o_block, o_block, axis=0)]
    for d in range(1, n_lon):
        part = lax.dynamic_slice_in_dim(up_row, ((lon_at - d) % n_lon) * o_block, o_block, axis=0)
        both = lax.ppermute(
            jnp.concatenate([fields[:, 0], part], axis=0),
            "lon",
            [(p, (p - d) % n_lon) for p in range(n_lon)],
        )
        blocks.append(both[:channels])
        up_parts.append(both[channels:])
    up_rel = jnp.stack(up_parts, axis=0)
    row = jnp.concatenate(blocks, axis=1)
    count = lax.axis_size("lat")
    below = lax.ppermute(row, "lat", [(i, i + 1) for i in range(count - 1)])
    above = lax.ppermute(row, "lat", [(i + 1, i) for i in range(count - 1)])
    rows = jnp.stack([below, row, above], axis=0)
    ext = jnp.concatenate([rows[:, :, rows.shape[2] - HALO :], rows, rows[:, :, :HALO]], axis=2)
    out_row, grad_terms = row_products(ext, matrix, weights, up_rel)
    outputs = out_row[:, None, :]
    weight_grad = lat_allreduce(grad_terms, "lat", 1)
    accumulated = jnp.zeros((channels, lat_rows + 2, window_len), jnp.float32)
    cycle_row = 0
    accumulated = accumulated.at[:, cycle_row : cycle_row + 3].add(
        contrib.reshape(channels, 3, window_len)
    )
    rim_columns = jnp.concatenate(
        [accumulated[:, :, :HALO], accumulated[:, :, HALO + lon_cols :]], axis=2
    )
    arrived = padded_2(rim_columns, (("lon", 2),), HALO, True)
    interior = accumulated[:, :, HALO : HALO + lon_cols]
    interior = interior.at[:, :, :HALO].add(arrived[:, :, :HALO])
    interior = interior.at[:, :, lon_cols - HALO :].add(arrived[:, :, 3 * HALO :])
    edge_rows = jnp.stack([interior[:, 0], interior[:, lat_rows + 1]], axis=1)
    arrived = padded_2(edge_rows, (("lat", 1),), 1, False)
    result = interior[:, 1 : lat_rows + 1]
    result = result.at[:, 0].add(arrived[:, 0])
    result = result.at[:, lat_rows - 1].add(arrived[:, 3])
    return (outputs, result.astype(jnp.bfloat16), weight_grad)


def solution(mesh):
    return jax.shard_map(
        body,
        mesh=mesh,
        in_specs=(
            P("groups", "lat", "lon"),
            P("groups", "lat", "lon"),
            P(),
            P("lat", None, None, None, None),
            P("lat"),
            P("lat", None),
        ),
        out_specs=(P("groups", "lat", "lon"), P("groups", "lat", "lon"), P("groups", "lon", None)),
        check_vma=False,
    )
```

```python
import jax
import jax.numpy as jnp
from jax import lax
from jax.experimental import pallas as pl
from jax.experimental.pallas import tpu as pltpu
from jax.sharding import PartitionSpec as P

HALO = 128


def padded_2(cells, sides, width, closed):
    for axis, dim in sides:
        count = lax.axis_size(axis)
        ends = count if closed else count - 1
        head = lax.slice_in_dim(cells, 0, width, axis=dim)
        tail = lax.slice_in_dim(cells, cells.shape[dim] - width, cells.shape[dim], axis=dim)
        cells = jnp.concatenate(
            [
                lax.ppermute(tail, axis, [(i, (i + 1) % count) for i in range(ends)]),
                cells,
                lax.ppermute(head, axis, [((i + 1) % count, i) for i in range(ends)]),
            ],
            axis=dim,
        )
    return cells


def build_taps(filter_taps, cycle_counts, cycle_blocks):
    slot_total = cycle_blocks.shape[1]
    width_block = filter_taps.shape[4]
    offsets = jnp.arange(width_block, dtype=jnp.int32)
    places = HALO + width_block * cycle_blocks[:, :, None] + offsets[None, None, :]
    live_slots = jnp.arange(slot_total, dtype=jnp.int32)[None, :] < cycle_counts[:, None]
    positions = jnp.arange(2 * HALO, dtype=jnp.int32)
    onehot = jnp.where(
        (places[:, :, :, None] == positions) & live_slots[:, :, None, None], 1.0, 0.0
    ).astype(jnp.float32)
    return jnp.einsum("ikrst,istu->ikru", filter_taps.astype(jnp.float32), onehot)


def toeplitz_kernel(tap_ref, grad_ref, out_ref, contrib_ref):
    kernels, lon_cols, width = out_ref.shape
    window_len = tap_ref.shape[1]
    stencil_rows = width // window_len
    acc = None
    for k in range(kernels):
        for r in range(stencil_rows):
            row = tap_ref[pl.ds(k * stencil_rows + r, 1), :]
            tiled = jnp.broadcast_to(row, (lon_cols, window_len))
            rolled = pltpu.roll(tiled, 0, 1, stride=1, stride_axis=0)
            out_ref[k, :, pl.ds(r * window_len, window_len)] = rolled.astype(out_ref.dtype)
        term = jnp.dot(
            grad_ref[:, pl.ds(k * lon_cols, lon_cols)],
            out_ref[k],
            preferred_element_type=jnp.float32,
        )
        acc = term if acc is None else acc + term
    contrib_ref[...] = acc


def toeplitz(tap_row, out_width, grad_piece):
    kernels, stencil_rows, reach = tap_row.shape
    window_len = out_width + reach
    padded = jnp.pad(tap_row.astype(jnp.float32), ((0, 0), (0, 0), (0, window_len - reach)))
    padded = padded.reshape(kernels * stencil_rows, window_len)
    out, contrib = pl.pallas_call(
        toeplitz_kernel,
        out_shape=(
            jax.ShapeDtypeStruct((kernels, out_width, stencil_rows * window_len), jnp.bfloat16),
            jax.ShapeDtypeStruct((grad_piece.shape[0], stencil_rows * window_len), jnp.float32),
        ),
    )(padded, grad_piece)
    return out.reshape(kernels * out_width, stencil_rows * window_len), contrib


def lat_allreduce(x, axis, dim):
    count = lax.axis_size(axis)
    steps = count.bit_length() - 1
    if (1 << steps) != count or x.shape[dim] % count:
        return lax.psum(x, axis)
    index = lax.axis_index(axis)
    size = x.shape[dim] // count
    parts = [lax.dynamic_slice_in_dim(x, index * size, size, axis=dim)]
    for d in range(1, count):
        send = lax.dynamic_slice_in_dim(x, (index ^ d) * size, size, axis=dim)
        parts.append(lax.ppermute(send, axis, [(i, i ^ d) for i in range(count)]))
    for s in range(steps):
        parts = [parts[2 * e] + parts[2 * e + 1] for e in range(len(parts) // 2)]
    mine = parts[0]
    out = jnp.zeros(x.shape, x.dtype)
    out = lax.dynamic_update_slice_in_dim(out, mine, index * size, axis=dim)
    for d in range(1, count):
        recv = lax.ppermute(mine, axis, [(i, i ^ d) for i in range(count)])
        out = lax.dynamic_update_slice_in_dim(out, recv, (index ^ d) * size, axis=dim)
    return out


def row_kernel(ext_ref, mt_ref, w_ref, up_ref, out_ref, gt_ref):
    stencil_rows, _, channels = ext_ref.shape
    n_blocks, o_block, lon_cols = up_ref.shape
    kernels = w_ref.shape[0]
    window_len = mt_ref.shape[1] // stencil_rows
    contract_last = (((1,), (1,)), ((), ()))
    gt_ref[...] = jnp.zeros(gt_ref.shape, gt_ref.dtype)
    for d in range(n_blocks):
        acc = None
        for r in range(stencil_rows):
            part = jnp.dot(
                mt_ref[:, pl.ds(r * window_len, window_len)],
                ext_ref[r, pl.ds(d * lon_cols, window_len), :],
                preferred_element_type=jnp.float32,
            )
            acc = part if acc is None else acc + part
        resp_t = acc.astype(jnp.bfloat16)
        up_d = up_ref[d]
        for k in range(kernels):
            gt_ref[k] += jnp.dot(
                up_d, resp_t[k * lon_cols : (k + 1) * lon_cols], preferred_element_type=jnp.float32
            )
        if d == 0:
            total = None
            for k in range(kernels):
                term = lax.dot_general(
                    w_ref[k],
                    resp_t[k * lon_cols : (k + 1) * lon_cols],
                    contract_last,
                    preferred_element_type=jnp.float32,
                )
                total = term if total is None else total + term
            out_ref[...] = total.astype(out_ref.dtype)


def row_products(ext_t, matrix, weights, up_rel):
    stencil_rows, _, channels = ext_t.shape
    n_blocks, o_block, lon_cols = up_rel.shape
    kernels = weights.shape[0]
    flops = 2 * n_blocks * channels * matrix.shape[0] * matrix.shape[1]
    flops += 2 * n_blocks * kernels * o_block * lon_cols * channels
    flops += 2 * kernels * weights.shape[1] * channels * lon_cols
    nbytes = 2 * (ext_t.size + matrix.size + weights.size + up_rel.size)
    nbytes += 2 * weights.shape[1] * lon_cols + 4 * kernels * o_block * channels
    return pl.pallas_call(
        row_kernel,
        out_shape=(
            jax.ShapeDtypeStruct((weights.shape[1], lon_cols), jnp.bfloat16),
            jax.ShapeDtypeStruct((kernels, o_block, channels), jnp.float32),
        ),
        cost_estimate=pl.CostEstimate(flops=flops, transcendentals=0, bytes_accessed=nbytes),
    )(ext_t, matrix, weights, up_rel)


def body(fields, upstream, weights, filter_taps, cycle_counts, cycle_blocks):
    channels, lat_rows, lon_cols = fields.shape
    kernels = weights.shape[0]
    window_len = lon_cols + 2 * HALO
    n_lon = lax.axis_size("lon")
    lon_at = lax.axis_index("lon")
    tap_table = build_taps(filter_taps, cycle_counts, cycle_blocks).astype(jnp.bfloat16)
    response_grad = jnp.einsum(
        "koc,oij->cikj", weights, upstream, preferred_element_type=jnp.float32
    ).astype(jnp.bfloat16)
    grad_piece = response_grad[:, 0].reshape(channels, kernels * lon_cols)
    o_block = upstream.shape[0] // n_lon
    up_row = upstream[:, 0]
    blocks = [fields[:, 0]]
    up_parts = [lax.dynamic_slice_in_dim(up_row, lon_at * o_block, o_block, axis=0)]
    for d in range(1, n_lon):
        part = lax.dynamic_slice_in_dim(up_row, ((lon_at - d) % n_lon) * o_block, o_block, axis=0)
        both = lax.ppermute(
            jnp.concatenate([fields[:, 0], part], axis=0),
            "lon",
            [(p, (p - d) % n_lon) for p in range(n_lon)],
        )
        blocks.append(both[:channels])
        up_parts.append(both[channels:])
    up_rel = jnp.stack(up_parts, axis=0)
    row = jnp.concatenate(blocks, axis=1)
    row, tap_row, grad_piece = lax.optimization_barrier((row, tap_table[0], grad_piece))
    count = lax.axis_size("lat")
    below = lax.ppermute(row, "lat", [(i, i + 1) for i in range(count - 1)])
    above = lax.ppermute(row, "lat", [(i + 1, i) for i in range(count - 1)])
    matrix, contrib = toeplitz(tap_row, lon_cols, grad_piece)
    rows = jnp.stack([below, row, above], axis=0).transpose(0, 2, 1)
    ext_t = jnp.concatenate([rows[:, rows.shape[1] - HALO :], rows, rows[:, :HALO]], axis=1)
    out_row, grad_terms = row_products(ext_t, matrix, weights, up_rel)
    outputs = out_row[:, None, :]
    weight_grad = lat_allreduce(grad_terms, "lat", 1)
    accumulated = jnp.zeros((channels, lat_rows + 2, window_len), jnp.float32)
    cycle_row = 0
    accumulated = accumulated.at[:, cycle_row : cycle_row + 3].add(
        contrib.reshape(channels, 3, window_len)
    )
    rim_columns = jnp.concatenate(
        [accumulated[:, :, :HALO], accumulated[:, :, HALO + lon_cols :]], axis=2
    )
    arrived = padded_2(rim_columns, (("lon", 2),), HALO, True)
    interior = accumulated[:, :, HALO : HALO + lon_cols]
    interior = interior.at[:, :, :HALO].add(arrived[:, :, :HALO])
    interior = interior.at[:, :, lon_cols - HALO :].add(arrived[:, :, 3 * HALO :])
    edge_rows = jnp.stack([interior[:, 0], interior[:, lat_rows + 1]], axis=1)
    arrived = padded_2(edge_rows, (("lat", 1),), 1, False)
    result = interior[:, 1 : lat_rows + 1]
    result = result.at[:, 0].add(arrived[:, 0])
    result = result.at[:, lat_rows - 1].add(arrived[:, 3])
    return (outputs, result.astype(jnp.bfloat16), weight_grad)


def solution(mesh):
    return jax.shard_map(
        body,
        mesh=mesh,
        in_specs=(
            P("groups", "lat", "lon"),
            P("groups", "lat", "lon"),
            P(),
            P("lat", None, None, None, None),
            P("lat"),
            P("lat", None),
        ),
        out_specs=(P("groups", "lat", "lon"), P("groups", "lat", "lon"), P("groups", "lon", None)),
        check_vma=False,
    )
```

```python
import jax
import jax.numpy as jnp
from jax import lax
from jax.experimental import pallas as pl
from jax.experimental.pallas import tpu as pltpu
from jax.sharding import PartitionSpec as P

HALO = 128


def padded_2(cells, sides, width, closed):
    for axis, dim in sides:
        count = lax.axis_size(axis)
        ends = count if closed else count - 1
        head = lax.slice_in_dim(cells, 0, width, axis=dim)
        tail = lax.slice_in_dim(cells, cells.shape[dim] - width, cells.shape[dim], axis=dim)
        cells = jnp.concatenate(
            [
                lax.ppermute(tail, axis, [(i, (i + 1) % count) for i in range(ends)]),
                cells,
                lax.ppermute(head, axis, [((i + 1) % count, i) for i in range(ends)]),
            ],
            axis=dim,
        )
    return cells


def build_taps(filter_taps, cycle_counts, cycle_blocks):
    slot_total = cycle_blocks.shape[1]
    width_block = filter_taps.shape[4]
    offsets = jnp.arange(width_block, dtype=jnp.int32)
    places = HALO + width_block * cycle_blocks[:, :, None] + offsets[None, None, :]
    live_slots = jnp.arange(slot_total, dtype=jnp.int32)[None, :] < cycle_counts[:, None]
    positions = jnp.arange(2 * HALO, dtype=jnp.int32)
    onehot = jnp.where(
        (places[:, :, :, None] == positions) & live_slots[:, :, None, None], 1.0, 0.0
    ).astype(jnp.float32)
    return jnp.einsum("ikrst,istu->ikru", filter_taps.astype(jnp.float32), onehot)


def toeplitz_kernel(tap_ref, grad_ref, out_ref, contrib_ref):
    kernels, lon_cols, width = out_ref.shape
    window_len = tap_ref.shape[1]
    stencil_rows = width // window_len
    acc = None
    for k in range(kernels):
        for r in range(stencil_rows):
            row = tap_ref[pl.ds(k * stencil_rows + r, 1), :]
            tiled = jnp.broadcast_to(row, (lon_cols, window_len))
            rolled = pltpu.roll(tiled, 0, 1, stride=1, stride_axis=0)
            out_ref[k, :, pl.ds(r * window_len, window_len)] = rolled.astype(out_ref.dtype)
        term = jnp.dot(
            grad_ref[:, pl.ds(k * lon_cols, lon_cols)],
            out_ref[k],
            preferred_element_type=jnp.float32,
        )
        acc = term if acc is None else acc + term
    contrib_ref[...] = acc


def toeplitz(tap_row, out_width, grad_piece):
    kernels, stencil_rows, reach = tap_row.shape
    window_len = out_width + reach
    padded = jnp.pad(tap_row.astype(jnp.float32), ((0, 0), (0, 0), (0, window_len - reach)))
    padded = padded.reshape(kernels * stencil_rows, window_len)
    out, contrib = pl.pallas_call(
        toeplitz_kernel,
        out_shape=(
            jax.ShapeDtypeStruct((kernels, out_width, stencil_rows * window_len), jnp.bfloat16),
            jax.ShapeDtypeStruct((grad_piece.shape[0], stencil_rows * window_len), jnp.float32),
        ),
    )(padded, grad_piece)
    return out.reshape(kernels * out_width, stencil_rows * window_len), contrib


def lat_allreduce(x, axis, dim):
    count = lax.axis_size(axis)
    steps = count.bit_length() - 1
    if (1 << steps) != count or x.shape[dim] % count:
        return lax.psum(x, axis)
    index = lax.axis_index(axis)
    size = x.shape[dim] // count
    parts = [lax.dynamic_slice_in_dim(x, index * size, size, axis=dim)]
    for d in range(1, count):
        send = lax.dynamic_slice_in_dim(x, (index ^ d) * size, size, axis=dim)
        parts.append(lax.ppermute(send, axis, [(i, i ^ d) for i in range(count)]))
    for s in range(steps):
        parts = [parts[2 * e] + parts[2 * e + 1] for e in range(len(parts) // 2)]
    mine = parts[0]
    out = jnp.zeros(x.shape, x.dtype)
    out = lax.dynamic_update_slice_in_dim(out, mine, index * size, axis=dim)
    for d in range(1, count):
        recv = lax.ppermute(mine, axis, [(i, i ^ d) for i in range(count)])
        out = lax.dynamic_update_slice_in_dim(out, recv, (index ^ d) * size, axis=dim)
    return out


def row_kernel(ext_ref, mt_ref, w_ref, up_ref, out_ref, gt_ref):
    stencil_rows, channels, _ = ext_ref.shape
    n_blocks, o_block, lon_cols = up_ref.shape
    kernels = w_ref.shape[0]
    window_len = mt_ref.shape[1] // stencil_rows
    contract_last = (((1,), (1,)), ((), ()))
    gt_ref[...] = jnp.zeros(gt_ref.shape, gt_ref.dtype)
    for d in range(n_blocks):
        acc = None
        for r in range(stencil_rows):
            win = ext_ref[r, :, pl.ds(d * lon_cols, window_len)]
            part = lax.dot_general(
                win,
                mt_ref[:, pl.ds(r * window_len, window_len)],
                contract_last,
                preferred_element_type=jnp.float32,
            )
            acc = part if acc is None else acc + part
        resp = acc.astype(jnp.bfloat16)
        up_d = up_ref[d]
        for k in range(kernels):
            resp_k = resp[:, k * lon_cols : (k + 1) * lon_cols]
            gt_ref[k] += lax.dot_general(
                up_d, resp_k, contract_last, preferred_element_type=jnp.float32
            )
        if d == 0:
            total = None
            for k in range(kernels):
                term = jnp.dot(
                    w_ref[k],
                    resp[:, k * lon_cols : (k + 1) * lon_cols],
                    preferred_element_type=jnp.float32,
                )
                total = term if total is None else total + term
            out_ref[...] = total.astype(out_ref.dtype)


def row_products(ext, matrix, weights, up_rel):
    stencil_rows, channels, _ = ext.shape
    n_blocks, o_block, lon_cols = up_rel.shape
    kernels = weights.shape[0]
    flops = 2 * n_blocks * channels * matrix.shape[0] * matrix.shape[1]
    flops += 2 * n_blocks * kernels * o_block * lon_cols * channels
    flops += 2 * kernels * weights.shape[1] * channels * lon_cols
    nbytes = 2 * (ext.size + matrix.size + weights.size + up_rel.size)
    nbytes += 2 * weights.shape[1] * lon_cols + 4 * kernels * o_block * channels
    return pl.pallas_call(
        row_kernel,
        out_shape=(
            jax.ShapeDtypeStruct((weights.shape[1], lon_cols), jnp.bfloat16),
            jax.ShapeDtypeStruct((kernels, o_block, channels), jnp.float32),
        ),
        cost_estimate=pl.CostEstimate(flops=flops, transcendentals=0, bytes_accessed=nbytes),
    )(ext, matrix, weights, up_rel)


def body(fields, upstream, weights, filter_taps, cycle_counts, cycle_blocks):
    channels, lat_rows, lon_cols = fields.shape
    kernels = weights.shape[0]
    window_len = lon_cols + 2 * HALO
    n_lon = lax.axis_size("lon")
    lon_at = lax.axis_index("lon")
    tap_table = build_taps(filter_taps, cycle_counts, cycle_blocks).astype(jnp.bfloat16)
    response_grad = jnp.einsum(
        "koc,oij->cikj", weights, upstream, preferred_element_type=jnp.float32
    ).astype(jnp.bfloat16)
    grad_piece = response_grad[:, 0].reshape(channels, kernels * lon_cols)
    o_block = upstream.shape[0] // n_lon
    up_row = upstream[:, 0]
    blocks = [fields[:, 0]]
    up_parts = [lax.dynamic_slice_in_dim(up_row, lon_at * o_block, o_block, axis=0)]
    for d in range(1, n_lon):
        part = lax.dynamic_slice_in_dim(up_row, ((lon_at - d) % n_lon) * o_block, o_block, axis=0)
        both = lax.ppermute(
            jnp.concatenate([fields[:, 0], part], axis=0),
            "lon",
            [(p, (p - d) % n_lon) for p in range(n_lon)],
        )
        blocks.append(both[:channels])
        up_parts.append(both[channels:])
    up_rel = jnp.stack(up_parts, axis=0)
    row = jnp.concatenate(blocks, axis=1)
    row, tap_row, grad_piece = lax.optimization_barrier((row, tap_table[0], grad_piece))
    count = lax.axis_size("lat")
    below = lax.ppermute(row, "lat", [(i, i + 1) for i in range(count - 1)])
    above = lax.ppermute(row, "lat", [(i + 1, i) for i in range(count - 1)])
    matrix, contrib = toeplitz(tap_row, lon_cols, grad_piece)
    rows = jnp.stack([below, row, above], axis=0)
    ext = jnp.concatenate([rows[:, :, rows.shape[2] - HALO :], rows, rows[:, :, :HALO]], axis=2)
    out_row, grad_terms = row_products(ext, matrix, weights, up_rel)
    outputs = out_row[:, None, :]
    weight_grad = lat_allreduce(grad_terms, "lat", 1)
    accumulated = jnp.zeros((channels, lat_rows + 2, window_len), jnp.float32)
    cycle_row = 0
    accumulated = accumulated.at[:, cycle_row : cycle_row + 3].add(
        contrib.reshape(channels, 3, window_len)
    )
    rim_columns = jnp.concatenate(
        [accumulated[:, :, :HALO], accumulated[:, :, HALO + lon_cols :]], axis=2
    )
    arrived = padded_2(rim_columns, (("lon", 2),), HALO, True)
    interior = accumulated[:, :, HALO : HALO + lon_cols]
    interior = interior.at[:, :, :HALO].add(arrived[:, :, :HALO])
    interior = interior.at[:, :, lon_cols - HALO :].add(arrived[:, :, 3 * HALO :])
    edge_rows = jnp.stack([interior[:, 0], interior[:, lat_rows + 1]], axis=1)
    arrived = padded_2(edge_rows, (("lat", 1),), 1, False)
    result = interior[:, 1 : lat_rows + 1]
    result = result.at[:, 0].add(arrived[:, 0])
    result = result.at[:, lat_rows - 1].add(arrived[:, 3])
    return (outputs, result.astype(jnp.bfloat16), weight_grad)


def solution(mesh):
    return jax.shard_map(
        body,
        mesh=mesh,
        in_specs=(
            P("groups", "lat", "lon"),
            P("groups", "lat", "lon"),
            P(),
            P("lat", None, None, None, None),
            P("lat"),
            P("lat", None),
        ),
        out_specs=(P("groups", "lat", "lon"), P("groups", "lat", "lon"), P("groups", "lon", None)),
        check_vma=False,
    )
```

```python
import jax
import jax.numpy as jnp
from jax import lax
from jax.experimental import pallas as pl
from jax.experimental.pallas import tpu as pltpu
from jax.sharding import PartitionSpec as P

HALO = 128


def padded_2(cells, sides, width, closed):
    for axis, dim in sides:
        count = lax.axis_size(axis)
        ends = count if closed else count - 1
        head = lax.slice_in_dim(cells, 0, width, axis=dim)
        tail = lax.slice_in_dim(cells, cells.shape[dim] - width, cells.shape[dim], axis=dim)
        cells = jnp.concatenate(
            [
                lax.ppermute(tail, axis, [(i, (i + 1) % count) for i in range(ends)]),
                cells,
                lax.ppermute(head, axis, [((i + 1) % count, i) for i in range(ends)]),
            ],
            axis=dim,
        )
    return cells


def build_taps(filter_taps, cycle_counts, cycle_blocks):
    slot_total = cycle_blocks.shape[1]
    width_block = filter_taps.shape[4]
    offsets = jnp.arange(width_block, dtype=jnp.int32)
    places = HALO + width_block * cycle_blocks[:, :, None] + offsets[None, None, :]
    live_slots = jnp.arange(slot_total, dtype=jnp.int32)[None, :] < cycle_counts[:, None]
    positions = jnp.arange(2 * HALO, dtype=jnp.int32)
    onehot = jnp.where(
        (places[:, :, :, None] == positions) & live_slots[:, :, None, None], 1.0, 0.0
    ).astype(jnp.float32)
    return jnp.einsum("ikrst,istu->ikru", filter_taps.astype(jnp.float32), onehot)


def toeplitz_kernel(tap_ref, grad_ref, out_ref, contrib_ref):
    kernels, lon_cols, width = out_ref.shape
    window_len = tap_ref.shape[1]
    stencil_rows = width // window_len
    acc = None
    for k in range(kernels):
        for r in range(stencil_rows):
            row = tap_ref[pl.ds(k * stencil_rows + r, 1), :]
            tiled = jnp.broadcast_to(row, (lon_cols, window_len))
            rolled = pltpu.roll(tiled, 0, 1, stride=1, stride_axis=0)
            out_ref[k, :, pl.ds(r * window_len, window_len)] = rolled.astype(out_ref.dtype)
        term = jnp.dot(
            grad_ref[:, pl.ds(k * lon_cols, lon_cols)],
            out_ref[k],
            preferred_element_type=jnp.float32,
        )
        acc = term if acc is None else acc + term
    contrib_ref[...] = acc


def toeplitz(tap_row, out_width, grad_piece):
    kernels, stencil_rows, reach = tap_row.shape
    window_len = out_width + reach
    padded = jnp.pad(tap_row.astype(jnp.float32), ((0, 0), (0, 0), (0, window_len - reach)))
    padded = padded.reshape(kernels * stencil_rows, window_len)
    out, contrib = pl.pallas_call(
        toeplitz_kernel,
        out_shape=(
            jax.ShapeDtypeStruct((kernels, out_width, stencil_rows * window_len), jnp.bfloat16),
            jax.ShapeDtypeStruct((grad_piece.shape[0], stencil_rows * window_len), jnp.float32),
        ),
    )(padded, grad_piece)
    return out.reshape(kernels * out_width, stencil_rows * window_len), contrib


def lat_allreduce(x, axis, dim):
    count = lax.axis_size(axis)
    steps = count.bit_length() - 1
    if (1 << steps) != count or x.shape[dim] % count:
        return lax.psum(x, axis)
    index = lax.axis_index(axis)
    size = x.shape[dim] // count
    parts = [lax.dynamic_slice_in_dim(x, index * size, size, axis=dim)]
    for d in range(1, count):
        send = lax.dynamic_slice_in_dim(x, (index ^ d) * size, size, axis=dim)
        parts.append(lax.ppermute(send, axis, [(i, i ^ d) for i in range(count)]))
    for s in range(steps):
        parts = [parts[2 * e] + parts[2 * e + 1] for e in range(len(parts) // 2)]
    mine = parts[0]
    out = jnp.zeros(x.shape, x.dtype)
    out = lax.dynamic_update_slice_in_dim(out, mine, index * size, axis=dim)
    for d in range(1, count):
        recv = lax.ppermute(mine, axis, [(i, i ^ d) for i in range(count)])
        out = lax.dynamic_update_slice_in_dim(out, recv, (index ^ d) * size, axis=dim)
    return out


def row_kernel(ext_ref, mt_ref, w_ref, up_ref, out_ref, gt_ref):
    stencil_rows, channels, _ = ext_ref.shape
    n_blocks, o_block, lon_cols = up_ref.shape
    kernels = w_ref.shape[0]
    window_len = mt_ref.shape[1] // stencil_rows
    contract_last = (((1,), (1,)), ((), ()))
    gt_ref[...] = jnp.zeros(gt_ref.shape, gt_ref.dtype)
    for d in range(n_blocks):
        acc = None
        for r in range(stencil_rows):
            win = ext_ref[r, :, pl.ds(d * lon_cols, window_len)]
            part = lax.dot_general(
                win,
                mt_ref[:, pl.ds(r * window_len, window_len)],
                contract_last,
                preferred_element_type=jnp.float32,
            )
            acc = part if acc is None else acc + part
        resp = acc.astype(jnp.bfloat16)
        up_d = up_ref[d]
        for k in range(kernels):
            resp_k = resp[:, k * lon_cols : (k + 1) * lon_cols]
            gt_ref[k] += lax.dot_general(
                up_d, resp_k, contract_last, preferred_element_type=jnp.float32
            )
        if d == 0:
            total = None
            for k in range(kernels):
                term = jnp.dot(
                    w_ref[k],
                    resp[:, k * lon_cols : (k + 1) * lon_cols],
                    preferred_element_type=jnp.float32,
                )
                total = term if total is None else total + term
            out_ref[...] = total.astype(out_ref.dtype)


def row_products(ext, matrix, weights, up_rel):
    stencil_rows, channels, _ = ext.shape
    n_blocks, o_block, lon_cols = up_rel.shape
    kernels = weights.shape[0]
    flops = 2 * n_blocks * channels * matrix.shape[0] * matrix.shape[1]
    flops += 2 * n_blocks * kernels * o_block * lon_cols * channels
    flops += 2 * kernels * weights.shape[1] * channels * lon_cols
    nbytes = 2 * (ext.size + matrix.size + weights.size + up_rel.size)
    nbytes += 2 * weights.shape[1] * lon_cols + 4 * kernels * o_block * channels
    return pl.pallas_call(
        row_kernel,
        out_shape=(
            jax.ShapeDtypeStruct((weights.shape[1], lon_cols), jnp.bfloat16),
            jax.ShapeDtypeStruct((kernels, o_block, channels), jnp.float32),
        ),
        cost_estimate=pl.CostEstimate(flops=flops, transcendentals=0, bytes_accessed=nbytes),
    )(ext, matrix, weights, up_rel)


def body(fields, upstream, weights, filter_taps, cycle_counts, cycle_blocks):
    channels, lat_rows, lon_cols = fields.shape
    kernels = weights.shape[0]
    window_len = lon_cols + 2 * HALO
    n_lon = lax.axis_size("lon")
    lon_at = lax.axis_index("lon")
    tap_table = build_taps(filter_taps, cycle_counts, cycle_blocks).astype(jnp.bfloat16)
    response_grad = jnp.einsum(
        "koc,oij->cikj", weights, upstream, preferred_element_type=jnp.float32
    ).astype(jnp.bfloat16)
    grad_piece = response_grad[:, 0].reshape(channels, kernels * lon_cols)
    matrix, contrib = toeplitz(tap_table[0], lon_cols, grad_piece)
    o_block = upstream.shape[0] // n_lon
    up_row = upstream[:, 0]
    blocks = [fields[:, 0]]
    up_parts = [lax.dynamic_slice_in_dim(up_row, lon_at * o_block, o_block, axis=0)]
    for d in range(1, n_lon):
        part = lax.dynamic_slice_in_dim(up_row, ((lon_at - d) % n_lon) * o_block, o_block, axis=0)
        both = lax.ppermute(
            jnp.concatenate([fields[:, 0], part], axis=0),
            "lon",
            [(p, (p - d) % n_lon) for p in range(n_lon)],
        )
        blocks.append(both[:channels])
        up_parts.append(both[channels:])
    up_rel = jnp.stack(up_parts, axis=0)
    row = jnp.concatenate(blocks, axis=1)
    count = lax.axis_size("lat")
    below = lax.ppermute(row, "lat", [(i, i + 1) for i in range(count - 1)])
    above = lax.ppermute(row, "lat", [(i + 1, i) for i in range(count - 1)])
    rows = jnp.stack([below, row, above], axis=0)
    ext = jnp.concatenate([rows[:, :, rows.shape[2] - HALO :], rows, rows[:, :, :HALO]], axis=2)
    out_row, grad_terms = row_products(ext, matrix, weights, up_rel)
    outputs = out_row[:, None, :]
    weight_grad = lat_allreduce(grad_terms, "lat", 1)
    terms = contrib.reshape(channels, 3, window_len)
    count = lax.axis_size("lat")
    from_below = lax.ppermute(terms[:, 2], "lat", [(i, i + 1) for i in range(count - 1)])
    from_above = lax.ppermute(terms[:, 0], "lat", [(i + 1, i) for i in range(count - 1)])
    own = terms[:, 1] + from_below + from_above
    rims = jnp.stack([own[:, :HALO], own[:, HALO + lon_cols :]], axis=1)
    arrived = padded_2(rims, (("lon", 1),), 1, True)
    result = own[:, HALO : HALO + lon_cols]
    result = result.at[:, :HALO].add(arrived[:, 0])
    result = result.at[:, lon_cols - HALO :].add(arrived[:, 3])
    result = result[:, None, :]
    return (outputs, result.astype(jnp.bfloat16), weight_grad)


def solution(mesh):
    return jax.shard_map(
        body,
        mesh=mesh,
        in_specs=(
            P("groups", "lat", "lon"),
            P("groups", "lat", "lon"),
            P(),
            P("lat", None, None, None, None),
            P("lat"),
            P("lat", None),
        ),
        out_specs=(P("groups", "lat", "lon"), P("groups", "lat", "lon"), P("groups", "lon", None)),
        check_vma=False,
    )
```

```python
import jax
import jax.numpy as jnp
from jax import lax
from jax.experimental import pallas as pl
from jax.experimental.pallas import tpu as pltpu
from jax.sharding import PartitionSpec as P

HALO = 128


def padded_2(cells, sides, width, closed):
    for axis, dim in sides:
        count = lax.axis_size(axis)
        ends = count if closed else count - 1
        head = lax.slice_in_dim(cells, 0, width, axis=dim)
        tail = lax.slice_in_dim(cells, cells.shape[dim] - width, cells.shape[dim], axis=dim)
        cells = jnp.concatenate(
            [
                lax.ppermute(tail, axis, [(i, (i + 1) % count) for i in range(ends)]),
                cells,
                lax.ppermute(head, axis, [((i + 1) % count, i) for i in range(ends)]),
            ],
            axis=dim,
        )
    return cells


def build_taps(filter_taps, cycle_counts, cycle_blocks):
    slot_total = cycle_blocks.shape[1]
    width_block = filter_taps.shape[4]
    offsets = jnp.arange(width_block, dtype=jnp.int32)
    places = HALO + width_block * cycle_blocks[:, :, None] + offsets[None, None, :]
    live_slots = jnp.arange(slot_total, dtype=jnp.int32)[None, :] < cycle_counts[:, None]
    positions = jnp.arange(2 * HALO, dtype=jnp.int32)
    onehot = jnp.where(
        (places[:, :, :, None] == positions) & live_slots[:, :, None, None], 1.0, 0.0
    ).astype(jnp.float32)
    return jnp.einsum("ikrst,istu->ikru", filter_taps.astype(jnp.float32), onehot)


def toeplitz_kernel(tap_ref, grad_ref, out_ref, contrib_ref):
    kernels, lon_cols, width = out_ref.shape
    window_len = tap_ref.shape[1]
    stencil_rows = width // window_len
    acc = None
    for k in range(kernels):
        for r in range(stencil_rows):
            row = tap_ref[pl.ds(k * stencil_rows + r, 1), :]
            tiled = jnp.broadcast_to(row, (lon_cols, window_len))
            rolled = pltpu.roll(tiled, 0, 1, stride=1, stride_axis=0)
            out_ref[k, :, pl.ds(r * window_len, window_len)] = rolled.astype(out_ref.dtype)
        term = jnp.dot(
            grad_ref[:, pl.ds(k * lon_cols, lon_cols)],
            out_ref[k],
            preferred_element_type=jnp.float32,
        )
        acc = term if acc is None else acc + term
    contrib_ref[...] = acc


def toeplitz(tap_row, out_width, grad_piece):
    kernels, stencil_rows, reach = tap_row.shape
    window_len = out_width + reach
    padded = jnp.pad(tap_row.astype(jnp.float32), ((0, 0), (0, 0), (0, window_len - reach)))
    padded = padded.reshape(kernels * stencil_rows, window_len)
    out, contrib = pl.pallas_call(
        toeplitz_kernel,
        out_shape=(
            jax.ShapeDtypeStruct((kernels, out_width, stencil_rows * window_len), jnp.bfloat16),
            jax.ShapeDtypeStruct((grad_piece.shape[0], stencil_rows * window_len), jnp.float32),
        ),
    )(padded, grad_piece)
    return out.reshape(kernels * out_width, stencil_rows * window_len), contrib


def lat_allreduce(x, axis, dim):
    count = lax.axis_size(axis)
    steps = count.bit_length() - 1
    if (1 << steps) != count or x.shape[dim] % count:
        return lax.psum(x, axis)
    index = lax.axis_index(axis)
    size = x.shape[dim] // count
    parts = [lax.dynamic_slice_in_dim(x, index * size, size, axis=dim)]
    for d in range(1, count):
        send = lax.dynamic_slice_in_dim(x, (index ^ d) * size, size, axis=dim)
        parts.append(lax.ppermute(send, axis, [(i, i ^ d) for i in range(count)]))
    for s in range(steps):
        parts = [parts[2 * e] + parts[2 * e + 1] for e in range(len(parts) // 2)]
    mine = parts[0]
    out = jnp.zeros(x.shape, x.dtype)
    out = lax.dynamic_update_slice_in_dim(out, mine, index * size, axis=dim)
    for d in range(1, count):
        recv = lax.ppermute(mine, axis, [(i, i ^ d) for i in range(count)])
        out = lax.dynamic_update_slice_in_dim(out, recv, (index ^ d) * size, axis=dim)
    return out


def row_kernel(ext_ref, mt_ref, w_ref, up_ref, out_ref, gt_ref):
    stencil_rows, channels, _ = ext_ref.shape
    n_blocks, o_block, lon_cols = up_ref.shape
    kernels = w_ref.shape[0]
    window_len = mt_ref.shape[1] // stencil_rows
    contract_last = (((1,), (1,)), ((), ()))
    gt_ref[...] = jnp.zeros(gt_ref.shape, gt_ref.dtype)
    for d in range(n_blocks):
        acc = None
        for r in range(stencil_rows):
            win = ext_ref[r, :, pl.ds(d * lon_cols, window_len)]
            part = lax.dot_general(
                win,
                mt_ref[:, pl.ds(r * window_len, window_len)],
                contract_last,
                preferred_element_type=jnp.float32,
            )
            acc = part if acc is None else acc + part
        resp = acc.astype(jnp.bfloat16)
        up_d = up_ref[d]
        for k in range(kernels):
            resp_k = resp[:, k * lon_cols : (k + 1) * lon_cols]
            gt_ref[k] += lax.dot_general(
                up_d, resp_k, contract_last, preferred_element_type=jnp.float32
            )
        if d == 0:
            total = None
            for k in range(kernels):
                term = jnp.dot(
                    w_ref[k],
                    resp[:, k * lon_cols : (k + 1) * lon_cols],
                    preferred_element_type=jnp.float32,
                )
                total = term if total is None else total + term
            out_ref[...] = total.astype(out_ref.dtype)


def row_products(ext, matrix, weights, up_rel):
    stencil_rows, channels, _ = ext.shape
    n_blocks, o_block, lon_cols = up_rel.shape
    kernels = weights.shape[0]
    flops = 2 * n_blocks * channels * matrix.shape[0] * matrix.shape[1]
    flops += 2 * n_blocks * kernels * o_block * lon_cols * channels
    flops += 2 * kernels * weights.shape[1] * channels * lon_cols
    nbytes = 2 * (ext.size + matrix.size + weights.size + up_rel.size)
    nbytes += 2 * weights.shape[1] * lon_cols + 4 * kernels * o_block * channels
    return pl.pallas_call(
        row_kernel,
        out_shape=(
            jax.ShapeDtypeStruct((weights.shape[1], lon_cols), jnp.bfloat16),
            jax.ShapeDtypeStruct((kernels, o_block, channels), jnp.float32),
        ),
        cost_estimate=pl.CostEstimate(flops=flops, transcendentals=0, bytes_accessed=nbytes),
    )(ext, matrix, weights, up_rel)


def body(fields, upstream, weights, filter_taps, cycle_counts, cycle_blocks):
    channels, lat_rows, lon_cols = fields.shape
    kernels = weights.shape[0]
    window_len = lon_cols + 2 * HALO
    n_lon = lax.axis_size("lon")
    lon_at = lax.axis_index("lon")
    tap_table = build_taps(filter_taps, cycle_counts, cycle_blocks).astype(jnp.bfloat16)
    response_grad = jnp.einsum(
        "koc,oij->cikj", weights, upstream, preferred_element_type=jnp.float32
    ).astype(jnp.bfloat16)
    grad_piece = response_grad[:, 0].reshape(channels, kernels * lon_cols)
    matrix, contrib = toeplitz(tap_table[0], lon_cols, grad_piece)
    o_block = upstream.shape[0] // n_lon
    up_row = upstream[:, 0]
    terms = contrib.reshape(channels, 3, window_len)
    left_rim = terms[:, :, :HALO].reshape(3 * channels, HALO)
    right_rim = terms[:, :, HALO + lon_cols :].reshape(3 * channels, HALO)
    interior = terms[:, :, HALO : HALO + lon_cols]
    blocks = [fields[:, 0]]
    up_parts = [lax.dynamic_slice_in_dim(up_row, lon_at * o_block, o_block, axis=0)]
    for d in range(1, n_lon):
        part = lax.dynamic_slice_in_dim(up_row, ((lon_at - d) % n_lon) * o_block, o_block, axis=0)
        pieces = [fields[:, 0].astype(jnp.float32), part.astype(jnp.float32)]
        if d == 1:
            pieces.append(left_rim)
        if d == n_lon - 1:
            pieces.append(right_rim)
        got = lax.ppermute(
            jnp.concatenate(pieces, axis=0), "lon", [(p, (p - d) % n_lon) for p in range(n_lon)]
        )
        blocks.append(got[:channels].astype(jnp.bfloat16))
        up_parts.append(got[channels : channels + o_block].astype(jnp.bfloat16))
        at = channels + o_block
        if d == 1:
            rim = got[at : at + 3 * channels].reshape(channels, 3, HALO)
            interior = interior.at[:, :, lon_cols - HALO :].add(rim)
            at += 3 * channels
        if d == n_lon - 1:
            rim = got[at : at + 3 * channels].reshape(channels, 3, HALO)
            interior = interior.at[:, :, :HALO].add(rim)
    up_rel = jnp.stack(up_parts, axis=0)
    row = jnp.concatenate(blocks, axis=1)
    width = row.shape[1]
    count = lax.axis_size("lat")
    below = lax.ppermute(
        jnp.concatenate([row.astype(jnp.float32), interior[:, 2]], axis=1),
        "lat",
        [(i, i + 1) for i in range(count - 1)],
    )
    above = lax.ppermute(
        jnp.concatenate([row.astype(jnp.float32), interior[:, 0]], axis=1),
        "lat",
        [(i + 1, i) for i in range(count - 1)],
    )
    result = interior[:, 1] + below[:, width:] + above[:, width:]
    result = result[:, None, :]
    rows = jnp.stack(
        [below[:, :width].astype(jnp.bfloat16), row, above[:, :width].astype(jnp.bfloat16)], axis=0
    )
    ext = jnp.concatenate([rows[:, :, width - HALO :], rows, rows[:, :, :HALO]], axis=2)
    out_row, grad_terms = row_products(ext, matrix, weights, up_rel)
    outputs = out_row[:, None, :]
    weight_grad = lat_allreduce(grad_terms, "lat", 1)
    return (outputs, result.astype(jnp.bfloat16), weight_grad)


def solution(mesh):
    return jax.shard_map(
        body,
        mesh=mesh,
        in_specs=(
            P("groups", "lat", "lon"),
            P("groups", "lat", "lon"),
            P(),
            P("lat", None, None, None, None),
            P("lat"),
            P("lat", None),
        ),
        out_specs=(P("groups", "lat", "lon"), P("groups", "lat", "lon"), P("groups", "lon", None)),
        check_vma=False,
    )
```

```python
import jax
import jax.numpy as jnp
from jax import lax
from jax.experimental import pallas as pl
from jax.experimental.pallas import tpu as pltpu
from jax.sharding import PartitionSpec as P

HALO = 128


def padded_2(cells, sides, width, closed):
    for axis, dim in sides:
        count = lax.axis_size(axis)
        ends = count if closed else count - 1
        head = lax.slice_in_dim(cells, 0, width, axis=dim)
        tail = lax.slice_in_dim(cells, cells.shape[dim] - width, cells.shape[dim], axis=dim)
        cells = jnp.concatenate(
            [
                lax.ppermute(tail, axis, [(i, (i + 1) % count) for i in range(ends)]),
                cells,
                lax.ppermute(head, axis, [((i + 1) % count, i) for i in range(ends)]),
            ],
            axis=dim,
        )
    return cells


def build_taps(filter_taps, cycle_counts, cycle_blocks):
    slot_total = cycle_blocks.shape[1]
    width_block = filter_taps.shape[4]
    offsets = jnp.arange(width_block, dtype=jnp.int32)
    places = HALO + width_block * cycle_blocks[:, :, None] + offsets[None, None, :]
    live_slots = jnp.arange(slot_total, dtype=jnp.int32)[None, :] < cycle_counts[:, None]
    positions = jnp.arange(2 * HALO, dtype=jnp.int32)
    onehot = jnp.where(
        (places[:, :, :, None] == positions) & live_slots[:, :, None, None], 1.0, 0.0
    ).astype(jnp.float32)
    return jnp.einsum("ikrst,istu->ikru", filter_taps.astype(jnp.float32), onehot)


def toeplitz_kernel(tap_ref, grad_ref, out_ref, contrib_ref):
    kernels, lon_cols, width = out_ref.shape
    window_len = tap_ref.shape[1]
    stencil_rows = width // window_len
    acc = None
    for k in range(kernels):
        for r in range(stencil_rows):
            row = tap_ref[pl.ds(k * stencil_rows + r, 1), :]
            tiled = jnp.broadcast_to(row, (lon_cols, window_len))
            rolled = pltpu.roll(tiled, 0, 1, stride=1, stride_axis=0)
            out_ref[k, :, pl.ds(r * window_len, window_len)] = rolled.astype(out_ref.dtype)
        term = jnp.dot(
            grad_ref[:, pl.ds(k * lon_cols, lon_cols)],
            out_ref[k],
            preferred_element_type=jnp.float32,
        )
        acc = term if acc is None else acc + term
    contrib_ref[...] = acc


def toeplitz(tap_row, out_width, grad_piece):
    kernels, stencil_rows, reach = tap_row.shape
    window_len = out_width + reach
    padded = jnp.pad(tap_row.astype(jnp.float32), ((0, 0), (0, 0), (0, window_len - reach)))
    padded = padded.reshape(kernels * stencil_rows, window_len)
    out, contrib = pl.pallas_call(
        toeplitz_kernel,
        out_shape=(
            jax.ShapeDtypeStruct((kernels, out_width, stencil_rows * window_len), jnp.bfloat16),
            jax.ShapeDtypeStruct((grad_piece.shape[0], stencil_rows * window_len), jnp.float32),
        ),
    )(padded, grad_piece)
    return out.reshape(kernels * out_width, stencil_rows * window_len), contrib


def group_allreduce(x, axis, dim, stride, count):
    size = lax.axis_size(axis)
    parts = [x]
    for e in range(1, count):
        parts.append(lax.ppermute(x, axis, [(i, i ^ (stride * e)) for i in range(size)]))
    while len(parts) > 1:
        parts = [parts[2 * e] + parts[2 * e + 1] for e in range(len(parts) // 2)]
    return parts[0]


def lat_allreduce(x, axis, dim):
    count = lax.axis_size(axis)
    steps = count.bit_length() - 1
    if (1 << steps) != count or x.shape[dim] % 2 or count < 4:
        return lax.psum(x, axis)
    index = lax.axis_index(axis)
    partner = [(i, i ^ 1) for i in range(count)]
    half = x.shape[dim] // 2
    bit = index & 1
    keep = lax.dynamic_slice_in_dim(x, bit * half, half, axis=dim)
    send = lax.dynamic_slice_in_dim(x, (1 - bit) * half, half, axis=dim)
    mine = keep + lax.ppermute(send, axis, partner)
    mine = group_allreduce(mine, axis, dim, 2, count // 2)
    other = lax.ppermute(mine, axis, partner)
    out = jnp.zeros(x.shape, x.dtype)
    out = lax.dynamic_update_slice_in_dim(out, mine, bit * half, axis=dim)
    return lax.dynamic_update_slice_in_dim(out, other, (1 - bit) * half, axis=dim)


def row_kernel(ext_ref, mt_ref, w_ref, up_ref, out_ref, gt_ref):
    stencil_rows, channels, _ = ext_ref.shape
    n_blocks, o_block, lon_cols = up_ref.shape
    kernels = w_ref.shape[0]
    window_len = mt_ref.shape[1] // stencil_rows
    contract_last = (((1,), (1,)), ((), ()))
    gt_ref[...] = jnp.zeros(gt_ref.shape, gt_ref.dtype)
    for d in range(n_blocks):
        acc = None
        for r in range(stencil_rows):
            win = ext_ref[r, :, pl.ds(d * lon_cols, window_len)]
            part = lax.dot_general(
                win,
                mt_ref[:, pl.ds(r * window_len, window_len)],
                contract_last,
                preferred_element_type=jnp.float32,
            )
            acc = part if acc is None else acc + part
        resp = acc.astype(jnp.bfloat16)
        up_d = up_ref[d]
        for k in range(kernels):
            resp_k = resp[:, k * lon_cols : (k + 1) * lon_cols]
            gt_ref[k] += lax.dot_general(
                up_d, resp_k, contract_last, preferred_element_type=jnp.float32
            )
        if d == 0:
            total = None
            for k in range(kernels):
                term = jnp.dot(
                    w_ref[k],
                    resp[:, k * lon_cols : (k + 1) * lon_cols],
                    preferred_element_type=jnp.float32,
                )
                total = term if total is None else total + term
            out_ref[...] = total.astype(out_ref.dtype)


def row_products(ext, matrix, weights, up_rel):
    stencil_rows, channels, _ = ext.shape
    n_blocks, o_block, lon_cols = up_rel.shape
    kernels = weights.shape[0]
    flops = 2 * n_blocks * channels * matrix.shape[0] * matrix.shape[1]
    flops += 2 * n_blocks * kernels * o_block * lon_cols * channels
    flops += 2 * kernels * weights.shape[1] * channels * lon_cols
    nbytes = 2 * (ext.size + matrix.size + weights.size + up_rel.size)
    nbytes += 2 * weights.shape[1] * lon_cols + 4 * kernels * o_block * channels
    return pl.pallas_call(
        row_kernel,
        out_shape=(
            jax.ShapeDtypeStruct((weights.shape[1], lon_cols), jnp.bfloat16),
            jax.ShapeDtypeStruct((kernels, o_block, channels), jnp.float32),
        ),
        cost_estimate=pl.CostEstimate(flops=flops, transcendentals=0, bytes_accessed=nbytes),
    )(ext, matrix, weights, up_rel)


def body(fields, upstream, weights, filter_taps, cycle_counts, cycle_blocks):
    channels, lat_rows, lon_cols = fields.shape
    kernels = weights.shape[0]
    window_len = lon_cols + 2 * HALO
    n_lon = lax.axis_size("lon")
    lon_at = lax.axis_index("lon")
    tap_table = build_taps(filter_taps, cycle_counts, cycle_blocks).astype(jnp.bfloat16)
    response_grad = jnp.einsum(
        "koc,oij->cikj", weights, upstream, preferred_element_type=jnp.float32
    ).astype(jnp.bfloat16)
    grad_piece = response_grad[:, 0].reshape(channels, kernels * lon_cols)
    matrix, contrib = toeplitz(tap_table[0], lon_cols, grad_piece)
    o_block = upstream.shape[0] // n_lon
    up_row = upstream[:, 0]
    blocks = [fields[:, 0]]
    up_parts = [lax.dynamic_slice_in_dim(up_row, lon_at * o_block, o_block, axis=0)]
    for d in range(1, n_lon):
        part = lax.dynamic_slice_in_dim(up_row, ((lon_at - d) % n_lon) * o_block, o_block, axis=0)
        both = lax.ppermute(
            jnp.concatenate([fields[:, 0], part], axis=0),
            "lon",
            [(p, (p - d) % n_lon) for p in range(n_lon)],
        )
        blocks.append(both[:channels])
        up_parts.append(both[channels:])
    up_rel = jnp.stack(up_parts, axis=0)
    row = jnp.concatenate(blocks, axis=1)
    count = lax.axis_size("lat")
    below = lax.ppermute(row, "lat", [(i, i + 1) for i in range(count - 1)])
    above = lax.ppermute(row, "lat", [(i + 1, i) for i in range(count - 1)])
    rows = jnp.stack([below, row, above], axis=0)
    ext = jnp.concatenate([rows[:, :, rows.shape[2] - HALO :], rows, rows[:, :, :HALO]], axis=2)
    out_row, grad_terms = row_products(ext, matrix, weights, up_rel)
    outputs = out_row[:, None, :]
    weight_grad = lat_allreduce(grad_terms, "lat", 1)
    accumulated = jnp.zeros((channels, lat_rows + 2, window_len), jnp.float32)
    cycle_row = 0
    accumulated = accumulated.at[:, cycle_row : cycle_row + 3].add(
        contrib.reshape(channels, 3, window_len)
    )
    rim_columns = jnp.concatenate(
        [accumulated[:, :, :HALO], accumulated[:, :, HALO + lon_cols :]], axis=2
    )
    arrived = padded_2(rim_columns, (("lon", 2),), HALO, True)
    interior = accumulated[:, :, HALO : HALO + lon_cols]
    interior = interior.at[:, :, :HALO].add(arrived[:, :, :HALO])
    interior = interior.at[:, :, lon_cols - HALO :].add(arrived[:, :, 3 * HALO :])
    edge_rows = jnp.stack([interior[:, 0], interior[:, lat_rows + 1]], axis=1)
    arrived = padded_2(edge_rows, (("lat", 1),), 1, False)
    result = interior[:, 1 : lat_rows + 1]
    result = result.at[:, 0].add(arrived[:, 0])
    result = result.at[:, lat_rows - 1].add(arrived[:, 3])
    return (outputs, result.astype(jnp.bfloat16), weight_grad)


def solution(mesh):
    return jax.shard_map(
        body,
        mesh=mesh,
        in_specs=(
            P("groups", "lat", "lon"),
            P("groups", "lat", "lon"),
            P(),
            P("lat", None, None, None, None),
            P("lat"),
            P("lat", None),
        ),
        out_specs=(P("groups", "lat", "lon"), P("groups", "lat", "lon"), P("groups", "lon", None)),
        check_vma=False,
    )
```

```python
import jax
import jax.numpy as jnp
from jax import lax
from jax.experimental import pallas as pl
from jax.experimental.pallas import tpu as pltpu
from jax.sharding import PartitionSpec as P

HALO = 128


def padded_2(cells, sides, width, closed):
    for axis, dim in sides:
        count = lax.axis_size(axis)
        ends = count if closed else count - 1
        head = lax.slice_in_dim(cells, 0, width, axis=dim)
        tail = lax.slice_in_dim(cells, cells.shape[dim] - width, cells.shape[dim], axis=dim)
        cells = jnp.concatenate(
            [
                lax.ppermute(tail, axis, [(i, (i + 1) % count) for i in range(ends)]),
                cells,
                lax.ppermute(head, axis, [((i + 1) % count, i) for i in range(ends)]),
            ],
            axis=dim,
        )
    return cells


def build_taps(filter_taps, cycle_counts, cycle_blocks):
    slot_total = cycle_blocks.shape[1]
    width_block = filter_taps.shape[4]
    offsets = jnp.arange(width_block, dtype=jnp.int32)
    places = HALO + width_block * cycle_blocks[:, :, None] + offsets[None, None, :]
    live_slots = jnp.arange(slot_total, dtype=jnp.int32)[None, :] < cycle_counts[:, None]
    positions = jnp.arange(2 * HALO, dtype=jnp.int32)
    onehot = jnp.where(
        (places[:, :, :, None] == positions) & live_slots[:, :, None, None], 1.0, 0.0
    ).astype(jnp.float32)
    return jnp.einsum("ikrst,istu->ikru", filter_taps.astype(jnp.float32), onehot)


def toeplitz_kernel(tap_ref, grad_ref, out_ref, contrib_ref):
    kernels, lon_cols, width = out_ref.shape
    window_len = tap_ref.shape[1]
    stencil_rows = width // window_len
    acc = None
    for k in range(kernels):
        for r in range(stencil_rows):
            row = tap_ref[pl.ds(k * stencil_rows + r, 1), :]
            tiled = jnp.broadcast_to(row, (lon_cols, window_len))
            rolled = pltpu.roll(tiled, 0, 1, stride=1, stride_axis=0)
            out_ref[k, :, pl.ds(r * window_len, window_len)] = rolled.astype(out_ref.dtype)
        term = jnp.dot(
            grad_ref[:, pl.ds(k * lon_cols, lon_cols)],
            out_ref[k],
            preferred_element_type=jnp.float32,
        )
        acc = term if acc is None else acc + term
    contrib_ref[...] = acc


def toeplitz(tap_row, out_width, grad_piece):
    kernels, stencil_rows, reach = tap_row.shape
    window_len = out_width + reach
    padded = jnp.pad(tap_row.astype(jnp.float32), ((0, 0), (0, 0), (0, window_len - reach)))
    padded = padded.reshape(kernels * stencil_rows, window_len)
    out, contrib = pl.pallas_call(
        toeplitz_kernel,
        out_shape=(
            jax.ShapeDtypeStruct((kernels, out_width, stencil_rows * window_len), jnp.bfloat16),
            jax.ShapeDtypeStruct((grad_piece.shape[0], stencil_rows * window_len), jnp.float32),
        ),
    )(padded, grad_piece)
    return out.reshape(kernels * out_width, stencil_rows * window_len), contrib


def lat_allreduce(x, axis, dim):
    count = lax.axis_size(axis)
    steps = count.bit_length() - 1
    if (1 << steps) != count or x.shape[dim] % count:
        return lax.psum(x, axis)
    index = lax.axis_index(axis)
    size = x.shape[dim] // count
    parts = [lax.dynamic_slice_in_dim(x, index * size, size, axis=dim)]
    for d in range(1, count):
        send = lax.dynamic_slice_in_dim(x, (index ^ d) * size, size, axis=dim)
        parts.append(lax.ppermute(send, axis, [(i, i ^ d) for i in range(count)]))
    for s in range(steps):
        parts = [parts[2 * e] + parts[2 * e + 1] for e in range(len(parts) // 2)]
    mine = parts[0]
    out = jnp.zeros(x.shape, x.dtype)
    out = lax.dynamic_update_slice_in_dim(out, mine, index * size, axis=dim)
    for d in range(1, count):
        recv = lax.ppermute(mine, axis, [(i, i ^ d) for i in range(count)])
        out = lax.dynamic_update_slice_in_dim(out, recv, (index ^ d) * size, axis=dim)
    return out


def row_kernel(ext_ref, mt_ref, w_ref, up_ref, out_ref, gt_ref, m_ref):
    stencil_rows, channels, _ = ext_ref.shape
    n_blocks, o_block, lon_cols = up_ref.shape
    kernels = w_ref.shape[0]
    window_len = mt_ref.shape[1] // stencil_rows
    contract_last = (((1,), (1,)), ((), ()))
    gt_ref[...] = jnp.zeros(gt_ref.shape, gt_ref.dtype)
    for r in range(stencil_rows):
        m_ref[r] = mt_ref[:, pl.ds(r * window_len, window_len)].T
    for d in range(n_blocks):
        acc = None
        for r in range(stencil_rows):
            win = ext_ref[r, :, pl.ds(d * lon_cols, window_len)]
            part = jnp.dot(win, m_ref[r], preferred_element_type=jnp.float32)
            acc = part if acc is None else acc + part
        resp = acc.astype(jnp.bfloat16)
        up_d = up_ref[d]
        for k in range(kernels):
            resp_k = resp[:, k * lon_cols : (k + 1) * lon_cols]
            gt_ref[k] += lax.dot_general(
                up_d, resp_k, contract_last, preferred_element_type=jnp.float32
            )
        if d == 0:
            total = None
            for k in range(kernels):
                term = jnp.dot(
                    w_ref[k],
                    resp[:, k * lon_cols : (k + 1) * lon_cols],
                    preferred_element_type=jnp.float32,
                )
                total = term if total is None else total + term
            out_ref[...] = total.astype(out_ref.dtype)


def row_products(ext, matrix, weights, up_rel):
    stencil_rows, channels, _ = ext.shape
    n_blocks, o_block, lon_cols = up_rel.shape
    kernels = weights.shape[0]
    flops = 2 * n_blocks * channels * matrix.shape[0] * matrix.shape[1]
    flops += 2 * n_blocks * kernels * o_block * lon_cols * channels
    flops += 2 * kernels * weights.shape[1] * channels * lon_cols
    nbytes = 2 * (ext.size + matrix.size + weights.size + up_rel.size)
    nbytes += 2 * weights.shape[1] * lon_cols + 4 * kernels * o_block * channels
    return pl.pallas_call(
        row_kernel,
        out_shape=(
            jax.ShapeDtypeStruct((weights.shape[1], lon_cols), jnp.bfloat16),
            jax.ShapeDtypeStruct((kernels, o_block, channels), jnp.float32),
        ),
        scratch_shapes=[pltpu.VMEM((stencil_rows, matrix.shape[1] // stencil_rows, matrix.shape[0]), matrix.dtype)],
        cost_estimate=pl.CostEstimate(flops=flops, transcendentals=0, bytes_accessed=nbytes),
    )(ext, matrix, weights, up_rel)


def body(fields, upstream, weights, filter_taps, cycle_counts, cycle_blocks):
    channels, lat_rows, lon_cols = fields.shape
    kernels = weights.shape[0]
    window_len = lon_cols + 2 * HALO
    n_lon = lax.axis_size("lon")
    lon_at = lax.axis_index("lon")
    tap_table = build_taps(filter_taps, cycle_counts, cycle_blocks).astype(jnp.bfloat16)
    response_grad = jnp.einsum(
        "koc,oij->cikj", weights, upstream, preferred_element_type=jnp.float32
    ).astype(jnp.bfloat16)
    grad_piece = response_grad[:, 0].reshape(channels, kernels * lon_cols)
    matrix, contrib = toeplitz(tap_table[0], lon_cols, grad_piece)
    o_block = upstream.shape[0] // n_lon
    up_row = upstream[:, 0]
    blocks = [fields[:, 0]]
    up_parts = [lax.dynamic_slice_in_dim(up_row, lon_at * o_block, o_block, axis=0)]
    for d in range(1, n_lon):
        part = lax.dynamic_slice_in_dim(up_row, ((lon_at - d) % n_lon) * o_block, o_block, axis=0)
        both = lax.ppermute(
            jnp.concatenate([fields[:, 0], part], axis=0),
            "lon",
            [(p, (p - d) % n_lon) for p in range(n_lon)],
        )
        blocks.append(both[:channels])
        up_parts.append(both[channels:])
    up_rel = jnp.stack(up_parts, axis=0)
    row = jnp.concatenate(blocks, axis=1)
    count = lax.axis_size("lat")
    below = lax.ppermute(row, "lat", [(i, i + 1) for i in range(count - 1)])
    above = lax.ppermute(row, "lat", [(i + 1, i) for i in range(count - 1)])
    rows = jnp.stack([below, row, above], axis=0)
    ext = jnp.concatenate([rows[:, :, rows.shape[2] - HALO :], rows, rows[:, :, :HALO]], axis=2)
    out_row, grad_terms = row_products(ext, matrix, weights, up_rel)
    outputs = out_row[:, None, :]
    weight_grad = lat_allreduce(grad_terms, "lat", 1)
    accumulated = jnp.zeros((channels, lat_rows + 2, window_len), jnp.float32)
    cycle_row = 0
    accumulated = accumulated.at[:, cycle_row : cycle_row + 3].add(
        contrib.reshape(channels, 3, window_len)
    )
    rim_columns = jnp.concatenate(
        [accumulated[:, :, :HALO], accumulated[:, :, HALO + lon_cols :]], axis=2
    )
    arrived = padded_2(rim_columns, (("lon", 2),), HALO, True)
    interior = accumulated[:, :, HALO : HALO + lon_cols]
    interior = interior.at[:, :, :HALO].add(arrived[:, :, :HALO])
    interior = interior.at[:, :, lon_cols - HALO :].add(arrived[:, :, 3 * HALO :])
    edge_rows = jnp.stack([interior[:, 0], interior[:, lat_rows + 1]], axis=1)
    arrived = padded_2(edge_rows, (("lat", 1),), 1, False)
    result = interior[:, 1 : lat_rows + 1]
    result = result.at[:, 0].add(arrived[:, 0])
    result = result.at[:, lat_rows - 1].add(arrived[:, 3])
    return (outputs, result.astype(jnp.bfloat16), weight_grad)


def solution(mesh):
    return jax.shard_map(
        body,
        mesh=mesh,
        in_specs=(
            P("groups", "lat", "lon"),
            P("groups", "lat", "lon"),
            P(),
            P("lat", None, None, None, None),
            P("lat"),
            P("lat", None),
        ),
        out_specs=(P("groups", "lat", "lon"), P("groups", "lat", "lon"), P("groups", "lon", None)),
        check_vma=False,
    )
```

```python
import jax
import jax.numpy as jnp
from jax import lax
from jax.experimental import pallas as pl
from jax.experimental.pallas import tpu as pltpu
from jax.sharding import PartitionSpec as P

HALO = 128


def padded_2(cells, sides, width, closed):
    for axis, dim in sides:
        count = lax.axis_size(axis)
        ends = count if closed else count - 1
        head = lax.slice_in_dim(cells, 0, width, axis=dim)
        tail = lax.slice_in_dim(cells, cells.shape[dim] - width, cells.shape[dim], axis=dim)
        cells = jnp.concatenate(
            [
                lax.ppermute(tail, axis, [(i, (i + 1) % count) for i in range(ends)]),
                cells,
                lax.ppermute(head, axis, [((i + 1) % count, i) for i in range(ends)]),
            ],
            axis=dim,
        )
    return cells


def build_taps(filter_taps, cycle_counts, cycle_blocks):
    slot_total = cycle_blocks.shape[1]
    width_block = filter_taps.shape[4]
    offsets = jnp.arange(width_block, dtype=jnp.int32)
    places = HALO + width_block * cycle_blocks[:, :, None] + offsets[None, None, :]
    live_slots = jnp.arange(slot_total, dtype=jnp.int32)[None, :] < cycle_counts[:, None]
    positions = jnp.arange(2 * HALO, dtype=jnp.int32)
    onehot = jnp.where(
        (places[:, :, :, None] == positions) & live_slots[:, :, None, None], 1.0, 0.0
    ).astype(jnp.float32)
    return jnp.einsum("ikrst,istu->ikru", filter_taps.astype(jnp.float32), onehot)


def toeplitz_kernel(tap_ref, grad_ref, out_ref, contrib_ref):
    kernels, lon_cols, width = out_ref.shape
    window_len = tap_ref.shape[1]
    stencil_rows = width // window_len
    acc = None
    for k in range(kernels):
        for r in range(stencil_rows):
            row = tap_ref[pl.ds(k * stencil_rows + r, 1), :]
            tiled = jnp.broadcast_to(row, (lon_cols, window_len))
            rolled = pltpu.roll(tiled, 0, 1, stride=1, stride_axis=0)
            out_ref[k, :, pl.ds(r * window_len, window_len)] = rolled.astype(out_ref.dtype)
        term = jnp.dot(
            grad_ref[:, pl.ds(k * lon_cols, lon_cols)],
            out_ref[k],
            preferred_element_type=jnp.float32,
        )
        acc = term if acc is None else acc + term
    contrib_ref[...] = acc


def toeplitz(tap_row, out_width, grad_piece):
    kernels, stencil_rows, reach = tap_row.shape
    window_len = out_width + reach
    padded = jnp.pad(tap_row.astype(jnp.float32), ((0, 0), (0, 0), (0, window_len - reach)))
    padded = padded.reshape(kernels * stencil_rows, window_len)
    out, contrib = pl.pallas_call(
        toeplitz_kernel,
        out_shape=(
            jax.ShapeDtypeStruct((kernels, out_width, stencil_rows * window_len), jnp.bfloat16),
            jax.ShapeDtypeStruct((grad_piece.shape[0], stencil_rows * window_len), jnp.float32),
        ),
    )(padded, grad_piece)
    return out.reshape(kernels * out_width, stencil_rows * window_len), contrib


def lat_allreduce(x, axis, dim):
    count = lax.axis_size(axis)
    steps = count.bit_length() - 1
    if (1 << steps) != count or x.shape[dim] % count:
        return lax.psum(x, axis)
    index = lax.axis_index(axis)
    size = x.shape[dim] // count
    parts = [lax.dynamic_slice_in_dim(x, index * size, size, axis=dim)]
    for d in range(1, count):
        send = lax.dynamic_slice_in_dim(x, (index ^ d) * size, size, axis=dim)
        parts.append(lax.ppermute(send, axis, [(i, i ^ d) for i in range(count)]))
    for s in range(steps):
        parts = [parts[2 * e] + parts[2 * e + 1] for e in range(len(parts) // 2)]
    mine = parts[0]
    out = jnp.zeros(x.shape, x.dtype)
    out = lax.dynamic_update_slice_in_dim(out, mine, index * size, axis=dim)
    for d in range(1, count):
        recv = lax.ppermute(mine, axis, [(i, i ^ d) for i in range(count)])
        out = lax.dynamic_update_slice_in_dim(out, recv, (index ^ d) * size, axis=dim)
    return out


def row_kernel(ext_ref, mt_ref, w_ref, upt_ref, out_ref, gt_ref, m_ref, rs_ref):
    stencil_rows, channels, _ = ext_ref.shape
    n_blocks, lon_cols, o_block = upt_ref.shape
    kernels = w_ref.shape[0]
    window_len = mt_ref.shape[1] // stencil_rows
    acc = None
    for r in range(stencil_rows):
        m_ref[...] = mt_ref[:, pl.ds(r * window_len, window_len)].T
        wins = jnp.concatenate(
            [ext_ref[r, :, pl.ds(d * lon_cols, window_len)] for d in range(n_blocks)], axis=0
        )
        part = jnp.dot(wins, m_ref[...], preferred_element_type=jnp.float32)
        acc = part if acc is None else acc + part
    rs_ref[...] = acc.astype(jnp.bfloat16)
    up_t = upt_ref[...].reshape(n_blocks * lon_cols, o_block)
    for k in range(kernels):
        lhs = jnp.concatenate(
            [
                rs_ref[pl.ds(d * channels, channels), pl.ds(k * lon_cols, lon_cols)]
                for d in range(n_blocks)
            ],
            axis=1,
        )
        grad_t = jnp.dot(lhs, up_t, preferred_element_type=jnp.float32)
        gt_ref[k] = grad_t.T
    total = None
    for k in range(kernels):
        term = jnp.dot(
            w_ref[k],
            rs_ref[pl.ds(0, channels), pl.ds(k * lon_cols, lon_cols)],
            preferred_element_type=jnp.float32,
        )
        total = term if total is None else total + term
    out_ref[...] = total.astype(out_ref.dtype)


def row_products(ext, matrix, weights, up_rel):
    stencil_rows, channels, _ = ext.shape
    n_blocks, o_block, lon_cols = up_rel.shape
    kernels = weights.shape[0]
    up_t = jnp.swapaxes(up_rel, 1, 2)
    window_len = matrix.shape[1] // stencil_rows
    flops = 2 * n_blocks * channels * matrix.shape[0] * matrix.shape[1]
    flops += 2 * n_blocks * kernels * o_block * lon_cols * channels
    flops += 2 * kernels * weights.shape[1] * channels * lon_cols
    nbytes = 2 * (ext.size + matrix.size + weights.size + up_rel.size)
    nbytes += 2 * weights.shape[1] * lon_cols + 4 * kernels * o_block * channels
    return pl.pallas_call(
        row_kernel,
        out_shape=(
            jax.ShapeDtypeStruct((weights.shape[1], lon_cols), jnp.bfloat16),
            jax.ShapeDtypeStruct((kernels, o_block, channels), jnp.float32),
        ),
        scratch_shapes=[
            pltpu.VMEM((window_len, matrix.shape[0]), matrix.dtype),
            pltpu.VMEM((n_blocks * channels, matrix.shape[0]), jnp.bfloat16),
        ],
        cost_estimate=pl.CostEstimate(flops=flops, transcendentals=0, bytes_accessed=nbytes),
    )(ext, matrix, weights, up_t)


def body(fields, upstream, weights, filter_taps, cycle_counts, cycle_blocks):
    channels, lat_rows, lon_cols = fields.shape
    kernels = weights.shape[0]
    window_len = lon_cols + 2 * HALO
    n_lon = lax.axis_size("lon")
    lon_at = lax.axis_index("lon")
    tap_table = build_taps(filter_taps, cycle_counts, cycle_blocks).astype(jnp.bfloat16)
    response_grad = jnp.einsum(
        "koc,oij->cikj", weights, upstream, preferred_element_type=jnp.float32
    ).astype(jnp.bfloat16)
    grad_piece = response_grad[:, 0].reshape(channels, kernels * lon_cols)
    matrix, contrib = toeplitz(tap_table[0], lon_cols, grad_piece)
    o_block = upstream.shape[0] // n_lon
    up_row = upstream[:, 0]
    blocks = [fields[:, 0]]
    up_parts = [lax.dynamic_slice_in_dim(up_row, lon_at * o_block, o_block, axis=0)]
    for d in range(1, n_lon):
        part = lax.dynamic_slice_in_dim(up_row, ((lon_at - d) % n_lon) * o_block, o_block, axis=0)
        both = lax.ppermute(
            jnp.concatenate([fields[:, 0], part], axis=0),
            "lon",
            [(p, (p - d) % n_lon) for p in range(n_lon)],
        )
        blocks.append(both[:channels])
        up_parts.append(both[channels:])
    up_rel = jnp.stack(up_parts, axis=0)
    row = jnp.concatenate(blocks, axis=1)
    count = lax.axis_size("lat")
    below = lax.ppermute(row, "lat", [(i, i + 1) for i in range(count - 1)])
    above = lax.ppermute(row, "lat", [(i + 1, i) for i in range(count - 1)])
    rows = jnp.stack([below, row, above], axis=0)
    ext = jnp.concatenate([rows[:, :, rows.shape[2] - HALO :], rows, rows[:, :, :HALO]], axis=2)
    out_row, grad_terms = row_products(ext, matrix, weights, up_rel)
    outputs = out_row[:, None, :]
    weight_grad = lat_allreduce(grad_terms, "lat", 1)
    accumulated = jnp.zeros((channels, lat_rows + 2, window_len), jnp.float32)
    cycle_row = 0
    accumulated = accumulated.at[:, cycle_row : cycle_row + 3].add(
        contrib.reshape(channels, 3, window_len)
    )
    rim_columns = jnp.concatenate(
        [accumulated[:, :, :HALO], accumulated[:, :, HALO + lon_cols :]], axis=2
    )
    arrived = padded_2(rim_columns, (("lon", 2),), HALO, True)
    interior = accumulated[:, :, HALO : HALO + lon_cols]
    interior = interior.at[:, :, :HALO].add(arrived[:, :, :HALO])
    interior = interior.at[:, :, lon_cols - HALO :].add(arrived[:, :, 3 * HALO :])
    edge_rows = jnp.stack([interior[:, 0], interior[:, lat_rows + 1]], axis=1)
    arrived = padded_2(edge_rows, (("lat", 1),), 1, False)
    result = interior[:, 1 : lat_rows + 1]
    result = result.at[:, 0].add(arrived[:, 0])
    result = result.at[:, lat_rows - 1].add(arrived[:, 3])
    return (outputs, result.astype(jnp.bfloat16), weight_grad)


def solution(mesh):
    return jax.shard_map(
        body,
        mesh=mesh,
        in_specs=(
            P("groups", "lat", "lon"),
            P("groups", "lat", "lon"),
            P(),
            P("lat", None, None, None, None),
            P("lat"),
            P("lat", None),
        ),
        out_specs=(P("groups", "lat", "lon"), P("groups", "lat", "lon"), P("groups", "lon", None)),
        check_vma=False,
    )
```

```python
import jax
import jax.numpy as jnp
from jax import lax
from jax.experimental import pallas as pl
from jax.experimental.pallas import tpu as pltpu
from jax.sharding import PartitionSpec as P

HALO = 128


def padded_2(cells, sides, width, closed):
    for axis, dim in sides:
        count = lax.axis_size(axis)
        ends = count if closed else count - 1
        head = lax.slice_in_dim(cells, 0, width, axis=dim)
        tail = lax.slice_in_dim(cells, cells.shape[dim] - width, cells.shape[dim], axis=dim)
        cells = jnp.concatenate(
            [
                lax.ppermute(tail, axis, [(i, (i + 1) % count) for i in range(ends)]),
                cells,
                lax.ppermute(head, axis, [((i + 1) % count, i) for i in range(ends)]),
            ],
            axis=dim,
        )
    return cells


def build_taps(filter_taps, cycle_counts, cycle_blocks):
    slot_total = cycle_blocks.shape[1]
    width_block = filter_taps.shape[4]
    offsets = jnp.arange(width_block, dtype=jnp.int32)
    places = HALO + width_block * cycle_blocks[:, :, None] + offsets[None, None, :]
    live_slots = jnp.arange(slot_total, dtype=jnp.int32)[None, :] < cycle_counts[:, None]
    positions = jnp.arange(2 * HALO, dtype=jnp.int32)
    onehot = jnp.where(
        (places[:, :, :, None] == positions) & live_slots[:, :, None, None], 1.0, 0.0
    ).astype(jnp.float32)
    return jnp.einsum("ikrst,istu->ikru", filter_taps.astype(jnp.float32), onehot)


def toeplitz_kernel(tap_ref, grad_ref, out_ref, contrib_ref):
    kernels, lon_cols, width = out_ref.shape
    window_len = tap_ref.shape[1]
    stencil_rows = width // window_len
    acc = None
    for k in range(kernels):
        for r in range(stencil_rows):
            row = tap_ref[pl.ds(k * stencil_rows + r, 1), :]
            tiled = jnp.broadcast_to(row, (lon_cols, window_len))
            rolled = pltpu.roll(tiled, 0, 1, stride=1, stride_axis=0)
            out_ref[k, :, pl.ds(r * window_len, window_len)] = rolled.astype(out_ref.dtype)
        term = jnp.dot(
            grad_ref[:, pl.ds(k * lon_cols, lon_cols)],
            out_ref[k],
            preferred_element_type=jnp.float32,
        )
        acc = term if acc is None else acc + term
    contrib_ref[...] = acc


def toeplitz(tap_row, out_width, grad_piece):
    kernels, stencil_rows, reach = tap_row.shape
    window_len = out_width + reach
    padded = jnp.pad(tap_row.astype(jnp.float32), ((0, 0), (0, 0), (0, window_len - reach)))
    padded = padded.reshape(kernels * stencil_rows, window_len)
    out, contrib = pl.pallas_call(
        toeplitz_kernel,
        out_shape=(
            jax.ShapeDtypeStruct((kernels, out_width, stencil_rows * window_len), jnp.bfloat16),
            jax.ShapeDtypeStruct((grad_piece.shape[0], stencil_rows * window_len), jnp.float32),
        ),
    )(padded, grad_piece)
    return out.reshape(kernels * out_width, stencil_rows * window_len), contrib


def lat_allreduce(x, axis, dim):
    count = lax.axis_size(axis)
    steps = count.bit_length() - 1
    if (1 << steps) != count or x.shape[dim] % count:
        return lax.psum(x, axis)
    index = lax.axis_index(axis)
    size = x.shape[dim] // count
    parts = [lax.dynamic_slice_in_dim(x, index * size, size, axis=dim)]
    for d in range(1, count):
        send = lax.dynamic_slice_in_dim(x, (index ^ d) * size, size, axis=dim)
        parts.append(lax.ppermute(send, axis, [(i, i ^ d) for i in range(count)]))
    for s in range(steps):
        parts = [parts[2 * e] + parts[2 * e + 1] for e in range(len(parts) // 2)]
    mine = parts[0]
    out = jnp.zeros(x.shape, x.dtype)
    out = lax.dynamic_update_slice_in_dim(out, mine, index * size, axis=dim)
    for d in range(1, count):
        recv = lax.ppermute(mine, axis, [(i, i ^ d) for i in range(count)])
        out = lax.dynamic_update_slice_in_dim(out, recv, (index ^ d) * size, axis=dim)
    return out


def row_kernel(ext_ref, mt_ref, w_ref, up_ref, out_ref, gt_ref, acc_ref):
    _, channels, _ = ext_ref.shape
    n_blocks, o_block, lon_cols = up_ref.shape
    kernels = w_ref.shape[0]
    window_len = mt_ref.shape[1]
    contract_last = (((1,), (1,)), ((), ()))
    r = pl.program_id(0)

    @pl.when(r == 0)
    def _():
        acc_ref[...] = jnp.zeros(acc_ref.shape, acc_ref.dtype)

    for d in range(n_blocks):
        win = ext_ref[0, :, pl.ds(d * lon_cols, window_len)]
        acc_ref[d] += lax.dot_general(
            win, mt_ref[...], contract_last, preferred_element_type=jnp.float32
        )

    @pl.when(r == pl.num_programs(0) - 1)
    def _():
        grads = [None] * kernels
        for d in range(n_blocks):
            resp = acc_ref[d].astype(jnp.bfloat16)
            up_d = up_ref[d]
            for k in range(kernels):
                term = lax.dot_general(
                    up_d,
                    resp[:, k * lon_cols : (k + 1) * lon_cols],
                    contract_last,
                    preferred_element_type=jnp.float32,
                )
                grads[k] = term if grads[k] is None else grads[k] + term
            if d == 0:
                total = None
                for k in range(kernels):
                    term = jnp.dot(
                        w_ref[k],
                        resp[:, k * lon_cols : (k + 1) * lon_cols],
                        preferred_element_type=jnp.float32,
                    )
                    total = term if total is None else total + term
                out_ref[...] = total.astype(out_ref.dtype)
        for k in range(kernels):
            gt_ref[k] = grads[k]


def row_products(ext, matrix, weights, up_rel):
    stencil_rows, channels, ext_width = ext.shape
    n_blocks, o_block, lon_cols = up_rel.shape
    kernels = weights.shape[0]
    window_len = matrix.shape[1] // stencil_rows
    flops = 2 * n_blocks * channels * matrix.shape[0] * matrix.shape[1]
    flops += 2 * n_blocks * kernels * o_block * lon_cols * channels
    flops += 2 * kernels * weights.shape[1] * channels * lon_cols
    nbytes = 2 * (ext.size + matrix.size + weights.size + up_rel.size)
    nbytes += 2 * weights.shape[1] * lon_cols + 4 * kernels * o_block * channels
    return pl.pallas_call(
        row_kernel,
        grid=(stencil_rows,),
        in_specs=[
            pl.BlockSpec((1, channels, ext_width), lambda r: (r, 0, 0)),
            pl.BlockSpec((matrix.shape[0], window_len), lambda r: (0, r)),
            pl.BlockSpec(weights.shape, lambda r: (0, 0, 0)),
            pl.BlockSpec(up_rel.shape, lambda r: (0, 0, 0)),
        ],
        out_specs=[
            pl.BlockSpec((weights.shape[1], lon_cols), lambda r: (0, 0)),
            pl.BlockSpec((kernels, o_block, channels), lambda r: (0, 0, 0)),
        ],
        out_shape=(
            jax.ShapeDtypeStruct((weights.shape[1], lon_cols), jnp.bfloat16),
            jax.ShapeDtypeStruct((kernels, o_block, channels), jnp.float32),
        ),
        scratch_shapes=[pltpu.VMEM((n_blocks, channels, matrix.shape[0]), jnp.float32)],
        compiler_params=pltpu.CompilerParams(dimension_semantics=("arbitrary",)),
        cost_estimate=pl.CostEstimate(flops=flops, transcendentals=0, bytes_accessed=nbytes),
    )(ext, matrix, weights, up_rel)


def body(fields, upstream, weights, filter_taps, cycle_counts, cycle_blocks):
    channels, lat_rows, lon_cols = fields.shape
    kernels = weights.shape[0]
    window_len = lon_cols + 2 * HALO
    n_lon = lax.axis_size("lon")
    lon_at = lax.axis_index("lon")
    tap_table = build_taps(filter_taps, cycle_counts, cycle_blocks).astype(jnp.bfloat16)
    response_grad = jnp.einsum(
        "koc,oij->cikj", weights, upstream, preferred_element_type=jnp.float32
    ).astype(jnp.bfloat16)
    grad_piece = response_grad[:, 0].reshape(channels, kernels * lon_cols)
    matrix, contrib = toeplitz(tap_table[0], lon_cols, grad_piece)
    o_block = upstream.shape[0] // n_lon
    up_row = upstream[:, 0]
    blocks = [fields[:, 0]]
    up_parts = [lax.dynamic_slice_in_dim(up_row, lon_at * o_block, o_block, axis=0)]
    for d in range(1, n_lon):
        part = lax.dynamic_slice_in_dim(up_row, ((lon_at - d) % n_lon) * o_block, o_block, axis=0)
        both = lax.ppermute(
            jnp.concatenate([fields[:, 0], part], axis=0),
            "lon",
            [(p, (p - d) % n_lon) for p in range(n_lon)],
        )
        blocks.append(both[:channels])
        up_parts.append(both[channels:])
    up_rel = jnp.stack(up_parts, axis=0)
    row = jnp.concatenate(blocks, axis=1)
    count = lax.axis_size("lat")
    below = lax.ppermute(row, "lat", [(i, i + 1) for i in range(count - 1)])
    above = lax.ppermute(row, "lat", [(i + 1, i) for i in range(count - 1)])
    rows = jnp.stack([below, row, above], axis=0)
    ext = jnp.concatenate([rows[:, :, rows.shape[2] - HALO :], rows, rows[:, :, :HALO]], axis=2)
    out_row, grad_terms = row_products(ext, matrix, weights, up_rel)
    outputs = out_row[:, None, :]
    weight_grad = lat_allreduce(grad_terms, "lat", 1)
    accumulated = jnp.zeros((channels, lat_rows + 2, window_len), jnp.float32)
    cycle_row = 0
    accumulated = accumulated.at[:, cycle_row : cycle_row + 3].add(
        contrib.reshape(channels, 3, window_len)
    )
    rim_columns = jnp.concatenate(
        [accumulated[:, :, :HALO], accumulated[:, :, HALO + lon_cols :]], axis=2
    )
    arrived = padded_2(rim_columns, (("lon", 2),), HALO, True)
    interior = accumulated[:, :, HALO : HALO + lon_cols]
    interior = interior.at[:, :, :HALO].add(arrived[:, :, :HALO])
    interior = interior.at[:, :, lon_cols - HALO :].add(arrived[:, :, 3 * HALO :])
    edge_rows = jnp.stack([interior[:, 0], interior[:, lat_rows + 1]], axis=1)
    arrived = padded_2(edge_rows, (("lat", 1),), 1, False)
    result = interior[:, 1 : lat_rows + 1]
    result = result.at[:, 0].add(arrived[:, 0])
    result = result.at[:, lat_rows - 1].add(arrived[:, 3])
    return (outputs, result.astype(jnp.bfloat16), weight_grad)


def solution(mesh):
    return jax.shard_map(
        body,
        mesh=mesh,
        in_specs=(
            P("groups", "lat", "lon"),
            P("groups", "lat", "lon"),
            P(),
            P("lat", None, None, None, None),
            P("lat"),
            P("lat", None),
        ),
        out_specs=(P("groups", "lat", "lon"), P("groups", "lat", "lon"), P("groups", "lon", None)),
        check_vma=False,
    )
```

```python
import jax
import jax.numpy as jnp
from jax import lax
from jax.experimental import pallas as pl
from jax.experimental.pallas import tpu as pltpu
from jax.sharding import PartitionSpec as P

HALO = 128


def padded_2(cells, sides, width, closed):
    for axis, dim in sides:
        count = lax.axis_size(axis)
        ends = count if closed else count - 1
        head = lax.slice_in_dim(cells, 0, width, axis=dim)
        tail = lax.slice_in_dim(cells, cells.shape[dim] - width, cells.shape[dim], axis=dim)
        cells = jnp.concatenate(
            [
                lax.ppermute(tail, axis, [(i, (i + 1) % count) for i in range(ends)]),
                cells,
                lax.ppermute(head, axis, [((i + 1) % count, i) for i in range(ends)]),
            ],
            axis=dim,
        )
    return cells


def build_taps(filter_taps, cycle_counts, cycle_blocks):
    slot_total = cycle_blocks.shape[1]
    width_block = filter_taps.shape[4]
    offsets = jnp.arange(width_block, dtype=jnp.int32)
    places = HALO + width_block * cycle_blocks[:, :, None] + offsets[None, None, :]
    live_slots = jnp.arange(slot_total, dtype=jnp.int32)[None, :] < cycle_counts[:, None]
    positions = jnp.arange(2 * HALO, dtype=jnp.int32)
    onehot = jnp.where(
        (places[:, :, :, None] == positions) & live_slots[:, :, None, None], 1.0, 0.0
    ).astype(jnp.float32)
    return jnp.einsum("ikrst,istu->ikru", filter_taps.astype(jnp.float32), onehot)


def toeplitz_kernel(tap_ref, grad_ref, out_ref, contrib_ref):
    kernels, lon_cols, width = out_ref.shape
    window_len = tap_ref.shape[1]
    stencil_rows = width // window_len
    acc = None
    for k in range(kernels):
        for r in range(stencil_rows):
            row = tap_ref[pl.ds(k * stencil_rows + r, 1), :]
            tiled = jnp.broadcast_to(row, (lon_cols, window_len))
            rolled = pltpu.roll(tiled, 0, 1, stride=1, stride_axis=0)
            out_ref[k, :, pl.ds(r * window_len, window_len)] = rolled.astype(out_ref.dtype)
        term = jnp.dot(
            grad_ref[:, pl.ds(k * lon_cols, lon_cols)],
            out_ref[k],
            preferred_element_type=jnp.float32,
        )
        acc = term if acc is None else acc + term
    contrib_ref[...] = acc


def toeplitz(tap_row, out_width, grad_piece):
    kernels, stencil_rows, reach = tap_row.shape
    window_len = out_width + reach
    padded = jnp.pad(tap_row.astype(jnp.float32), ((0, 0), (0, 0), (0, window_len - reach)))
    padded = padded.reshape(kernels * stencil_rows, window_len)
    out, contrib = pl.pallas_call(
        toeplitz_kernel,
        out_shape=(
            jax.ShapeDtypeStruct((kernels, out_width, stencil_rows * window_len), jnp.bfloat16),
            jax.ShapeDtypeStruct((grad_piece.shape[0], stencil_rows * window_len), jnp.float32),
        ),
    )(padded, grad_piece)
    return out.reshape(kernels * out_width, stencil_rows * window_len), contrib


def lat_allreduce(x, axis, dim):
    count = lax.axis_size(axis)
    steps = count.bit_length() - 1
    if (1 << steps) != count or x.shape[dim] % count:
        return lax.psum(x, axis)
    index = lax.axis_index(axis)
    size = x.shape[dim] // count
    parts = [lax.dynamic_slice_in_dim(x, index * size, size, axis=dim)]
    for d in range(1, count):
        send = lax.dynamic_slice_in_dim(x, (index ^ d) * size, size, axis=dim)
        parts.append(lax.ppermute(send, axis, [(i, i ^ d) for i in range(count)]))
    for s in range(steps):
        parts = [parts[2 * e] + parts[2 * e + 1] for e in range(len(parts) // 2)]
    mine = parts[0]
    out = jnp.zeros(x.shape, x.dtype)
    out = lax.dynamic_update_slice_in_dim(out, mine, index * size, axis=dim)
    for d in range(1, count):
        recv = lax.ppermute(mine, axis, [(i, i ^ d) for i in range(count)])
        out = lax.dynamic_update_slice_in_dim(out, recv, (index ^ d) * size, axis=dim)
    return out


def lat_allreduce_with_rims(x, axis, dim, interior):
    count = lax.axis_size(axis)
    index = lax.axis_index(axis)
    size = x.shape[dim] // count
    odd = (index & 1) == 1
    lanes = interior.shape[2]
    chunk_shape = lax.dynamic_slice_in_dim(x, 0, size, axis=dim).shape
    parts = [lax.dynamic_slice_in_dim(x, index * size, size, axis=dim)]
    rims = {}
    for d in range(1, count):
        send = lax.dynamic_slice_in_dim(x, (index ^ d) * size, size, axis=dim).reshape(-1, lanes)
        rows = send.shape[0]
        if d in (1, 3):
            to_upper = jnp.logical_not(odd) if d == 1 else odd
            edge = jnp.where(to_upper, interior[:, 2], interior[:, 0])
            send = jnp.concatenate([send, edge], axis=0)
        got = lax.ppermute(send, axis, [(i, i ^ d) for i in range(count)])
        parts.append(got[:rows].reshape(chunk_shape))
        if d in (1, 3):
            rims[d] = got[rows:]
    while len(parts) > 1:
        parts = [parts[2 * e] + parts[2 * e + 1] for e in range(len(parts) // 2)]
    mine = parts[0]
    out = jnp.zeros(x.shape, x.dtype)
    out = lax.dynamic_update_slice_in_dim(out, mine, index * size, axis=dim)
    for d in range(1, count):
        recv = lax.ppermute(mine, axis, [(i, i ^ d) for i in range(count)])
        out = lax.dynamic_update_slice_in_dim(out, recv, (index ^ d) * size, axis=dim)
    middle = (index == 1) | (index == 2)
    result = interior[:, 1] + rims[1] + jnp.where(middle, rims[3], jnp.zeros_like(rims[3]))
    return out, result


def row_kernel(ext_ref, mt_ref, w_ref, up_ref, out_ref, gt_ref, acc_ref):
    _, channels, _ = ext_ref.shape
    n_blocks, o_block, lon_cols = up_ref.shape
    kernels = w_ref.shape[0]
    window_len = mt_ref.shape[1]
    contract_last = (((1,), (1,)), ((), ()))
    r = pl.program_id(0)

    @pl.when(r == 0)
    def _():
        acc_ref[...] = jnp.zeros(acc_ref.shape, acc_ref.dtype)

    for d in range(n_blocks):
        win = ext_ref[0, :, pl.ds(d * lon_cols, window_len)]
        acc_ref[d] += lax.dot_general(
            win, mt_ref[...], contract_last, preferred_element_type=jnp.float32
        )

    @pl.when(r == pl.num_programs(0) - 1)
    def _():
        grads = [None] * kernels
        for d in range(n_blocks):
            resp = acc_ref[d].astype(jnp.bfloat16)
            up_d = up_ref[d]
            for k in range(kernels):
                term = lax.dot_general(
                    up_d,
                    resp[:, k * lon_cols : (k + 1) * lon_cols],
                    contract_last,
                    preferred_element_type=jnp.float32,
                )
                grads[k] = term if grads[k] is None else grads[k] + term
            if d == 0:
                total = None
                for k in range(kernels):
                    term = jnp.dot(
                        w_ref[k],
                        resp[:, k * lon_cols : (k + 1) * lon_cols],
                        preferred_element_type=jnp.float32,
                    )
                    total = term if total is None else total + term
                out_ref[...] = total.astype(out_ref.dtype)
        for k in range(kernels):
            gt_ref[k] = grads[k]


def row_products(ext, matrix, weights, up_rel):
    stencil_rows, channels, ext_width = ext.shape
    n_blocks, o_block, lon_cols = up_rel.shape
    kernels = weights.shape[0]
    window_len = matrix.shape[1] // stencil_rows
    flops = 2 * n_blocks * channels * matrix.shape[0] * matrix.shape[1]
    flops += 2 * n_blocks * kernels * o_block * lon_cols * channels
    flops += 2 * kernels * weights.shape[1] * channels * lon_cols
    nbytes = 2 * (ext.size + matrix.size + weights.size + up_rel.size)
    nbytes += 2 * weights.shape[1] * lon_cols + 4 * kernels * o_block * channels
    return pl.pallas_call(
        row_kernel,
        grid=(stencil_rows,),
        in_specs=[
            pl.BlockSpec((1, channels, ext_width), lambda r: (r, 0, 0)),
            pl.BlockSpec((matrix.shape[0], window_len), lambda r: (0, r)),
            pl.BlockSpec(weights.shape, lambda r: (0, 0, 0)),
            pl.BlockSpec(up_rel.shape, lambda r: (0, 0, 0)),
        ],
        out_specs=[
            pl.BlockSpec((weights.shape[1], lon_cols), lambda r: (0, 0)),
            pl.BlockSpec((kernels, o_block, channels), lambda r: (0, 0, 0)),
        ],
        out_shape=(
            jax.ShapeDtypeStruct((weights.shape[1], lon_cols), jnp.bfloat16),
            jax.ShapeDtypeStruct((kernels, o_block, channels), jnp.float32),
        ),
        scratch_shapes=[pltpu.VMEM((n_blocks, channels, matrix.shape[0]), jnp.float32)],
        compiler_params=pltpu.CompilerParams(dimension_semantics=("arbitrary",)),
        cost_estimate=pl.CostEstimate(flops=flops, transcendentals=0, bytes_accessed=nbytes),
    )(ext, matrix, weights, up_rel)


def body(fields, upstream, weights, filter_taps, cycle_counts, cycle_blocks):
    channels, lat_rows, lon_cols = fields.shape
    kernels = weights.shape[0]
    window_len = lon_cols + 2 * HALO
    n_lon = lax.axis_size("lon")
    lon_at = lax.axis_index("lon")
    tap_table = build_taps(filter_taps, cycle_counts, cycle_blocks).astype(jnp.bfloat16)
    response_grad = jnp.einsum(
        "koc,oij->cikj", weights, upstream, preferred_element_type=jnp.float32
    ).astype(jnp.bfloat16)
    grad_piece = response_grad[:, 0].reshape(channels, kernels * lon_cols)
    matrix, contrib = toeplitz(tap_table[0], lon_cols, grad_piece)
    o_block = upstream.shape[0] // n_lon
    up_row = upstream[:, 0]
    blocks = [fields[:, 0]]
    up_parts = [lax.dynamic_slice_in_dim(up_row, lon_at * o_block, o_block, axis=0)]
    for d in range(1, n_lon):
        part = lax.dynamic_slice_in_dim(up_row, ((lon_at - d) % n_lon) * o_block, o_block, axis=0)
        both = lax.ppermute(
            jnp.concatenate([fields[:, 0], part], axis=0),
            "lon",
            [(p, (p - d) % n_lon) for p in range(n_lon)],
        )
        blocks.append(both[:channels])
        up_parts.append(both[channels:])
    up_rel = jnp.stack(up_parts, axis=0)
    row = jnp.concatenate(blocks, axis=1)
    count = lax.axis_size("lat")
    below = lax.ppermute(row, "lat", [(i, i + 1) for i in range(count - 1)])
    above = lax.ppermute(row, "lat", [(i + 1, i) for i in range(count - 1)])
    rows = jnp.stack([below, row, above], axis=0)
    ext = jnp.concatenate([rows[:, :, rows.shape[2] - HALO :], rows, rows[:, :, :HALO]], axis=2)
    out_row, grad_terms = row_products(ext, matrix, weights, up_rel)
    outputs = out_row[:, None, :]
    terms = contrib.reshape(channels, 3, window_len)
    rim_columns = jnp.concatenate([terms[:, :, :HALO], terms[:, :, HALO + lon_cols :]], axis=2)
    arrived = padded_2(rim_columns, (("lon", 2),), HALO, True)
    interior = terms[:, :, HALO : HALO + lon_cols]
    interior = interior.at[:, :, :HALO].add(arrived[:, :, :HALO])
    interior = interior.at[:, :, lon_cols - HALO :].add(arrived[:, :, 3 * HALO :])
    chunk = grad_terms.size // 4
    if lax.axis_size("lat") == 4 and grad_terms.shape[1] % 4 == 0 and chunk % lon_cols == 0:
        weight_grad, result = lat_allreduce_with_rims(grad_terms, "lat", 1, interior)
        result = result[:, None, :]
    else:
        weight_grad = lat_allreduce(grad_terms, "lat", 1)
        edge_rows = jnp.stack([interior[:, 0], interior[:, 2]], axis=1)
        arrived = padded_2(edge_rows, (("lat", 1),), 1, False)
        result = interior[:, 1:2]
        result = result.at[:, 0].add(arrived[:, 0])
        result = result.at[:, 0].add(arrived[:, 3])
    return (outputs, result.astype(jnp.bfloat16), weight_grad)


def solution(mesh):
    return jax.shard_map(
        body,
        mesh=mesh,
        in_specs=(
            P("groups", "lat", "lon"),
            P("groups", "lat", "lon"),
            P(),
            P("lat", None, None, None, None),
            P("lat"),
            P("lat", None),
        ),
        out_specs=(P("groups", "lat", "lon"), P("groups", "lat", "lon"), P("groups", "lon", None)),
        check_vma=False,
    )
```

```python
import jax
import jax.numpy as jnp
from jax import lax
from jax.experimental import pallas as pl
from jax.experimental.pallas import tpu as pltpu
from jax.sharding import PartitionSpec as P

HALO = 128


def padded_2(cells, sides, width, closed):
    for axis, dim in sides:
        count = lax.axis_size(axis)
        ends = count if closed else count - 1
        head = lax.slice_in_dim(cells, 0, width, axis=dim)
        tail = lax.slice_in_dim(cells, cells.shape[dim] - width, cells.shape[dim], axis=dim)
        cells = jnp.concatenate(
            [
                lax.ppermute(tail, axis, [(i, (i + 1) % count) for i in range(ends)]),
                cells,
                lax.ppermute(head, axis, [((i + 1) % count, i) for i in range(ends)]),
            ],
            axis=dim,
        )
    return cells


def build_taps(filter_taps, cycle_counts, cycle_blocks):
    slot_total = cycle_blocks.shape[1]
    width_block = filter_taps.shape[4]
    offsets = jnp.arange(width_block, dtype=jnp.int32)
    places = HALO + width_block * cycle_blocks[:, :, None] + offsets[None, None, :]
    live_slots = jnp.arange(slot_total, dtype=jnp.int32)[None, :] < cycle_counts[:, None]
    positions = jnp.arange(2 * HALO, dtype=jnp.int32)
    onehot = jnp.where(
        (places[:, :, :, None] == positions) & live_slots[:, :, None, None], 1.0, 0.0
    ).astype(jnp.float32)
    return jnp.einsum("ikrst,istu->ikru", filter_taps.astype(jnp.float32), onehot)


def toeplitz_kernel(tap_ref, grad_ref, out_ref, contrib_ref):
    kernels, lon_cols, width = out_ref.shape
    acc = None
    for k in range(kernels):
        row = tap_ref[pl.ds(k, 1), :]
        tiled = jnp.broadcast_to(row, (lon_cols, width))
        out_ref[k] = pltpu.roll(tiled, 0, 1, stride=1, stride_axis=0)
        term = jnp.dot(
            grad_ref[:, pl.ds(k * lon_cols, lon_cols)],
            out_ref[k],
            preferred_element_type=jnp.float32,
        )
        acc = term if acc is None else acc + term
    contrib_ref[...] = acc


def toeplitz(tap_row, out_width, grad_piece):
    kernels, stencil_rows, reach = tap_row.shape
    window_len = out_width + reach
    padded = jnp.pad(tap_row.astype(jnp.float32), ((0, 0), (0, 0), (0, window_len - reach)))
    padded = padded.reshape(kernels, stencil_rows * window_len).astype(jnp.bfloat16)
    out, contrib = pl.pallas_call(
        toeplitz_kernel,
        out_shape=(
            jax.ShapeDtypeStruct((kernels, out_width, stencil_rows * window_len), jnp.bfloat16),
            jax.ShapeDtypeStruct((grad_piece.shape[0], stencil_rows * window_len), jnp.float32),
        ),
    )(padded, grad_piece)
    return out.reshape(kernels * out_width, stencil_rows * window_len), contrib


def lat_allreduce(x, axis, dim):
    count = lax.axis_size(axis)
    steps = count.bit_length() - 1
    if (1 << steps) != count or x.shape[dim] % count:
        return lax.psum(x, axis)
    index = lax.axis_index(axis)
    size = x.shape[dim] // count
    parts = [lax.dynamic_slice_in_dim(x, index * size, size, axis=dim)]
    for d in range(1, count):
        send = lax.dynamic_slice_in_dim(x, (index ^ d) * size, size, axis=dim)
        parts.append(lax.ppermute(send, axis, [(i, i ^ d) for i in range(count)]))
    for s in range(steps):
        parts = [parts[2 * e] + parts[2 * e + 1] for e in range(len(parts) // 2)]
    mine = parts[0]
    out = jnp.zeros(x.shape, x.dtype)
    out = lax.dynamic_update_slice_in_dim(out, mine, index * size, axis=dim)
    for d in range(1, count):
        recv = lax.ppermute(mine, axis, [(i, i ^ d) for i in range(count)])
        out = lax.dynamic_update_slice_in_dim(out, recv, (index ^ d) * size, axis=dim)
    return out


def row_kernel(ext_ref, mt_ref, w_ref, up_ref, out_ref, gt_ref):
    stencil_rows, channels, _ = ext_ref.shape
    n_blocks, o_block, lon_cols = up_ref.shape
    kernels = w_ref.shape[0]
    window_len = mt_ref.shape[1] // stencil_rows
    contract_last = (((1,), (1,)), ((), ()))
    gt_ref[...] = jnp.zeros(gt_ref.shape, gt_ref.dtype)
    for d in range(n_blocks):
        acc = None
        for r in range(stencil_rows):
            win = ext_ref[r, :, pl.ds(d * lon_cols, window_len)]
            part = lax.dot_general(
                win,
                mt_ref[:, pl.ds(r * window_len, window_len)],
                contract_last,
                preferred_element_type=jnp.float32,
            )
            acc = part if acc is None else acc + part
        resp = acc.astype(jnp.bfloat16)
        up_d = up_ref[d]
        for k in range(kernels):
            resp_k = resp[:, k * lon_cols : (k + 1) * lon_cols]
            gt_ref[k] += lax.dot_general(
                up_d, resp_k, contract_last, preferred_element_type=jnp.float32
            )
        if d == 0:
            total = None
            for k in range(kernels):
                term = jnp.dot(
                    w_ref[k],
                    resp[:, k * lon_cols : (k + 1) * lon_cols],
                    preferred_element_type=jnp.float32,
                )
                total = term if total is None else total + term
            out_ref[...] = total.astype(out_ref.dtype)


def row_products(ext, matrix, weights, up_rel):
    stencil_rows, channels, _ = ext.shape
    n_blocks, o_block, lon_cols = up_rel.shape
    kernels = weights.shape[0]
    flops = 2 * n_blocks * channels * matrix.shape[0] * matrix.shape[1]
    flops += 2 * n_blocks * kernels * o_block * lon_cols * channels
    flops += 2 * kernels * weights.shape[1] * channels * lon_cols
    nbytes = 2 * (ext.size + matrix.size + weights.size + up_rel.size)
    nbytes += 2 * weights.shape[1] * lon_cols + 4 * kernels * o_block * channels
    return pl.pallas_call(
        row_kernel,
        out_shape=(
            jax.ShapeDtypeStruct((weights.shape[1], lon_cols), jnp.bfloat16),
            jax.ShapeDtypeStruct((kernels, o_block, channels), jnp.float32),
        ),
        cost_estimate=pl.CostEstimate(flops=flops, transcendentals=0, bytes_accessed=nbytes),
    )(ext, matrix, weights, up_rel)


def body(fields, upstream, weights, filter_taps, cycle_counts, cycle_blocks):
    channels, lat_rows, lon_cols = fields.shape
    kernels = weights.shape[0]
    window_len = lon_cols + 2 * HALO
    n_lon = lax.axis_size("lon")
    lon_at = lax.axis_index("lon")
    tap_table = build_taps(filter_taps, cycle_counts, cycle_blocks).astype(jnp.bfloat16)
    response_grad = jnp.einsum(
        "koc,oij->cikj", weights, upstream, preferred_element_type=jnp.float32
    ).astype(jnp.bfloat16)
    grad_piece = response_grad[:, 0].reshape(channels, kernels * lon_cols)
    matrix, contrib = toeplitz(tap_table[0], lon_cols, grad_piece)
    o_block = upstream.shape[0] // n_lon
    up_row = upstream[:, 0]
    blocks = [fields[:, 0]]
    up_parts = [lax.dynamic_slice_in_dim(up_row, lon_at * o_block, o_block, axis=0)]
    for d in range(1, n_lon):
        part = lax.dynamic_slice_in_dim(up_row, ((lon_at - d) % n_lon) * o_block, o_block, axis=0)
        both = lax.ppermute(
            jnp.concatenate([fields[:, 0], part], axis=0),
            "lon",
            [(p, (p - d) % n_lon) for p in range(n_lon)],
        )
        blocks.append(both[:channels])
        up_parts.append(both[channels:])
    up_rel = jnp.stack(up_parts, axis=0)
    row = jnp.concatenate(blocks, axis=1)
    count = lax.axis_size("lat")
    below = lax.ppermute(row, "lat", [(i, i + 1) for i in range(count - 1)])
    above = lax.ppermute(row, "lat", [(i + 1, i) for i in range(count - 1)])
    rows = jnp.stack([below, row, above], axis=0)
    ext = jnp.concatenate([rows[:, :, rows.shape[2] - HALO :], rows, rows[:, :, :HALO]], axis=2)
    out_row, grad_terms = row_products(ext, matrix, weights, up_rel)
    outputs = out_row[:, None, :]
    weight_grad = lat_allreduce(grad_terms, "lat", 1)
    accumulated = jnp.zeros((channels, lat_rows + 2, window_len), jnp.float32)
    cycle_row = 0
    accumulated = accumulated.at[:, cycle_row : cycle_row + 3].add(
        contrib.reshape(channels, 3, window_len)
    )
    rim_columns = jnp.concatenate(
        [accumulated[:, :, :HALO], accumulated[:, :, HALO + lon_cols :]], axis=2
    )
    arrived = padded_2(rim_columns, (("lon", 2),), HALO, True)
    interior = accumulated[:, :, HALO : HALO + lon_cols]
    interior = interior.at[:, :, :HALO].add(arrived[:, :, :HALO])
    interior = interior.at[:, :, lon_cols - HALO :].add(arrived[:, :, 3 * HALO :])
    edge_rows = jnp.stack([interior[:, 0], interior[:, lat_rows + 1]], axis=1)
    arrived = padded_2(edge_rows, (("lat", 1),), 1, False)
    result = interior[:, 1 : lat_rows + 1]
    result = result.at[:, 0].add(arrived[:, 0])
    result = result.at[:, lat_rows - 1].add(arrived[:, 3])
    return (outputs, result.astype(jnp.bfloat16), weight_grad)


def solution(mesh):
    return jax.shard_map(
        body,
        mesh=mesh,
        in_specs=(
            P("groups", "lat", "lon"),
            P("groups", "lat", "lon"),
            P(),
            P("lat", None, None, None, None),
            P("lat"),
            P("lat", None),
        ),
        out_specs=(P("groups", "lat", "lon"), P("groups", "lat", "lon"), P("groups", "lon", None)),
        check_vma=False,
    )
```

```python
import jax
import jax.numpy as jnp
from jax import lax
from jax.experimental import pallas as pl
from jax.experimental.pallas import tpu as pltpu
from jax.sharding import PartitionSpec as P

HALO = 128


def padded_2(cells, sides, width, closed):
    for axis, dim in sides:
        count = lax.axis_size(axis)
        ends = count if closed else count - 1
        head = lax.slice_in_dim(cells, 0, width, axis=dim)
        tail = lax.slice_in_dim(cells, cells.shape[dim] - width, cells.shape[dim], axis=dim)
        cells = jnp.concatenate(
            [
                lax.ppermute(tail, axis, [(i, (i + 1) % count) for i in range(ends)]),
                cells,
                lax.ppermute(head, axis, [((i + 1) % count, i) for i in range(ends)]),
            ],
            axis=dim,
        )
    return cells


def build_taps(filter_taps, cycle_counts, cycle_blocks):
    slot_total = cycle_blocks.shape[1]
    width_block = filter_taps.shape[4]
    offsets = jnp.arange(width_block, dtype=jnp.int32)
    places = HALO + width_block * cycle_blocks[:, :, None] + offsets[None, None, :]
    live_slots = jnp.arange(slot_total, dtype=jnp.int32)[None, :] < cycle_counts[:, None]
    positions = jnp.arange(2 * HALO, dtype=jnp.int32)
    onehot = jnp.where(
        (places[:, :, :, None] == positions) & live_slots[:, :, None, None], 1.0, 0.0
    ).astype(jnp.float32)
    return jnp.einsum("ikrst,istu->ikru", filter_taps.astype(jnp.float32), onehot)


def toeplitz_kernel(tap_ref, grad_ref, out_ref, contrib_ref):
    _, lon_cols, width = out_ref.shape
    k = pl.program_id(0)
    row = tap_ref[0]
    tiled = jnp.broadcast_to(row, (lon_cols, width))
    out_ref[0] = pltpu.roll(tiled, 0, 1, stride=1, stride_axis=0)
    term = jnp.dot(grad_ref[...], out_ref[0], preferred_element_type=jnp.float32)

    @pl.when(k == 0)
    def _():
        contrib_ref[...] = term

    @pl.when(k > 0)
    def _():
        contrib_ref[...] += term


def toeplitz(tap_row, out_width, grad_piece):
    kernels, stencil_rows, reach = tap_row.shape
    window_len = out_width + reach
    width = stencil_rows * window_len
    padded = jnp.pad(tap_row.astype(jnp.float32), ((0, 0), (0, 0), (0, window_len - reach)))
    padded = padded.reshape(kernels, 1, width).astype(jnp.bfloat16)
    channels = grad_piece.shape[0]
    out, contrib = pl.pallas_call(
        toeplitz_kernel,
        grid=(kernels,),
        in_specs=[
            pl.BlockSpec((1, 1, width), lambda k: (k, 0, 0)),
            pl.BlockSpec((channels, out_width), lambda k: (0, k)),
        ],
        out_specs=[
            pl.BlockSpec((1, out_width, width), lambda k: (k, 0, 0)),
            pl.BlockSpec((channels, width), lambda k: (0, 0)),
        ],
        out_shape=(
            jax.ShapeDtypeStruct((kernels, out_width, width), jnp.bfloat16),
            jax.ShapeDtypeStruct((channels, width), jnp.float32),
        ),
        compiler_params=pltpu.CompilerParams(dimension_semantics=("arbitrary",)),
    )(padded, grad_piece)
    return out.reshape(kernels * out_width, width), contrib


def lat_allreduce(x, axis, dim):
    count = lax.axis_size(axis)
    steps = count.bit_length() - 1
    if (1 << steps) != count or x.shape[dim] % count:
        return lax.psum(x, axis)
    index = lax.axis_index(axis)
    size = x.shape[dim] // count
    parts = [lax.dynamic_slice_in_dim(x, index * size, size, axis=dim)]
    for d in range(1, count):
        send = lax.dynamic_slice_in_dim(x, (index ^ d) * size, size, axis=dim)
        parts.append(lax.ppermute(send, axis, [(i, i ^ d) for i in range(count)]))
    for s in range(steps):
        parts = [parts[2 * e] + parts[2 * e + 1] for e in range(len(parts) // 2)]
    mine = parts[0]
    out = jnp.zeros(x.shape, x.dtype)
    out = lax.dynamic_update_slice_in_dim(out, mine, index * size, axis=dim)
    for d in range(1, count):
        recv = lax.ppermute(mine, axis, [(i, i ^ d) for i in range(count)])
        out = lax.dynamic_update_slice_in_dim(out, recv, (index ^ d) * size, axis=dim)
    return out


def row_kernel(ext_ref, mt_ref, w_ref, up_ref, out_ref, gt_ref):
    stencil_rows, channels, _ = ext_ref.shape
    n_blocks, o_block, lon_cols = up_ref.shape
    kernels = w_ref.shape[0]
    window_len = mt_ref.shape[1] // stencil_rows
    contract_last = (((1,), (1,)), ((), ()))
    gt_ref[...] = jnp.zeros(gt_ref.shape, gt_ref.dtype)
    for d in range(n_blocks):
        acc = None
        for r in range(stencil_rows):
            win = ext_ref[r, :, pl.ds(d * lon_cols, window_len)]
            part = lax.dot_general(
                win,
                mt_ref[:, pl.ds(r * window_len, window_len)],
                contract_last,
                preferred_element_type=jnp.float32,
            )
            acc = part if acc is None else acc + part
        resp = acc.astype(jnp.bfloat16)
        up_d = up_ref[d]
        for k in range(kernels):
            resp_k = resp[:, k * lon_cols : (k + 1) * lon_cols]
            gt_ref[k] += lax.dot_general(
                up_d, resp_k, contract_last, preferred_element_type=jnp.float32
            )
        if d == 0:
            total = None
            for k in range(kernels):
                term = jnp.dot(
                    w_ref[k],
                    resp[:, k * lon_cols : (k + 1) * lon_cols],
                    preferred_element_type=jnp.float32,
                )
                total = term if total is None else total + term
            out_ref[...] = total.astype(out_ref.dtype)


def row_products(ext, matrix, weights, up_rel):
    stencil_rows, channels, _ = ext.shape
    n_blocks, o_block, lon_cols = up_rel.shape
    kernels = weights.shape[0]
    flops = 2 * n_blocks * channels * matrix.shape[0] * matrix.shape[1]
    flops += 2 * n_blocks * kernels * o_block * lon_cols * channels
    flops += 2 * kernels * weights.shape[1] * channels * lon_cols
    nbytes = 2 * (ext.size + matrix.size + weights.size + up_rel.size)
    nbytes += 2 * weights.shape[1] * lon_cols + 4 * kernels * o_block * channels
    return pl.pallas_call(
        row_kernel,
        out_shape=(
            jax.ShapeDtypeStruct((weights.shape[1], lon_cols), jnp.bfloat16),
            jax.ShapeDtypeStruct((kernels, o_block, channels), jnp.float32),
        ),
        cost_estimate=pl.CostEstimate(flops=flops, transcendentals=0, bytes_accessed=nbytes),
    )(ext, matrix, weights, up_rel)


def body(fields, upstream, weights, filter_taps, cycle_counts, cycle_blocks):
    channels, lat_rows, lon_cols = fields.shape
    kernels = weights.shape[0]
    window_len = lon_cols + 2 * HALO
    n_lon = lax.axis_size("lon")
    lon_at = lax.axis_index("lon")
    tap_table = build_taps(filter_taps, cycle_counts, cycle_blocks).astype(jnp.bfloat16)
    response_grad = jnp.einsum(
        "koc,oij->cikj", weights, upstream, preferred_element_type=jnp.float32
    ).astype(jnp.bfloat16)
    grad_piece = response_grad[:, 0].reshape(channels, kernels * lon_cols)
    matrix, contrib = toeplitz(tap_table[0], lon_cols, grad_piece)
    o_block = upstream.shape[0] // n_lon
    up_row = upstream[:, 0]
    blocks = [fields[:, 0]]
    up_parts = [lax.dynamic_slice_in_dim(up_row, lon_at * o_block, o_block, axis=0)]
    for d in range(1, n_lon):
        part = lax.dynamic_slice_in_dim(up_row, ((lon_at - d) % n_lon) * o_block, o_block, axis=0)
        both = lax.ppermute(
            jnp.concatenate([fields[:, 0], part], axis=0),
            "lon",
            [(p, (p - d) % n_lon) for p in range(n_lon)],
        )
        blocks.append(both[:channels])
        up_parts.append(both[channels:])
    up_rel = jnp.stack(up_parts, axis=0)
    row = jnp.concatenate(blocks, axis=1)
    count = lax.axis_size("lat")
    below = lax.ppermute(row, "lat", [(i, i + 1) for i in range(count - 1)])
    above = lax.ppermute(row, "lat", [(i + 1, i) for i in range(count - 1)])
    rows = jnp.stack([below, row, above], axis=0)
    ext = jnp.concatenate([rows[:, :, rows.shape[2] - HALO :], rows, rows[:, :, :HALO]], axis=2)
    out_row, grad_terms = row_products(ext, matrix, weights, up_rel)
    outputs = out_row[:, None, :]
    weight_grad = lat_allreduce(grad_terms, "lat", 1)
    accumulated = jnp.zeros((channels, lat_rows + 2, window_len), jnp.float32)
    cycle_row = 0
    accumulated = accumulated.at[:, cycle_row : cycle_row + 3].add(
        contrib.reshape(channels, 3, window_len)
    )
    rim_columns = jnp.concatenate(
        [accumulated[:, :, :HALO], accumulated[:, :, HALO + lon_cols :]], axis=2
    )
    arrived = padded_2(rim_columns, (("lon", 2),), HALO, True)
    interior = accumulated[:, :, HALO : HALO + lon_cols]
    interior = interior.at[:, :, :HALO].add(arrived[:, :, :HALO])
    interior = interior.at[:, :, lon_cols - HALO :].add(arrived[:, :, 3 * HALO :])
    edge_rows = jnp.stack([interior[:, 0], interior[:, lat_rows + 1]], axis=1)
    arrived = padded_2(edge_rows, (("lat", 1),), 1, False)
    result = interior[:, 1 : lat_rows + 1]
    result = result.at[:, 0].add(arrived[:, 0])
    result = result.at[:, lat_rows - 1].add(arrived[:, 3])
    return (outputs, result.astype(jnp.bfloat16), weight_grad)


def solution(mesh):
    return jax.shard_map(
        body,
        mesh=mesh,
        in_specs=(
            P("groups", "lat", "lon"),
            P("groups", "lat", "lon"),
            P(),
            P("lat", None, None, None, None),
            P("lat"),
            P("lat", None),
        ),
        out_specs=(P("groups", "lat", "lon"), P("groups", "lat", "lon"), P("groups", "lon", None)),
        check_vma=False,
    )
```

```python
import jax
import jax.numpy as jnp
from jax import lax
from jax.experimental import pallas as pl
from jax.experimental.pallas import tpu as pltpu
from jax.sharding import PartitionSpec as P

HALO = 128


def padded_2(cells, sides, width, closed):
    for axis, dim in sides:
        count = lax.axis_size(axis)
        ends = count if closed else count - 1
        head = lax.slice_in_dim(cells, 0, width, axis=dim)
        tail = lax.slice_in_dim(cells, cells.shape[dim] - width, cells.shape[dim], axis=dim)
        cells = jnp.concatenate(
            [
                lax.ppermute(tail, axis, [(i, (i + 1) % count) for i in range(ends)]),
                cells,
                lax.ppermute(head, axis, [((i + 1) % count, i) for i in range(ends)]),
            ],
            axis=dim,
        )
    return cells


def build_taps(filter_taps, cycle_counts, cycle_blocks):
    slot_total = cycle_blocks.shape[1]
    width_block = filter_taps.shape[4]
    offsets = jnp.arange(width_block, dtype=jnp.int32)
    places = HALO + width_block * cycle_blocks[:, :, None] + offsets[None, None, :]
    live_slots = jnp.arange(slot_total, dtype=jnp.int32)[None, :] < cycle_counts[:, None]
    positions = jnp.arange(2 * HALO, dtype=jnp.int32)
    onehot = jnp.where(
        (places[:, :, :, None] == positions) & live_slots[:, :, None, None], 1.0, 0.0
    ).astype(jnp.float32)
    return jnp.einsum("ikrst,istu->ikru", filter_taps.astype(jnp.float32), onehot)


def toeplitz_kernel(tap_ref, w_ref, up_ref, out_ref, contrib_ref):
    kernels, lon_cols, width = out_ref.shape
    contract_first = (((0,), (0,)), ((), ()))
    acc = None
    for k in range(kernels):
        row = tap_ref[pl.ds(k, 1), :]
        tiled = jnp.broadcast_to(row, (lon_cols, width))
        out_ref[k] = pltpu.roll(tiled, 0, 1, stride=1, stride_axis=0)
        grad_k = lax.dot_general(
            w_ref[k], up_ref[...], contract_first, preferred_element_type=jnp.float32
        ).astype(jnp.bfloat16)
        term = jnp.dot(grad_k, out_ref[k], preferred_element_type=jnp.float32)
        acc = term if acc is None else acc + term
    contrib_ref[...] = acc


def toeplitz(tap_row, out_width, weights, up_row):
    kernels, stencil_rows, reach = tap_row.shape
    window_len = out_width + reach
    padded = jnp.pad(tap_row.astype(jnp.float32), ((0, 0), (0, 0), (0, window_len - reach)))
    padded = padded.reshape(kernels, stencil_rows * window_len).astype(jnp.bfloat16)
    out, contrib = pl.pallas_call(
        toeplitz_kernel,
        out_shape=(
            jax.ShapeDtypeStruct((kernels, out_width, stencil_rows * window_len), jnp.bfloat16),
            jax.ShapeDtypeStruct((weights.shape[2], stencil_rows * window_len), jnp.float32),
        ),
    )(padded, weights, up_row)
    return out.reshape(kernels * out_width, stencil_rows * window_len), contrib


def lat_allreduce(x, axis, dim):
    count = lax.axis_size(axis)
    steps = count.bit_length() - 1
    if (1 << steps) != count or x.shape[dim] % count:
        return lax.psum(x, axis)
    index = lax.axis_index(axis)
    size = x.shape[dim] // count
    parts = [lax.dynamic_slice_in_dim(x, index * size, size, axis=dim)]
    for d in range(1, count):
        send = lax.dynamic_slice_in_dim(x, (index ^ d) * size, size, axis=dim)
        parts.append(lax.ppermute(send, axis, [(i, i ^ d) for i in range(count)]))
    for s in range(steps):
        parts = [parts[2 * e] + parts[2 * e + 1] for e in range(len(parts) // 2)]
    mine = parts[0]
    out = jnp.zeros(x.shape, x.dtype)
    out = lax.dynamic_update_slice_in_dim(out, mine, index * size, axis=dim)
    for d in range(1, count):
        recv = lax.ppermute(mine, axis, [(i, i ^ d) for i in range(count)])
        out = lax.dynamic_update_slice_in_dim(out, recv, (index ^ d) * size, axis=dim)
    return out


def row_kernel(ext_ref, mt_ref, w_ref, up_ref, out_ref, gt_ref):
    stencil_rows, channels, _ = ext_ref.shape
    n_blocks, o_block, lon_cols = up_ref.shape
    kernels = w_ref.shape[0]
    window_len = mt_ref.shape[1] // stencil_rows
    contract_last = (((1,), (1,)), ((), ()))
    gt_ref[...] = jnp.zeros(gt_ref.shape, gt_ref.dtype)
    for d in range(n_blocks):
        acc = None
        for r in range(stencil_rows):
            win = ext_ref[r, :, pl.ds(d * lon_cols, window_len)]
            part = lax.dot_general(
                win,
                mt_ref[:, pl.ds(r * window_len, window_len)],
                contract_last,
                preferred_element_type=jnp.float32,
            )
            acc = part if acc is None else acc + part
        resp = acc.astype(jnp.bfloat16)
        up_d = up_ref[d]
        for k in range(kernels):
            resp_k = resp[:, k * lon_cols : (k + 1) * lon_cols]
            gt_ref[k] += lax.dot_general(
                up_d, resp_k, contract_last, preferred_element_type=jnp.float32
            )
        if d == 0:
            total = None
            for k in range(kernels):
                term = jnp.dot(
                    w_ref[k],
                    resp[:, k * lon_cols : (k + 1) * lon_cols],
                    preferred_element_type=jnp.float32,
                )
                total = term if total is None else total + term
            out_ref[...] = total.astype(out_ref.dtype)


def row_products(ext, matrix, weights, up_rel):
    stencil_rows, channels, _ = ext.shape
    n_blocks, o_block, lon_cols = up_rel.shape
    kernels = weights.shape[0]
    flops = 2 * n_blocks * channels * matrix.shape[0] * matrix.shape[1]
    flops += 2 * n_blocks * kernels * o_block * lon_cols * channels
    flops += 2 * kernels * weights.shape[1] * channels * lon_cols
    nbytes = 2 * (ext.size + matrix.size + weights.size + up_rel.size)
    nbytes += 2 * weights.shape[1] * lon_cols + 4 * kernels * o_block * channels
    return pl.pallas_call(
        row_kernel,
        out_shape=(
            jax.ShapeDtypeStruct((weights.shape[1], lon_cols), jnp.bfloat16),
            jax.ShapeDtypeStruct((kernels, o_block, channels), jnp.float32),
        ),
        cost_estimate=pl.CostEstimate(flops=flops, transcendentals=0, bytes_accessed=nbytes),
    )(ext, matrix, weights, up_rel)


def body(fields, upstream, weights, filter_taps, cycle_counts, cycle_blocks):
    channels, lat_rows, lon_cols = fields.shape
    kernels = weights.shape[0]
    window_len = lon_cols + 2 * HALO
    n_lon = lax.axis_size("lon")
    lon_at = lax.axis_index("lon")
    tap_table = build_taps(filter_taps, cycle_counts, cycle_blocks).astype(jnp.bfloat16)
    matrix, contrib = toeplitz(tap_table[0], lon_cols, weights, upstream[:, 0])
    o_block = upstream.shape[0] // n_lon
    up_row = upstream[:, 0]
    blocks = [fields[:, 0]]
    up_parts = [lax.dynamic_slice_in_dim(up_row, lon_at * o_block, o_block, axis=0)]
    for d in range(1, n_lon):
        part = lax.dynamic_slice_in_dim(up_row, ((lon_at - d) % n_lon) * o_block, o_block, axis=0)
        both = lax.ppermute(
            jnp.concatenate([fields[:, 0], part], axis=0),
            "lon",
            [(p, (p - d) % n_lon) for p in range(n_lon)],
        )
        blocks.append(both[:channels])
        up_parts.append(both[channels:])
    up_rel = jnp.stack(up_parts, axis=0)
    row = jnp.concatenate(blocks, axis=1)
    count = lax.axis_size("lat")
    below = lax.ppermute(row, "lat", [(i, i + 1) for i in range(count - 1)])
    above = lax.ppermute(row, "lat", [(i + 1, i) for i in range(count - 1)])
    rows = jnp.stack([below, row, above], axis=0)
    ext = jnp.concatenate([rows[:, :, rows.shape[2] - HALO :], rows, rows[:, :, :HALO]], axis=2)
    out_row, grad_terms = row_products(ext, matrix, weights, up_rel)
    outputs = out_row[:, None, :]
    weight_grad = lat_allreduce(grad_terms, "lat", 1)
    accumulated = jnp.zeros((channels, lat_rows + 2, window_len), jnp.float32)
    cycle_row = 0
    accumulated = accumulated.at[:, cycle_row : cycle_row + 3].add(
        contrib.reshape(channels, 3, window_len)
    )
    rim_columns = jnp.concatenate(
        [accumulated[:, :, :HALO], accumulated[:, :, HALO + lon_cols :]], axis=2
    )
    arrived = padded_2(rim_columns, (("lon", 2),), HALO, True)
    interior = accumulated[:, :, HALO : HALO + lon_cols]
    interior = interior.at[:, :, :HALO].add(arrived[:, :, :HALO])
    interior = interior.at[:, :, lon_cols - HALO :].add(arrived[:, :, 3 * HALO :])
    edge_rows = jnp.stack([interior[:, 0], interior[:, lat_rows + 1]], axis=1)
    arrived = padded_2(edge_rows, (("lat", 1),), 1, False)
    result = interior[:, 1 : lat_rows + 1]
    result = result.at[:, 0].add(arrived[:, 0])
    result = result.at[:, lat_rows - 1].add(arrived[:, 3])
    return (outputs, result.astype(jnp.bfloat16), weight_grad)


def solution(mesh):
    return jax.shard_map(
        body,
        mesh=mesh,
        in_specs=(
            P("groups", "lat", "lon"),
            P("groups", "lat", "lon"),
            P(),
            P("lat", None, None, None, None),
            P("lat"),
            P("lat", None),
        ),
        out_specs=(P("groups", "lat", "lon"), P("groups", "lat", "lon"), P("groups", "lon", None)),
        check_vma=False,
    )
```

```python
import jax
import jax.numpy as jnp
from jax import lax
from jax.experimental import pallas as pl
from jax.experimental.pallas import tpu as pltpu
from jax.sharding import PartitionSpec as P

HALO = 128


def padded_2(cells, sides, width, closed):
    for axis, dim in sides:
        count = lax.axis_size(axis)
        ends = count if closed else count - 1
        head = lax.slice_in_dim(cells, 0, width, axis=dim)
        tail = lax.slice_in_dim(cells, cells.shape[dim] - width, cells.shape[dim], axis=dim)
        cells = jnp.concatenate(
            [
                lax.ppermute(tail, axis, [(i, (i + 1) % count) for i in range(ends)]),
                cells,
                lax.ppermute(head, axis, [((i + 1) % count, i) for i in range(ends)]),
            ],
            axis=dim,
        )
    return cells


def build_taps(filter_taps, cycle_counts, cycle_blocks):
    slot_total = cycle_blocks.shape[1]
    width_block = filter_taps.shape[4]
    offsets = jnp.arange(width_block, dtype=jnp.int32)
    places = HALO + width_block * cycle_blocks[:, :, None] + offsets[None, None, :]
    live_slots = jnp.arange(slot_total, dtype=jnp.int32)[None, :] < cycle_counts[:, None]
    positions = jnp.arange(2 * HALO, dtype=jnp.int32)
    onehot = jnp.where(
        (places[:, :, :, None] == positions) & live_slots[:, :, None, None], 1.0, 0.0
    ).astype(jnp.float32)
    return jnp.einsum("ikrst,istu->ikru", filter_taps.astype(jnp.float32), onehot)


def toeplitz_kernel(tap_ref, w_ref, up_ref, out_ref, contrib_ref):
    kernels, lon_cols, width = out_ref.shape
    contract_first = (((0,), (0,)), ((), ()))
    acc = None
    for k in range(kernels):
        row = tap_ref[pl.ds(k, 1), :]
        tiled = jnp.broadcast_to(row, (lon_cols, width))
        out_ref[k] = pltpu.roll(tiled, 0, 1, stride=1, stride_axis=0)
        grad_k = lax.dot_general(
            w_ref[k], up_ref[...], contract_first, preferred_element_type=jnp.float32
        ).astype(jnp.bfloat16)
        term = jnp.dot(grad_k, out_ref[k], preferred_element_type=jnp.float32)
        acc = term if acc is None else acc + term
    window_len = width // contrib_ref.shape[0]
    for r in range(contrib_ref.shape[0]):
        contrib_ref[r] = acc[:, r * window_len : (r + 1) * window_len]


def toeplitz(tap_row, out_width, weights, up_row):
    kernels, stencil_rows, reach = tap_row.shape
    window_len = out_width + reach
    padded = jnp.pad(tap_row.astype(jnp.float32), ((0, 0), (0, 0), (0, window_len - reach)))
    padded = padded.reshape(kernels, stencil_rows * window_len).astype(jnp.bfloat16)
    out, contrib = pl.pallas_call(
        toeplitz_kernel,
        out_shape=(
            jax.ShapeDtypeStruct((kernels, out_width, stencil_rows * window_len), jnp.bfloat16),
            jax.ShapeDtypeStruct((stencil_rows, weights.shape[2], window_len), jnp.float32),
        ),
    )(padded, weights, up_row)
    return out.reshape(kernels * out_width, stencil_rows * window_len), contrib


def lat_allreduce(x, axis, dim):
    count = lax.axis_size(axis)
    steps = count.bit_length() - 1
    if (1 << steps) != count or x.shape[dim] % count:
        return lax.psum(x, axis)
    index = lax.axis_index(axis)
    size = x.shape[dim] // count
    parts = [lax.dynamic_slice_in_dim(x, index * size, size, axis=dim)]
    for d in range(1, count):
        send = lax.dynamic_slice_in_dim(x, (index ^ d) * size, size, axis=dim)
        parts.append(lax.ppermute(send, axis, [(i, i ^ d) for i in range(count)]))
    for s in range(steps):
        parts = [parts[2 * e] + parts[2 * e + 1] for e in range(len(parts) // 2)]
    mine = parts[0]
    out = jnp.zeros(x.shape, x.dtype)
    out = lax.dynamic_update_slice_in_dim(out, mine, index * size, axis=dim)
    for d in range(1, count):
        recv = lax.ppermute(mine, axis, [(i, i ^ d) for i in range(count)])
        out = lax.dynamic_update_slice_in_dim(out, recv, (index ^ d) * size, axis=dim)
    return out


def row_kernel(ext_ref, mt_ref, w_ref, up_ref, out_ref, gt_ref):
    stencil_rows, channels, _ = ext_ref.shape
    n_blocks, o_block, lon_cols = up_ref.shape
    kernels = w_ref.shape[0]
    window_len = mt_ref.shape[1] // stencil_rows
    contract_last = (((1,), (1,)), ((), ()))
    gt_ref[...] = jnp.zeros(gt_ref.shape, gt_ref.dtype)
    for d in range(n_blocks):
        acc = None
        for r in range(stencil_rows):
            win = ext_ref[r, :, pl.ds(d * lon_cols, window_len)]
            part = lax.dot_general(
                win,
                mt_ref[:, pl.ds(r * window_len, window_len)],
                contract_last,
                preferred_element_type=jnp.float32,
            )
            acc = part if acc is None else acc + part
        resp = acc.astype(jnp.bfloat16)
        up_d = up_ref[d]
        for k in range(kernels):
            resp_k = resp[:, k * lon_cols : (k + 1) * lon_cols]
            gt_ref[k] += lax.dot_general(
                up_d, resp_k, contract_last, preferred_element_type=jnp.float32
            )
        if d == 0:
            total = None
            for k in range(kernels):
                term = jnp.dot(
                    w_ref[k],
                    resp[:, k * lon_cols : (k + 1) * lon_cols],
                    preferred_element_type=jnp.float32,
                )
                total = term if total is None else total + term
            out_ref[...] = total.astype(out_ref.dtype)


def row_products(ext, matrix, weights, up_rel):
    stencil_rows, channels, _ = ext.shape
    n_blocks, o_block, lon_cols = up_rel.shape
    kernels = weights.shape[0]
    flops = 2 * n_blocks * channels * matrix.shape[0] * matrix.shape[1]
    flops += 2 * n_blocks * kernels * o_block * lon_cols * channels
    flops += 2 * kernels * weights.shape[1] * channels * lon_cols
    nbytes = 2 * (ext.size + matrix.size + weights.size + up_rel.size)
    nbytes += 2 * weights.shape[1] * lon_cols + 4 * kernels * o_block * channels
    return pl.pallas_call(
        row_kernel,
        out_shape=(
            jax.ShapeDtypeStruct((weights.shape[1], lon_cols), jnp.bfloat16),
            jax.ShapeDtypeStruct((kernels, o_block, channels), jnp.float32),
        ),
        cost_estimate=pl.CostEstimate(flops=flops, transcendentals=0, bytes_accessed=nbytes),
    )(ext, matrix, weights, up_rel)


def body(fields, upstream, weights, filter_taps, cycle_counts, cycle_blocks):
    channels, lat_rows, lon_cols = fields.shape
    kernels = weights.shape[0]
    window_len = lon_cols + 2 * HALO
    n_lon = lax.axis_size("lon")
    lon_at = lax.axis_index("lon")
    tap_table = build_taps(filter_taps, cycle_counts, cycle_blocks).astype(jnp.bfloat16)
    matrix, contrib = toeplitz(tap_table[0], lon_cols, weights, upstream[:, 0])
    o_block = upstream.shape[0] // n_lon
    up_row = upstream[:, 0]
    blocks = [fields[:, 0]]
    up_parts = [lax.dynamic_slice_in_dim(up_row, lon_at * o_block, o_block, axis=0)]
    for d in range(1, n_lon):
        part = lax.dynamic_slice_in_dim(up_row, ((lon_at - d) % n_lon) * o_block, o_block, axis=0)
        both = lax.ppermute(
            jnp.concatenate([fields[:, 0], part], axis=0),
            "lon",
            [(p, (p - d) % n_lon) for p in range(n_lon)],
        )
        blocks.append(both[:channels])
        up_parts.append(both[channels:])
    up_rel = jnp.stack(up_parts, axis=0)
    row = jnp.concatenate(blocks, axis=1)
    count = lax.axis_size("lat")
    below = lax.ppermute(row, "lat", [(i, i + 1) for i in range(count - 1)])
    above = lax.ppermute(row, "lat", [(i + 1, i) for i in range(count - 1)])
    rows = jnp.stack([below, row, above], axis=0)
    ext = jnp.concatenate([rows[:, :, rows.shape[2] - HALO :], rows, rows[:, :, :HALO]], axis=2)
    out_row, grad_terms = row_products(ext, matrix, weights, up_rel)
    outputs = out_row[:, None, :]
    weight_grad = lat_allreduce(grad_terms, "lat", 1)
    accumulated = jnp.zeros((channels, lat_rows + 2, window_len), jnp.float32)
    cycle_row = 0
    accumulated = accumulated.at[:, cycle_row : cycle_row + 3].add(
        contrib.transpose(1, 0, 2)
    )
    rim_columns = jnp.concatenate(
        [accumulated[:, :, :HALO], accumulated[:, :, HALO + lon_cols :]], axis=2
    )
    arrived = padded_2(rim_columns, (("lon", 2),), HALO, True)
    interior = accumulated[:, :, HALO : HALO + lon_cols]
    interior = interior.at[:, :, :HALO].add(arrived[:, :, :HALO])
    interior = interior.at[:, :, lon_cols - HALO :].add(arrived[:, :, 3 * HALO :])
    edge_rows = jnp.stack([interior[:, 0], interior[:, lat_rows + 1]], axis=1)
    arrived = padded_2(edge_rows, (("lat", 1),), 1, False)
    result = interior[:, 1 : lat_rows + 1]
    result = result.at[:, 0].add(arrived[:, 0])
    result = result.at[:, lat_rows - 1].add(arrived[:, 3])
    return (outputs, result.astype(jnp.bfloat16), weight_grad)


def solution(mesh):
    return jax.shard_map(
        body,
        mesh=mesh,
        in_specs=(
            P("groups", "lat", "lon"),
            P("groups", "lat", "lon"),
            P(),
            P("lat", None, None, None, None),
            P("lat"),
            P("lat", None),
        ),
        out_specs=(P("groups", "lat", "lon"), P("groups", "lat", "lon"), P("groups", "lon", None)),
        check_vma=False,
    )
```

```python
import jax
import jax.numpy as jnp
from jax import lax
from jax.experimental import pallas as pl
from jax.experimental.pallas import tpu as pltpu
from jax.sharding import PartitionSpec as P

HALO = 128


def padded_2(cells, sides, width, closed):
    for axis, dim in sides:
        count = lax.axis_size(axis)
        ends = count if closed else count - 1
        head = lax.slice_in_dim(cells, 0, width, axis=dim)
        tail = lax.slice_in_dim(cells, cells.shape[dim] - width, cells.shape[dim], axis=dim)
        cells = jnp.concatenate(
            [
                lax.ppermute(tail, axis, [(i, (i + 1) % count) for i in range(ends)]),
                cells,
                lax.ppermute(head, axis, [((i + 1) % count, i) for i in range(ends)]),
            ],
            axis=dim,
        )
    return cells


def build_taps(filter_taps, cycle_counts, cycle_blocks):
    slot_total = cycle_blocks.shape[1]
    width_block = filter_taps.shape[4]
    offsets = jnp.arange(width_block, dtype=jnp.int32)
    places = HALO + width_block * cycle_blocks[:, :, None] + offsets[None, None, :]
    live_slots = jnp.arange(slot_total, dtype=jnp.int32)[None, :] < cycle_counts[:, None]
    positions = jnp.arange(2 * HALO, dtype=jnp.int32)
    onehot = jnp.where(
        (places[:, :, :, None] == positions) & live_slots[:, :, None, None], 1.0, 0.0
    ).astype(jnp.float32)
    return jnp.einsum("ikrst,istu->ikru", filter_taps.astype(jnp.float32), onehot)


def toeplitz_kernel(tap_ref, w_ref, up_ref, out_ref, contrib_ref):
    kernels, lon_cols, width = out_ref.shape
    contract_first = (((0,), (0,)), ((), ()))
    acc = None
    for k in range(kernels):
        row = tap_ref[pl.ds(k, 1), :]
        tiled = jnp.broadcast_to(row, (lon_cols, width))
        out_ref[k] = pltpu.roll(tiled, 0, 1, stride=1, stride_axis=0)
        grad_k = lax.dot_general(
            w_ref[k], up_ref[...], contract_first, preferred_element_type=jnp.float32
        ).astype(jnp.bfloat16)
        term = jnp.dot(grad_k, out_ref[k], preferred_element_type=jnp.float32)
        acc = term if acc is None else acc + term
    window_len = width // contrib_ref.shape[0]
    for r in range(contrib_ref.shape[0]):
        contrib_ref[r] = acc[:, r * window_len : (r + 1) * window_len]


def toeplitz(tap_row, out_width, weights, up_row):
    kernels, stencil_rows, reach = tap_row.shape
    window_len = out_width + reach
    padded = jnp.pad(tap_row.astype(jnp.float32), ((0, 0), (0, 0), (0, window_len - reach)))
    padded = padded.reshape(kernels, stencil_rows * window_len).astype(jnp.bfloat16)
    out, contrib = pl.pallas_call(
        toeplitz_kernel,
        out_shape=(
            jax.ShapeDtypeStruct((kernels, out_width, stencil_rows * window_len), jnp.bfloat16),
            jax.ShapeDtypeStruct((stencil_rows, weights.shape[2], window_len), jnp.float32),
        ),
    )(padded, weights, up_row)
    return out.reshape(kernels * out_width, stencil_rows * window_len), contrib


def lat_allreduce(x, axis, dim):
    count = lax.axis_size(axis)
    steps = count.bit_length() - 1
    if (1 << steps) != count or x.shape[dim] % count:
        return lax.psum(x, axis)
    index = lax.axis_index(axis)
    size = x.shape[dim] // count
    parts = [lax.dynamic_slice_in_dim(x, index * size, size, axis=dim)]
    for d in range(1, count):
        send = lax.dynamic_slice_in_dim(x, (index ^ d) * size, size, axis=dim)
        parts.append(lax.ppermute(send, axis, [(i, i ^ d) for i in range(count)]))
    for s in range(steps):
        parts = [parts[2 * e] + parts[2 * e + 1] for e in range(len(parts) // 2)]
    mine = parts[0]
    out = jnp.zeros(x.shape, x.dtype)
    out = lax.dynamic_update_slice_in_dim(out, mine, index * size, axis=dim)
    for d in range(1, count):
        recv = lax.ppermute(mine, axis, [(i, i ^ d) for i in range(count)])
        out = lax.dynamic_update_slice_in_dim(out, recv, (index ^ d) * size, axis=dim)
    return out


def row_kernel(below_ref, row_ref, above_ref, mt_ref, w_ref, up_ref, out_ref, gt_ref):
    channels, width = row_ref.shape
    stencil_rows = 3
    n_blocks, o_block, lon_cols = up_ref.shape
    kernels = w_ref.shape[0]
    window_len = mt_ref.shape[1] // stencil_rows
    contract_last = (((1,), (1,)), ((), ()))
    gt_ref[...] = jnp.zeros(gt_ref.shape, gt_ref.dtype)
    halo = (window_len - lon_cols) // 2
    exts = []
    for src_ref in (below_ref, row_ref, above_ref):
        full = src_ref[...]
        exts.append(jnp.concatenate([full[:, width - halo :], full, full[:, :halo]], axis=1))
    for d in range(n_blocks):
        acc = None
        for r in range(stencil_rows):
            win = exts[r][:, d * lon_cols : d * lon_cols + window_len]
            part = lax.dot_general(
                win,
                mt_ref[:, pl.ds(r * window_len, window_len)],
                contract_last,
                preferred_element_type=jnp.float32,
            )
            acc = part if acc is None else acc + part
        resp = acc.astype(jnp.bfloat16)
        up_d = up_ref[d]
        for k in range(kernels):
            resp_k = resp[:, k * lon_cols : (k + 1) * lon_cols]
            gt_ref[k] += lax.dot_general(
                up_d, resp_k, contract_last, preferred_element_type=jnp.float32
            )
        if d == 0:
            total = None
            for k in range(kernels):
                term = jnp.dot(
                    w_ref[k],
                    resp[:, k * lon_cols : (k + 1) * lon_cols],
                    preferred_element_type=jnp.float32,
                )
                total = term if total is None else total + term
            out_ref[...] = total.astype(out_ref.dtype)


def row_products(below, row, above, matrix, weights, up_rel):
    channels = row.shape[0]
    n_blocks, o_block, lon_cols = up_rel.shape
    kernels = weights.shape[0]
    flops = 2 * n_blocks * channels * matrix.shape[0] * matrix.shape[1]
    flops += 2 * n_blocks * kernels * o_block * lon_cols * channels
    flops += 2 * kernels * weights.shape[1] * channels * lon_cols
    nbytes = 2 * (3 * row.size + matrix.size + weights.size + up_rel.size)
    nbytes += 2 * weights.shape[1] * lon_cols + 4 * kernels * o_block * channels
    return pl.pallas_call(
        row_kernel,
        out_shape=(
            jax.ShapeDtypeStruct((weights.shape[1], lon_cols), jnp.bfloat16),
            jax.ShapeDtypeStruct((kernels, o_block, channels), jnp.float32),
        ),
        cost_estimate=pl.CostEstimate(flops=flops, transcendentals=0, bytes_accessed=nbytes),
    )(below, row, above, matrix, weights, up_rel)


def body(fields, upstream, weights, filter_taps, cycle_counts, cycle_blocks):
    channels, lat_rows, lon_cols = fields.shape
    kernels = weights.shape[0]
    window_len = lon_cols + 2 * HALO
    n_lon = lax.axis_size("lon")
    lon_at = lax.axis_index("lon")
    tap_table = build_taps(filter_taps, cycle_counts, cycle_blocks).astype(jnp.bfloat16)
    matrix, contrib = toeplitz(tap_table[0], lon_cols, weights, upstream[:, 0])
    o_block = upstream.shape[0] // n_lon
    up_row = upstream[:, 0]
    blocks = [fields[:, 0]]
    up_parts = [lax.dynamic_slice_in_dim(up_row, lon_at * o_block, o_block, axis=0)]
    for d in range(1, n_lon):
        part = lax.dynamic_slice_in_dim(up_row, ((lon_at - d) % n_lon) * o_block, o_block, axis=0)
        both = lax.ppermute(
            jnp.concatenate([fields[:, 0], part], axis=0),
            "lon",
            [(p, (p - d) % n_lon) for p in range(n_lon)],
        )
        blocks.append(both[:channels])
        up_parts.append(both[channels:])
    up_rel = jnp.stack(up_parts, axis=0)
    row = jnp.concatenate(blocks, axis=1)
    count = lax.axis_size("lat")
    below = lax.ppermute(row, "lat", [(i, i + 1) for i in range(count - 1)])
    above = lax.ppermute(row, "lat", [(i + 1, i) for i in range(count - 1)])
    out_row, grad_terms = row_products(below, row, above, matrix, weights, up_rel)
    outputs = out_row[:, None, :]
    weight_grad = lat_allreduce(grad_terms, "lat", 1)
    accumulated = jnp.zeros((channels, lat_rows + 2, window_len), jnp.float32)
    cycle_row = 0
    accumulated = accumulated.at[:, cycle_row : cycle_row + 3].add(
        contrib.transpose(1, 0, 2)
    )
    rim_columns = jnp.concatenate(
        [accumulated[:, :, :HALO], accumulated[:, :, HALO + lon_cols :]], axis=2
    )
    arrived = padded_2(rim_columns, (("lon", 2),), HALO, True)
    interior = accumulated[:, :, HALO : HALO + lon_cols]
    interior = interior.at[:, :, :HALO].add(arrived[:, :, :HALO])
    interior = interior.at[:, :, lon_cols - HALO :].add(arrived[:, :, 3 * HALO :])
    edge_rows = jnp.stack([interior[:, 0], interior[:, lat_rows + 1]], axis=1)
    arrived = padded_2(edge_rows, (("lat", 1),), 1, False)
    result = interior[:, 1 : lat_rows + 1]
    result = result.at[:, 0].add(arrived[:, 0])
    result = result.at[:, lat_rows - 1].add(arrived[:, 3])
    return (outputs, result.astype(jnp.bfloat16), weight_grad)


def solution(mesh):
    return jax.shard_map(
        body,
        mesh=mesh,
        in_specs=(
            P("groups", "lat", "lon"),
            P("groups", "lat", "lon"),
            P(),
            P("lat", None, None, None, None),
            P("lat"),
            P("lat", None),
        ),
        out_specs=(P("groups", "lat", "lon"), P("groups", "lat", "lon"), P("groups", "lon", None)),
        check_vma=False,
    )
```

```python
import jax
import jax.numpy as jnp
from jax import lax
from jax.experimental import pallas as pl
from jax.experimental.pallas import tpu as pltpu
from jax.sharding import PartitionSpec as P

HALO = 128


def padded_2(cells, sides, width, closed):
    for axis, dim in sides:
        count = lax.axis_size(axis)
        ends = count if closed else count - 1
        head = lax.slice_in_dim(cells, 0, width, axis=dim)
        tail = lax.slice_in_dim(cells, cells.shape[dim] - width, cells.shape[dim], axis=dim)
        cells = jnp.concatenate(
            [
                lax.ppermute(tail, axis, [(i, (i + 1) % count) for i in range(ends)]),
                cells,
                lax.ppermute(head, axis, [((i + 1) % count, i) for i in range(ends)]),
            ],
            axis=dim,
        )
    return cells


def build_taps(filter_taps, cycle_counts, cycle_blocks):
    slot_total = cycle_blocks.shape[1]
    width_block = filter_taps.shape[4]
    offsets = jnp.arange(width_block, dtype=jnp.int32)
    places = HALO + width_block * cycle_blocks[:, :, None] + offsets[None, None, :]
    live_slots = jnp.arange(slot_total, dtype=jnp.int32)[None, :] < cycle_counts[:, None]
    positions = jnp.arange(2 * HALO, dtype=jnp.int32)
    onehot = jnp.where(
        (places[:, :, :, None] == positions) & live_slots[:, :, None, None], 1.0, 0.0
    ).astype(jnp.float32)
    return jnp.einsum("ikrst,istu->ikru", filter_taps.astype(jnp.float32), onehot)


def toeplitz_kernel(tap_ref, w_ref, up_ref, out_ref, contrib_ref):
    kernels, lon_cols, width = out_ref.shape
    contract_first = (((0,), (0,)), ((), ()))
    acc = None
    for k in range(kernels):
        row = tap_ref[pl.ds(k, 1), :]
        tiled = jnp.broadcast_to(row, (lon_cols, width))
        out_ref[k] = pltpu.roll(tiled, 0, 1, stride=1, stride_axis=0)
        grad_k = lax.dot_general(
            w_ref[k], up_ref[...], contract_first, preferred_element_type=jnp.float32
        ).astype(jnp.bfloat16)
        term = jnp.dot(grad_k, out_ref[k], preferred_element_type=jnp.float32)
        acc = term if acc is None else acc + term
    window_len = width // contrib_ref.shape[0]
    for r in range(contrib_ref.shape[0]):
        contrib_ref[r] = acc[:, r * window_len : (r + 1) * window_len]


def toeplitz(tap_row, out_width, weights, up_row):
    kernels, stencil_rows, reach = tap_row.shape
    window_len = out_width + reach
    padded = jnp.pad(tap_row.astype(jnp.float32), ((0, 0), (0, 0), (0, window_len - reach)))
    padded = padded.reshape(kernels, stencil_rows * window_len).astype(jnp.bfloat16)
    out, contrib = pl.pallas_call(
        toeplitz_kernel,
        out_shape=(
            jax.ShapeDtypeStruct((kernels, out_width, stencil_rows * window_len), jnp.bfloat16),
            jax.ShapeDtypeStruct((stencil_rows, weights.shape[2], window_len), jnp.float32),
        ),
    )(padded, weights, up_row)
    return out.reshape(kernels * out_width, stencil_rows * window_len), contrib


def lat_allreduce(x, axis, dim):
    count = lax.axis_size(axis)
    steps = count.bit_length() - 1
    if (1 << steps) != count or x.shape[dim] % count:
        return lax.psum(x, axis)
    index = lax.axis_index(axis)
    size = x.shape[dim] // count
    parts = [lax.dynamic_slice_in_dim(x, index * size, size, axis=dim)]
    for d in range(1, count):
        send = lax.dynamic_slice_in_dim(x, (index ^ d) * size, size, axis=dim)
        parts.append(lax.ppermute(send, axis, [(i, i ^ d) for i in range(count)]))
    for s in range(steps):
        parts = [parts[2 * e] + parts[2 * e + 1] for e in range(len(parts) // 2)]
    mine = parts[0]
    out = jnp.zeros(x.shape, x.dtype)
    out = lax.dynamic_update_slice_in_dim(out, mine, index * size, axis=dim)
    for d in range(1, count):
        recv = lax.ppermute(mine, axis, [(i, i ^ d) for i in range(count)])
        out = lax.dynamic_update_slice_in_dim(out, recv, (index ^ d) * size, axis=dim)
    return out


def row_kernel(ext_ref, mt_ref, w_ref, up_ref, out_ref, gt_ref):
    stencil_rows, channels, _ = ext_ref.shape
    n_blocks, o_block, lon_cols = up_ref.shape
    kernels = w_ref.shape[0]
    window_len = mt_ref.shape[1] // stencil_rows
    contract_last = (((1,), (1,)), ((), ()))
    gt_ref[...] = jnp.zeros(gt_ref.shape, gt_ref.dtype)
    for d in range(n_blocks):
        acc = None
        for r in range(stencil_rows):
            win = ext_ref[r, :, pl.ds(d * lon_cols, window_len)]
            part = lax.dot_general(
                win,
                mt_ref[:, pl.ds(r * window_len, window_len)],
                contract_last,
                preferred_element_type=jnp.float32,
            )
            acc = part if acc is None else acc + part
        resp = acc.astype(jnp.bfloat16)
        up_d = up_ref[d]
        for k in range(kernels):
            resp_k = resp[:, k * lon_cols : (k + 1) * lon_cols]
            gt_ref[k] += lax.dot_general(
                up_d, resp_k, contract_last, preferred_element_type=jnp.float32
            )
        if d == 0:
            total = None
            for k in range(kernels):
                term = jnp.dot(
                    w_ref[k],
                    resp[:, k * lon_cols : (k + 1) * lon_cols],
                    preferred_element_type=jnp.float32,
                )
                total = term if total is None else total + term
            out_ref[...] = total.astype(out_ref.dtype)


def row_products(ext, matrix, weights, up_rel):
    stencil_rows, channels, _ = ext.shape
    n_blocks, o_block, lon_cols = up_rel.shape
    kernels = weights.shape[0]
    flops = 2 * n_blocks * channels * matrix.shape[0] * matrix.shape[1]
    flops += 2 * n_blocks * kernels * o_block * lon_cols * channels
    flops += 2 * kernels * weights.shape[1] * channels * lon_cols
    nbytes = 2 * (ext.size + matrix.size + weights.size + up_rel.size)
    nbytes += 2 * weights.shape[1] * lon_cols + 4 * kernels * o_block * channels
    return pl.pallas_call(
        row_kernel,
        out_shape=(
            jax.ShapeDtypeStruct((weights.shape[1], lon_cols), jnp.bfloat16),
            jax.ShapeDtypeStruct((kernels, o_block, channels), jnp.float32),
        ),
        cost_estimate=pl.CostEstimate(flops=flops, transcendentals=0, bytes_accessed=nbytes),
    )(ext, matrix, weights, up_rel)


def body(fields, upstream, weights, filter_taps, cycle_counts, cycle_blocks):
    channels, lat_rows, lon_cols = fields.shape
    kernels = weights.shape[0]
    window_len = lon_cols + 2 * HALO
    n_lon = lax.axis_size("lon")
    lon_at = lax.axis_index("lon")
    tap_table = build_taps(filter_taps, cycle_counts, cycle_blocks).astype(jnp.bfloat16)
    matrix, contrib = toeplitz(tap_table[0], lon_cols, weights, upstream[:, 0])
    o_block = upstream.shape[0] // n_lon
    up_row = upstream[:, 0]
    blocks = [fields[:, 0]] + [
        lax.ppermute(fields[:, 0], "lon", [(p, (p - d) % n_lon) for p in range(n_lon)])
        for d in range(1, n_lon)
    ]
    up_parts = [lax.dynamic_slice_in_dim(up_row, lon_at * o_block, o_block, axis=0)]
    for d in range(1, n_lon):
        part = lax.dynamic_slice_in_dim(up_row, ((lon_at - d) % n_lon) * o_block, o_block, axis=0)
        up_parts.append(lax.ppermute(part, "lon", [(p, (p - d) % n_lon) for p in range(n_lon)]))
    up_rel = jnp.stack(up_parts, axis=0)
    row = jnp.concatenate(blocks, axis=1)
    count = lax.axis_size("lat")
    below = lax.ppermute(row, "lat", [(i, i + 1) for i in range(count - 1)])
    above = lax.ppermute(row, "lat", [(i + 1, i) for i in range(count - 1)])
    rows = jnp.stack([below, row, above], axis=0)
    ext = jnp.concatenate([rows[:, :, rows.shape[2] - HALO :], rows, rows[:, :, :HALO]], axis=2)
    out_row, grad_terms = row_products(ext, matrix, weights, up_rel)
    outputs = out_row[:, None, :]
    weight_grad = lat_allreduce(grad_terms, "lat", 1)
    accumulated = jnp.zeros((channels, lat_rows + 2, window_len), jnp.float32)
    cycle_row = 0
    accumulated = accumulated.at[:, cycle_row : cycle_row + 3].add(
        contrib.transpose(1, 0, 2)
    )
    rim_columns = jnp.concatenate(
        [accumulated[:, :, :HALO], accumulated[:, :, HALO + lon_cols :]], axis=2
    )
    arrived = padded_2(rim_columns, (("lon", 2),), HALO, True)
    interior = accumulated[:, :, HALO : HALO + lon_cols]
    interior = interior.at[:, :, :HALO].add(arrived[:, :, :HALO])
    interior = interior.at[:, :, lon_cols - HALO :].add(arrived[:, :, 3 * HALO :])
    edge_rows = jnp.stack([interior[:, 0], interior[:, lat_rows + 1]], axis=1)
    arrived = padded_2(edge_rows, (("lat", 1),), 1, False)
    result = interior[:, 1 : lat_rows + 1]
    result = result.at[:, 0].add(arrived[:, 0])
    result = result.at[:, lat_rows - 1].add(arrived[:, 3])
    return (outputs, result.astype(jnp.bfloat16), weight_grad)


def solution(mesh):
    return jax.shard_map(
        body,
        mesh=mesh,
        in_specs=(
            P("groups", "lat", "lon"),
            P("groups", "lat", "lon"),
            P(),
            P("lat", None, None, None, None),
            P("lat"),
            P("lat", None),
        ),
        out_specs=(P("groups", "lat", "lon"), P("groups", "lat", "lon"), P("groups", "lon", None)),
        check_vma=False,
    )
```

```python
import jax
import jax.numpy as jnp
from jax import lax
from jax.experimental import pallas as pl
from jax.experimental.pallas import tpu as pltpu
from jax.sharding import PartitionSpec as P

HALO = 128


def padded_2(cells, sides, width, closed):
    for axis, dim in sides:
        count = lax.axis_size(axis)
        ends = count if closed else count - 1
        head = lax.slice_in_dim(cells, 0, width, axis=dim)
        tail = lax.slice_in_dim(cells, cells.shape[dim] - width, cells.shape[dim], axis=dim)
        cells = jnp.concatenate(
            [
                lax.ppermute(tail, axis, [(i, (i + 1) % count) for i in range(ends)]),
                cells,
                lax.ppermute(head, axis, [((i + 1) % count, i) for i in range(ends)]),
            ],
            axis=dim,
        )
    return cells


def build_taps(filter_taps, cycle_counts, cycle_blocks):
    slot_total = cycle_blocks.shape[1]
    width_block = filter_taps.shape[4]
    offsets = jnp.arange(width_block, dtype=jnp.int32)
    places = HALO + width_block * cycle_blocks[:, :, None] + offsets[None, None, :]
    live_slots = jnp.arange(slot_total, dtype=jnp.int32)[None, :] < cycle_counts[:, None]
    positions = jnp.arange(2 * HALO, dtype=jnp.int32)
    onehot = jnp.where(
        (places[:, :, :, None] == positions) & live_slots[:, :, None, None], 1.0, 0.0
    ).astype(jnp.float32)
    return jnp.einsum("ikrst,istu->ikru", filter_taps.astype(jnp.float32), onehot)


def toeplitz_kernel(tap_ref, w_ref, up_ref, out_ref, contrib_ref):
    kernels, lon_cols, width = out_ref.shape
    contract_first = (((0,), (0,)), ((), ()))
    acc = None
    for k in range(kernels):
        row = tap_ref[pl.ds(k, 1), :]
        tiled = jnp.broadcast_to(row, (lon_cols, width))
        out_ref[k] = pltpu.roll(tiled, 0, 1, stride=1, stride_axis=0)
        grad_k = lax.dot_general(
            w_ref[k], up_ref[...], contract_first, preferred_element_type=jnp.float32
        ).astype(jnp.bfloat16)
        term = jnp.dot(grad_k, out_ref[k], preferred_element_type=jnp.float32)
        acc = term if acc is None else acc + term
    window_len = width // contrib_ref.shape[0]
    for r in range(contrib_ref.shape[0]):
        contrib_ref[r] = acc[:, r * window_len : (r + 1) * window_len]


def toeplitz(tap_row, out_width, weights, up_row):
    kernels, stencil_rows, reach = tap_row.shape
    window_len = out_width + reach
    padded = jnp.pad(tap_row.astype(jnp.float32), ((0, 0), (0, 0), (0, window_len - reach)))
    padded = padded.reshape(kernels, stencil_rows * window_len).astype(jnp.bfloat16)
    out, contrib = pl.pallas_call(
        toeplitz_kernel,
        out_shape=(
            jax.ShapeDtypeStruct((kernels, out_width, stencil_rows * window_len), jnp.bfloat16),
            jax.ShapeDtypeStruct((stencil_rows, weights.shape[2], window_len), jnp.float32),
        ),
    )(padded, weights, up_row)
    return out.reshape(kernels * out_width, stencil_rows * window_len), contrib


def lat_allreduce(x, axis, dim):
    count = lax.axis_size(axis)
    steps = count.bit_length() - 1
    if (1 << steps) != count or x.shape[dim] % count:
        return lax.psum(x, axis)
    index = lax.axis_index(axis)
    size = x.shape[dim] // count
    chunks = [lax.slice_in_dim(x, c * size, (c + 1) * size, axis=dim) for c in range(count)]
    for s in range(steps):
        flip = ((index >> s) & 1) == 1
        chunks = [jnp.where(flip, chunks[c ^ (1 << s)], chunks[c]) for c in range(count)]
    parts = [chunks[0]]
    for d in range(1, count):
        parts.append(lax.ppermute(chunks[d], axis, [(i, i ^ d) for i in range(count)]))
    for s in range(steps):
        parts = [parts[2 * e] + parts[2 * e + 1] for e in range(len(parts) // 2)]
    mine = parts[0]
    out = jnp.zeros(x.shape, x.dtype)
    out = lax.dynamic_update_slice_in_dim(out, mine, index * size, axis=dim)
    for d in range(1, count):
        recv = lax.ppermute(mine, axis, [(i, i ^ d) for i in range(count)])
        out = lax.dynamic_update_slice_in_dim(out, recv, (index ^ d) * size, axis=dim)
    return out


def row_kernel(ext_ref, mt_ref, w_ref, up_ref, out_ref, gt_ref):
    stencil_rows, channels, _ = ext_ref.shape
    n_blocks, o_block, lon_cols = up_ref.shape
    kernels = w_ref.shape[0]
    window_len = mt_ref.shape[1] // stencil_rows
    contract_last = (((1,), (1,)), ((), ()))
    gt_ref[...] = jnp.zeros(gt_ref.shape, gt_ref.dtype)
    for d in range(n_blocks):
        acc = None
        for r in range(stencil_rows):
            win = ext_ref[r, :, pl.ds(d * lon_cols, window_len)]
            part = lax.dot_general(
                win,
                mt_ref[:, pl.ds(r * window_len, window_len)],
                contract_last,
                preferred_element_type=jnp.float32,
            )
            acc = part if acc is None else acc + part
        resp = acc.astype(jnp.bfloat16)
        up_d = up_ref[d]
        for k in range(kernels):
            resp_k = resp[:, k * lon_cols : (k + 1) * lon_cols]
            gt_ref[k] += lax.dot_general(
                up_d, resp_k, contract_last, preferred_element_type=jnp.float32
            )
        if d == 0:
            total = None
            for k in range(kernels):
                term = jnp.dot(
                    w_ref[k],
                    resp[:, k * lon_cols : (k + 1) * lon_cols],
                    preferred_element_type=jnp.float32,
                )
                total = term if total is None else total + term
            out_ref[...] = total.astype(out_ref.dtype)


def row_products(ext, matrix, weights, up_rel):
    stencil_rows, channels, _ = ext.shape
    n_blocks, o_block, lon_cols = up_rel.shape
    kernels = weights.shape[0]
    flops = 2 * n_blocks * channels * matrix.shape[0] * matrix.shape[1]
    flops += 2 * n_blocks * kernels * o_block * lon_cols * channels
    flops += 2 * kernels * weights.shape[1] * channels * lon_cols
    nbytes = 2 * (ext.size + matrix.size + weights.size + up_rel.size)
    nbytes += 2 * weights.shape[1] * lon_cols + 4 * kernels * o_block * channels
    return pl.pallas_call(
        row_kernel,
        out_shape=(
            jax.ShapeDtypeStruct((weights.shape[1], lon_cols), jnp.bfloat16),
            jax.ShapeDtypeStruct((kernels, o_block, channels), jnp.float32),
        ),
        cost_estimate=pl.CostEstimate(flops=flops, transcendentals=0, bytes_accessed=nbytes),
    )(ext, matrix, weights, up_rel)


def body(fields, upstream, weights, filter_taps, cycle_counts, cycle_blocks):
    channels, lat_rows, lon_cols = fields.shape
    kernels = weights.shape[0]
    window_len = lon_cols + 2 * HALO
    n_lon = lax.axis_size("lon")
    lon_at = lax.axis_index("lon")
    tap_table = build_taps(filter_taps, cycle_counts, cycle_blocks).astype(jnp.bfloat16)
    matrix, contrib = toeplitz(tap_table[0], lon_cols, weights, upstream[:, 0])
    o_block = upstream.shape[0] // n_lon
    up_row = upstream[:, 0]
    blocks = [fields[:, 0]]
    up_parts = [lax.dynamic_slice_in_dim(up_row, lon_at * o_block, o_block, axis=0)]
    for d in range(1, n_lon):
        part = lax.dynamic_slice_in_dim(up_row, ((lon_at - d) % n_lon) * o_block, o_block, axis=0)
        both = lax.ppermute(
            jnp.concatenate([fields[:, 0], part], axis=0),
            "lon",
            [(p, (p - d) % n_lon) for p in range(n_lon)],
        )
        blocks.append(both[:channels])
        up_parts.append(both[channels:])
    up_rel = jnp.stack(up_parts, axis=0)
    row = jnp.concatenate(blocks, axis=1)
    count = lax.axis_size("lat")
    below = lax.ppermute(row, "lat", [(i, i + 1) for i in range(count - 1)])
    above = lax.ppermute(row, "lat", [(i + 1, i) for i in range(count - 1)])
    rows = jnp.stack([below, row, above], axis=0)
    ext = jnp.concatenate([rows[:, :, rows.shape[2] - HALO :], rows, rows[:, :, :HALO]], axis=2)
    out_row, grad_terms = row_products(ext, matrix, weights, up_rel)
    outputs = out_row[:, None, :]
    weight_grad = lat_allreduce(grad_terms, "lat", 1)
    accumulated = jnp.zeros((channels, lat_rows + 2, window_len), jnp.float32)
    cycle_row = 0
    accumulated = accumulated.at[:, cycle_row : cycle_row + 3].add(
        contrib.transpose(1, 0, 2)
    )
    rim_columns = jnp.concatenate(
        [accumulated[:, :, :HALO], accumulated[:, :, HALO + lon_cols :]], axis=2
    )
    arrived = padded_2(rim_columns, (("lon", 2),), HALO, True)
    interior = accumulated[:, :, HALO : HALO + lon_cols]
    interior = interior.at[:, :, :HALO].add(arrived[:, :, :HALO])
    interior = interior.at[:, :, lon_cols - HALO :].add(arrived[:, :, 3 * HALO :])
    edge_rows = jnp.stack([interior[:, 0], interior[:, lat_rows + 1]], axis=1)
    arrived = padded_2(edge_rows, (("lat", 1),), 1, False)
    result = interior[:, 1 : lat_rows + 1]
    result = result.at[:, 0].add(arrived[:, 0])
    result = result.at[:, lat_rows - 1].add(arrived[:, 3])
    return (outputs, result.astype(jnp.bfloat16), weight_grad)


def solution(mesh):
    return jax.shard_map(
        body,
        mesh=mesh,
        in_specs=(
            P("groups", "lat", "lon"),
            P("groups", "lat", "lon"),
            P(),
            P("lat", None, None, None, None),
            P("lat"),
            P("lat", None),
        ),
        out_specs=(P("groups", "lat", "lon"), P("groups", "lat", "lon"), P("groups", "lon", None)),
        check_vma=False,
    )
```

```python
import jax
import jax.numpy as jnp
from jax import lax
from jax.experimental import pallas as pl
from jax.experimental.pallas import tpu as pltpu
from jax.sharding import PartitionSpec as P

HALO = 128


def padded_2(cells, sides, width, closed):
    for axis, dim in sides:
        count = lax.axis_size(axis)
        ends = count if closed else count - 1
        head = lax.slice_in_dim(cells, 0, width, axis=dim)
        tail = lax.slice_in_dim(cells, cells.shape[dim] - width, cells.shape[dim], axis=dim)
        cells = jnp.concatenate(
            [
                lax.ppermute(tail, axis, [(i, (i + 1) % count) for i in range(ends)]),
                cells,
                lax.ppermute(head, axis, [((i + 1) % count, i) for i in range(ends)]),
            ],
            axis=dim,
        )
    return cells


def build_taps(filter_taps, cycle_counts, cycle_blocks):
    slot_total = cycle_blocks.shape[1]
    width_block = filter_taps.shape[4]
    offsets = jnp.arange(width_block, dtype=jnp.int32)
    places = HALO + width_block * cycle_blocks[:, :, None] + offsets[None, None, :]
    live_slots = jnp.arange(slot_total, dtype=jnp.int32)[None, :] < cycle_counts[:, None]
    positions = jnp.arange(2 * HALO, dtype=jnp.int32)
    onehot = jnp.where(
        (places[:, :, :, None] == positions) & live_slots[:, :, None, None], 1.0, 0.0
    ).astype(jnp.float32)
    return jnp.einsum("ikrst,istu->ikru", filter_taps.astype(jnp.float32), onehot)


def toeplitz_kernel(tap_ref, w_ref, up_ref, out_ref, contrib_ref):
    kernels, lon_cols, width = out_ref.shape
    contract_first = (((0,), (0,)), ((), ()))
    acc = None
    for k in range(kernels):
        row = tap_ref[pl.ds(k, 1), :]
        tiled = jnp.broadcast_to(row, (lon_cols, width))
        out_ref[k] = pltpu.roll(tiled, 0, 1, stride=1, stride_axis=0)
        grad_k = lax.dot_general(
            w_ref[k], up_ref[...], contract_first, preferred_element_type=jnp.float32
        ).astype(jnp.bfloat16)
        term = jnp.dot(grad_k, out_ref[k], preferred_element_type=jnp.float32)
        acc = term if acc is None else acc + term
    window_len = width // contrib_ref.shape[0]
    for r in range(contrib_ref.shape[0]):
        contrib_ref[r] = acc[:, r * window_len : (r + 1) * window_len]


def toeplitz(tap_row, out_width, weights, up_row):
    kernels, stencil_rows, reach = tap_row.shape
    window_len = out_width + reach
    padded = jnp.pad(tap_row.astype(jnp.float32), ((0, 0), (0, 0), (0, window_len - reach)))
    padded = padded.reshape(kernels, stencil_rows * window_len).astype(jnp.bfloat16)
    out, contrib = pl.pallas_call(
        toeplitz_kernel,
        out_shape=(
            jax.ShapeDtypeStruct((kernels, out_width, stencil_rows * window_len), jnp.bfloat16),
            jax.ShapeDtypeStruct((stencil_rows, weights.shape[2], window_len), jnp.float32),
        ),
    )(padded, weights, up_row)
    return out.reshape(kernels * out_width, stencil_rows * window_len), contrib


def lat_allreduce(x, axis, dim):
    count = lax.axis_size(axis)
    steps = count.bit_length() - 1
    if (1 << steps) != count or x.shape[dim] % count:
        return lax.psum(x, axis)
    index = lax.axis_index(axis)
    size = x.shape[dim] // count
    chunks = [lax.slice_in_dim(x, c * size, (c + 1) * size, axis=dim) for c in range(count)]
    for s in range(steps):
        flip = ((index >> s) & 1) == 1
        chunks = [jnp.where(flip, chunks[c ^ (1 << s)], chunks[c]) for c in range(count)]
    parts = [chunks[0]]
    for d in range(1, count):
        parts.append(lax.ppermute(chunks[d], axis, [(i, i ^ d) for i in range(count)]))
    for s in range(steps):
        parts = [parts[2 * e] + parts[2 * e + 1] for e in range(len(parts) // 2)]
    mine = parts[0]
    gathered = [mine] + [
        lax.ppermute(mine, axis, [(i, i ^ d) for i in range(count)]) for d in range(1, count)
    ]
    for s in range(steps):
        flip = ((index >> s) & 1) == 1
        gathered = [jnp.where(flip, gathered[c ^ (1 << s)], gathered[c]) for c in range(count)]
    return jnp.concatenate(gathered, axis=dim)


def row_kernel(ext_ref, mt_ref, w_ref, up_ref, out_ref, gt_ref):
    stencil_rows, channels, _ = ext_ref.shape
    n_blocks, o_block, lon_cols = up_ref.shape
    kernels = w_ref.shape[0]
    window_len = mt_ref.shape[1] // stencil_rows
    contract_last = (((1,), (1,)), ((), ()))
    gt_ref[...] = jnp.zeros(gt_ref.shape, gt_ref.dtype)
    for d in range(n_blocks):
        acc = None
        for r in range(stencil_rows):
            win = ext_ref[r, :, pl.ds(d * lon_cols, window_len)]
            part = lax.dot_general(
                win,
                mt_ref[:, pl.ds(r * window_len, window_len)],
                contract_last,
                preferred_element_type=jnp.float32,
            )
            acc = part if acc is None else acc + part
        resp = acc.astype(jnp.bfloat16)
        up_d = up_ref[d]
        for k in range(kernels):
            resp_k = resp[:, k * lon_cols : (k + 1) * lon_cols]
            gt_ref[k] += lax.dot_general(
                up_d, resp_k, contract_last, preferred_element_type=jnp.float32
            )
        if d == 0:
            total = None
            for k in range(kernels):
                term = jnp.dot(
                    w_ref[k],
                    resp[:, k * lon_cols : (k + 1) * lon_cols],
                    preferred_element_type=jnp.float32,
                )
                total = term if total is None else total + term
            out_ref[...] = total.astype(out_ref.dtype)


def row_products(ext, matrix, weights, up_rel):
    stencil_rows, channels, _ = ext.shape
    n_blocks, o_block, lon_cols = up_rel.shape
    kernels = weights.shape[0]
    flops = 2 * n_blocks * channels * matrix.shape[0] * matrix.shape[1]
    flops += 2 * n_blocks * kernels * o_block * lon_cols * channels
    flops += 2 * kernels * weights.shape[1] * channels * lon_cols
    nbytes = 2 * (ext.size + matrix.size + weights.size + up_rel.size)
    nbytes += 2 * weights.shape[1] * lon_cols + 4 * kernels * o_block * channels
    return pl.pallas_call(
        row_kernel,
        out_shape=(
            jax.ShapeDtypeStruct((weights.shape[1], lon_cols), jnp.bfloat16),
            jax.ShapeDtypeStruct((kernels, o_block, channels), jnp.float32),
        ),
        cost_estimate=pl.CostEstimate(flops=flops, transcendentals=0, bytes_accessed=nbytes),
    )(ext, matrix, weights, up_rel)


def body(fields, upstream, weights, filter_taps, cycle_counts, cycle_blocks):
    channels, lat_rows, lon_cols = fields.shape
    kernels = weights.shape[0]
    window_len = lon_cols + 2 * HALO
    n_lon = lax.axis_size("lon")
    lon_at = lax.axis_index("lon")
    tap_table = build_taps(filter_taps, cycle_counts, cycle_blocks).astype(jnp.bfloat16)
    matrix, contrib = toeplitz(tap_table[0], lon_cols, weights, upstream[:, 0])
    o_block = upstream.shape[0] // n_lon
    up_row = upstream[:, 0]
    blocks = [fields[:, 0]]
    up_parts = [lax.dynamic_slice_in_dim(up_row, lon_at * o_block, o_block, axis=0)]
    for d in range(1, n_lon):
        part = lax.dynamic_slice_in_dim(up_row, ((lon_at - d) % n_lon) * o_block, o_block, axis=0)
        both = lax.ppermute(
            jnp.concatenate([fields[:, 0], part], axis=0),
            "lon",
            [(p, (p - d) % n_lon) for p in range(n_lon)],
        )
        blocks.append(both[:channels])
        up_parts.append(both[channels:])
    up_rel = jnp.stack(up_parts, axis=0)
    row = jnp.concatenate(blocks, axis=1)
    count = lax.axis_size("lat")
    below = lax.ppermute(row, "lat", [(i, i + 1) for i in range(count - 1)])
    above = lax.ppermute(row, "lat", [(i + 1, i) for i in range(count - 1)])
    rows = jnp.stack([below, row, above], axis=0)
    ext = jnp.concatenate([rows[:, :, rows.shape[2] - HALO :], rows, rows[:, :, :HALO]], axis=2)
    out_row, grad_terms = row_products(ext, matrix, weights, up_rel)
    outputs = out_row[:, None, :]
    weight_grad = lat_allreduce(grad_terms, "lat", 1)
    accumulated = jnp.zeros((channels, lat_rows + 2, window_len), jnp.float32)
    cycle_row = 0
    accumulated = accumulated.at[:, cycle_row : cycle_row + 3].add(
        contrib.transpose(1, 0, 2)
    )
    rim_columns = jnp.concatenate(
        [accumulated[:, :, :HALO], accumulated[:, :, HALO + lon_cols :]], axis=2
    )
    arrived = padded_2(rim_columns, (("lon", 2),), HALO, True)
    interior = accumulated[:, :, HALO : HALO + lon_cols]
    interior = interior.at[:, :, :HALO].add(arrived[:, :, :HALO])
    interior = interior.at[:, :, lon_cols - HALO :].add(arrived[:, :, 3 * HALO :])
    edge_rows = jnp.stack([interior[:, 0], interior[:, lat_rows + 1]], axis=1)
    arrived = padded_2(edge_rows, (("lat", 1),), 1, False)
    result = interior[:, 1 : lat_rows + 1]
    result = result.at[:, 0].add(arrived[:, 0])
    result = result.at[:, lat_rows - 1].add(arrived[:, 3])
    return (outputs, result.astype(jnp.bfloat16), weight_grad)


def solution(mesh):
    return jax.shard_map(
        body,
        mesh=mesh,
        in_specs=(
            P("groups", "lat", "lon"),
            P("groups", "lat", "lon"),
            P(),
            P("lat", None, None, None, None),
            P("lat"),
            P("lat", None),
        ),
        out_specs=(P("groups", "lat", "lon"), P("groups", "lat", "lon"), P("groups", "lon", None)),
        check_vma=False,
    )
```
